256 devices in a mesh: kv: 8 (over z), blk: 32 (over y, x, core).
Axes of the slice: x: 4, y: 4, z: 8, core: 2. Of those that a mesh axis runs over, the one named last changes fastest.
Arguments:
- hidden_in: bfloat16 [4, 16, 4096], P(None, None, 'blk'), may hold values from -6 to 6
- attn_gain: bfloat16 [4096], P('blk'), may hold values from 0.5 to 1.5
- ffn_gain: bfloat16 [4096], replicated, may hold values from 0.5 to 1.5
- query_key_value_weight: bfloat16 [4096, 8, 768], P('blk', 'kv'), may hold values from -0.09375 to 0.09375
- out_weight: bfloat16 [4096, 4096], P('kv', 'blk'), may hold values from -0.09375 to 0.09375
- router_weight: bfloat16 [4096, 8], replicated, may hold values from -0.09375 to 0.09375
- expert_in: bfloat16 [8, 4096, 2, 8192], P('kv', None, None, 'blk'), may hold values from -0.09375 to 0.09375
- expert_down: bfloat16 [8, 8192, 4096], P('kv', 'blk'), may hold values from -0.125 to 0.125
- kv_cache: bfloat16 [2048, 2, 8, 128, 128], P('blk', None, 'kv')
- lengths: int32 [2], replicated, may hold values from 1 to 16384, as said below
- tables: int32 [16, 128], replicated, may hold values from 0 to 2047, as said below
- parents: int32 [4, 16], replicated, may hold values from 0 to 15, as said below
- routes: int32 [4, 16, 2], replicated, may hold values from 0 to 7, all different within a row; in each aligned block of 16 rows (0 to 15, 16 to 31, ..., all dimensions but the last counted through in order) at most 6 rows name the same one
Outputs:
- layer_out: bfloat16 [4, 16, 4096], P(None, None, 'blk')
The draws below stay inside these ranges and needn't reach their ends.
Inputs may be any that keep to these rules, and one draw needn't show every extreme that they name: `lengths`: one group has exactly 16384 cached positions. `tables`: each pool block is named exactly once. `parents`: a beam's parent is a beam of its own group of 8 consecutive beams. `routes`: in each step no expert is named by more than 6 beams, a bound that some block reaches.
All inputs are finite; a program needn't handle non-finite values.
Results may differ from the reference program's by a relative error of at most 0.013.
Values may be sent and summed in bfloat16 or wider, within the bound.
No kernel may reach another device: no remote copies, remote signals or barrier semaphores. Data moves between devices by JAX's collectives and lax.ppermute only.
A program may use at most 64 MiB of HBM per device.

```python
import math
import jax
import jax.numpy as jnp
import numpy as np
from jax import lax

MODEL_WIDTH = 4096
QUERY_HEADS = 32
KEY_VALUE_HEADS = 8
HEAD_WIDTH = 128
QUERIES_PER_KEY = 4
EXPERTS = 8
FF = 8192
BEAM_W = 8
GROUPS = 2
DECODE_STEPS = 4
BLOCK_POSITIONS = 128
BEAM_BLOCKS = 128
BEAM_TOTAL = 16
CAP = 6


def draw_kv_cache(key, part):
    first_key = jax.random.fold_in(jax.random.fold_in(key, 11), 0)
    mean_key = jax.random.fold_in(jax.random.fold_in(key, 11), 2)
    pool_count = BEAM_TOTAL * BEAM_BLOCKS
    complete_shape = (pool_count, 2, KEY_VALUE_HEADS, BLOCK_POSITIONS, HEAD_WIDTH)
    selector = jnp.array([1.0, 0.0], jnp.float32).reshape(1, 2, 1, 1, 1)
    value_pick = 1.0 - selector
    mean_vector = jax.random.normal(mean_key, (1, 1, KEY_VALUE_HEADS, 1, HEAD_WIDTH), jnp.float32)
    fraction = (jnp.arange(pool_count, dtype=jnp.float32) / (pool_count - 1)).reshape(pool_count, 1, 1, 1, 1)
    ramp = 1.0 + 4.0 * fraction
    values = jax.random.normal(first_key, complete_shape, jnp.float32) + value_pick * ramp * mean_vector
    return values.astype(jnp.bfloat16)


def draw_lengths(key, part):
    first_key, following_key, third_key = jax.random.split(jax.random.fold_in(key, 29), 3)
    longest = BEAM_BLOCKS * BLOCK_POSITIONS
    base = jax.random.randint(first_key, (GROUPS,), 1, longest + 1)
    order = jax.random.permutation(following_key, GROUPS)
    other_len = jax.random.randint(third_key, (), 1, longest)
    base = base.at[order[0]].set(longest)
    base = base.at[order[1]].set(other_len)
    return base.astype(jnp.int32)


def draw_tables(key, part):
    order = jax.random.permutation(jax.random.fold_in(key, 37), BEAM_TOTAL * BEAM_BLOCKS)
    return order.reshape(BEAM_TOTAL, BEAM_BLOCKS).astype(jnp.int32)


def draw_parents(key, part):
    offsets = jax.random.randint(jax.random.fold_in(key, 41), (DECODE_STEPS, BEAM_TOTAL), 0, BEAM_W)
    group_base = jnp.arange(BEAM_TOTAL, dtype=jnp.int32) // BEAM_W * BEAM_W
    return (offsets + group_base[None, :]).astype(jnp.int32)


def spiked(entries, rng, source, target, parts, factor):
    def block_of(axis_at):
        return (jnp.arange(entries.shape[axis_at]) // (entries.shape[axis_at] // parts)).reshape((-1,) + (1,) * (entries.ndim - 1 - axis_at))

    first = jax.random.permutation(rng, parts)[block_of(target)]
    far = (block_of(target) + parts // 2) % parts
    return jnp.where((block_of(source) == first) | (block_of(source) == far), factor * entries, entries)


def block_levels(key, shape, pieces, least, largest):
    level, own = 1.0, jax.random.fold_in(key, 6)
    for dim, blocks in pieces:
        draws = jnp.exp(jax.random.uniform(jax.random.fold_in(own, dim), (blocks,), jnp.float32, least / len(pieces), largest / len(pieces)))
        level = level * jnp.repeat(draws, shape[dim] // blocks).reshape([-1 if axis == dim else 1 for axis in range(len(shape))])
    return level


def assign_block(stream_key, own, number, rows, amount, top, reach, skew):
    sequence = jax.random.permutation(stream_key, amount)
    crowded, ordinary = load_shares(amount, rows * top, reach, skew, True), load_shares(amount, rows * top, reach, skew, False)
    places = jnp.arange(amount)

    def named(sizes, rotation):
        used = int((sizes > 0).sum())
        fixed = max(1, used // 4)
        passed = fixed + (places - fixed + rotation * (used - fixed)) % max(1, amount - fixed)
        return jnp.zeros((amount,), jnp.int32).at[sequence[jnp.where(places < fixed, places, passed)]].set(jnp.asarray(sizes, jnp.int32))

    sizes = jnp.where(number % 4 == 0, named(crowded, number // 4), named(ordinary, number - number // 4 - 1))
    mixed = jax.random.permutation(jax.random.fold_in(own, 3), amount)
    donor, sink = mixed[0:amount // 2 * 2:2], mixed[1:amount // 2 * 2:2]
    margin = jnp.minimum(sizes[donor] - 1, reach - sizes[sink]) // 2
    margin = jnp.where((donor == sequence[0]) | (sink == sequence[0]) | (sizes[sink] == 0), 0, jnp.maximum(margin, 0))
    passed = jax.random.randint(jax.random.fold_in(own, 4), (amount // 2,), 0, 1 << 20) % (margin + 1)
    sizes = sizes.at[donor].add(-passed).at[sink].add(passed)
    labels = jnp.searchsorted(jnp.cumsum(sizes), jnp.arange(rows * top), side="right").astype(jnp.int32)
    listing = labels.reshape(top, rows).T
    listing = listing[jax.random.permutation(jax.random.fold_in(own, 1), rows)]
    rotation = jax.random.randint(jax.random.fold_in(own, 2), (rows, 1), 0, top)
    return jnp.take_along_axis(listing, (jnp.arange(top)[None, :] + rotation) % top, axis=1)


def load_shares(amount, total, reach, lean, full):
    weights = [(1 << 20) // math.isqrt(rank ** lean) + 1 for rank in range(1, amount + 1)]
    largest = reach if full else min(reach, max(-(-total // amount), total * weights[0] // sum(weights)))
    least = 1 if total - largest >= amount - 1 else 0
    given, spare = [largest] + [least] * (amount - 1), total - largest - least * (amount - 1)
    while spare > 0:
        free = [i for i in range(1, amount) if given[i] < largest] or [i for i in range(1, amount) if given[i] < reach]
        pool, left = sum([weights[i] for i in free]), spare
        for i in free:
            extra = min(reach - given[i], max(1, left * weights[i] // pool), spare)
            given[i] = given[i] + extra
            spare = spare - extra
    return np.array(given)


def centred(key, shape, scale, most, shards=(), kind=jnp.bfloat16):
    level = block_levels(key, shape, shards, -0.22, 0.18) if shards else 1.0
    drawn = jax.random.normal(key, shape, jnp.float32) * scale * level
    return jnp.minimum(jnp.maximum(drawn, -most), most).astype(kind)


def noise_with(own_key, extent, spread, reach, cuts, heavy, kind=jnp.bfloat16):
    values = spread * jax.random.normal(own_key, extent, jnp.float32)
    if cuts:
        values = values * block_levels(own_key, extent, cuts, -0.22, 0.18)
    return jnp.clip(spiked(values, jax.random.fold_in(own_key, 3), *heavy), -reach, reach).astype(kind)


def setup_inputs(seed: int = 0) -> dict:
    arg_keys = jax.random.split(jax.random.key(seed), 14)
    hidden_in = centred(arg_keys[0], (DECODE_STEPS, BEAM_TOTAL, MODEL_WIDTH), 1.0, 6.0, ((2, 32),))
    attn_gain = jnp.clip(1.0 + 0.1 * jax.random.normal(arg_keys[1], (MODEL_WIDTH,), jnp.float32), 0.5, 1.5).astype(jnp.bfloat16)
    ffn_gain = jnp.clip(1.0 + 0.1 * jax.random.normal(arg_keys[2], (MODEL_WIDTH,), jnp.float32), 0.5, 1.5).astype(jnp.bfloat16)
    query_key_value_weight = centred(arg_keys[3], (MODEL_WIDTH, KEY_VALUE_HEADS, (QUERY_HEADS // KEY_VALUE_HEADS + 2) * HEAD_WIDTH), MODEL_WIDTH ** -0.5, 0.09375, ((0, 32), (1, 8)))
    out_weight = centred(arg_keys[4], (QUERY_HEADS * HEAD_WIDTH, MODEL_WIDTH), (QUERY_HEADS * HEAD_WIDTH) ** -0.5, 0.09375, ((0, 8), (1, 32)))
    router_weight = centred(arg_keys[5], (MODEL_WIDTH, EXPERTS), MODEL_WIDTH ** -0.5, 0.09375)
    expert_in = centred(arg_keys[6], (EXPERTS, MODEL_WIDTH, 2, FF), MODEL_WIDTH ** -0.5, 0.09375, ((0, 8), (3, 32)))
    expert_down = noise_with(arg_keys[7], (EXPERTS, FF, MODEL_WIDTH), FF ** -0.5, 0.125, ((0, 8), (1, 32)), (1, 2, 32, 2.75))
    kv_cache = draw_kv_cache(jax.random.fold_in(arg_keys[13], 71), 0)
    lengths = draw_lengths(jax.random.fold_in(arg_keys[13], 71), 0)
    tables = draw_tables(jax.random.fold_in(arg_keys[13], 71), 0)
    parents = draw_parents(jax.random.fold_in(arg_keys[13], 71), 0)
    routes_keys = jax.random.split(jax.random.fold_in(arg_keys[12], 1), DECODE_STEPS * BEAM_TOTAL // BEAM_TOTAL)
    routes_turns = jax.random.permutation(jax.random.fold_in(arg_keys[12], 3), DECODE_STEPS * BEAM_TOTAL // BEAM_TOTAL)
    routes = jax.vmap(lambda own, number: assign_block(jax.random.fold_in(arg_keys[12], 2), own, number, BEAM_TOTAL, EXPERTS, 2, CAP, 2))(routes_keys, routes_turns).reshape((DECODE_STEPS, BEAM_TOTAL, 2))
    return dict(hidden_in=hidden_in, attn_gain=attn_gain, ffn_gain=ffn_gain, query_key_value_weight=query_key_value_weight, out_weight=out_weight, router_weight=router_weight, expert_in=expert_in, expert_down=expert_down, kv_cache=kv_cache, lengths=lengths, tables=tables, parents=parents, routes=routes)


NORM_FLOOR = 1e-05
ROPE_BASE = 1000000.0
NEG_FILL = -1e+30

def rotate_pairs(vectors, positions):
    half_width = vectors.shape[-1] // 2
    exponents = jnp.arange(half_width, dtype=jnp.float32) * (2.0 / vectors.shape[-1])
    frequency = ROPE_BASE ** (-exponents)
    angles = positions.astype(jnp.float32)[..., None] * frequency
    cosine = jnp.cos(angles)
    sine_part = jnp.sin(angles)
    lower_half = vectors[..., :half_width]
    upper_half = vectors[..., half_width:]
    return jnp.concatenate([lower_half * cosine - upper_half * sine_part, upper_half * cosine + lower_half * sine_part], axis=-1)

def lineage(parents):
    steps_count, beam_count = parents.shape
    beam_ids = jnp.arange(beam_count, dtype=jnp.int32)
    line_rows = []
    anchor_rows = []
    for step_index in range(steps_count):
        current = beam_ids
        levels = [jnp.full((beam_count,), -1, jnp.int32) for level_index in range(steps_count)]
        for level_index in range(step_index, -1, -1):
            levels[level_index] = current
            current = parents[level_index][current].astype(jnp.int32)
        line_rows.append(jnp.stack(levels))
        anchor_rows.append(current)
    return (jnp.stack(line_rows), jnp.stack(anchor_rows))

def expert_rank(routes):
    steps_count, beam_count, pick_count = routes.shape
    onehot = (routes[..., None] == jnp.arange(EXPERTS, dtype=jnp.int32)).astype(jnp.int32)
    flat_hits = onehot.reshape(steps_count, beam_count * pick_count, EXPERTS)
    before = jnp.cumsum(flat_hits, axis=1) - flat_hits
    return lax.optimization_barrier(jnp.sum(before * flat_hits, axis=-1)).reshape(steps_count, beam_count, pick_count).astype(jnp.int32)

def reference(hidden_in, attn_gain, ffn_gain, query_key_value_weight, out_weight, router_weight, expert_in, expert_down, kv_cache, lengths, tables, parents, routes):
    count_tokens = DECODE_STEPS * BEAM_TOTAL
    logit_scale = 1.0 / math.sqrt(HEAD_WIDTH)
    line_beams, anchor = lineage(parents)
    flat_in = hidden_in.reshape(count_tokens, MODEL_WIDTH).astype(jnp.float32)
    attention_mean = lax.optimization_barrier(jnp.mean(flat_in * flat_in, axis=1))
    pre_attn = (flat_in * attn_gain.astype(jnp.float32)).astype(jnp.bfloat16)
    projected_rows = jnp.dot(pre_attn, query_key_value_weight.reshape(MODEL_WIDTH, -1), preferred_element_type=jnp.float32)
    projected_rows = (projected_rows * lax.rsqrt(attention_mean + NORM_FLOOR)[:, None]).reshape(DECODE_STEPS, BEAM_TOTAL, KEY_VALUE_HEADS, QUERIES_PER_KEY + 2, HEAD_WIDTH)
    beam_groups = jnp.arange(BEAM_TOTAL, dtype=jnp.int32) // BEAM_W
    positions = lengths[beam_groups][None, :] + jnp.arange(DECODE_STEPS, dtype=jnp.int32)[:, None]
    queries = rotate_pairs(projected_rows[:, :, :, :QUERIES_PER_KEY], positions[:, :, None, None]).astype(jnp.bfloat16)
    new_key = rotate_pairs(projected_rows[:, :, :, QUERIES_PER_KEY], positions[:, :, None]).astype(jnp.bfloat16)
    new_value = projected_rows[:, :, :, QUERIES_PER_KEY + 1].astype(jnp.bfloat16)
    recent_allowed = jnp.transpose(line_beams[:, :, :, None] == jnp.arange(BEAM_TOTAL, dtype=jnp.int32), (0, 2, 1, 3)).reshape(DECODE_STEPS, BEAM_TOTAL, count_tokens)
    cache_allowed = jnp.arange(BEAM_BLOCKS * BLOCK_POSITIONS, dtype=jnp.int32)[None, :] < lengths[beam_groups][:, None]
    slot_rows = tables[anchor]

    def attend_heads(combined):
        head_index = combined // DECODE_STEPS
        step_index = combined % DECODE_STEPS
        cache_head = lax.dynamic_index_in_dim(kv_cache, head_index, axis=2, keepdims=False)
        picked = cache_head[lax.dynamic_index_in_dim(slot_rows, step_index, axis=0, keepdims=False)]
        key_matrix = picked[:, :, 0].reshape(BEAM_TOTAL, BEAM_BLOCKS * BLOCK_POSITIONS, HEAD_WIDTH).astype(jnp.float32)
        value_matrix = picked[:, :, 1].reshape(BEAM_TOTAL, BEAM_BLOCKS * BLOCK_POSITIONS, HEAD_WIDTH).astype(jnp.float32)
        query_matrix = lax.dynamic_index_in_dim(queries, step_index, axis=0, keepdims=False)
        query_matrix = lax.dynamic_index_in_dim(query_matrix, head_index, axis=1, keepdims=False).astype(jnp.float32)
        newest_keys = lax.dynamic_index_in_dim(new_key, head_index, axis=2, keepdims=False).reshape(count_tokens, HEAD_WIDTH).astype(jnp.float32)
        newest_values = lax.dynamic_index_in_dim(new_value, head_index, axis=2, keepdims=False).reshape(count_tokens, HEAD_WIDTH).astype(jnp.float32)
        cache_logits = jnp.einsum('uho,ulo->uhl', query_matrix, key_matrix) * logit_scale
        newest_logits = jnp.einsum('scr,xr->scx', query_matrix, newest_keys) * logit_scale
        recent_ok = lax.dynamic_index_in_dim(recent_allowed, step_index, axis=0, keepdims=False)[:, None, :]
        cache_ok = cache_allowed[:, None, :]
        cache_masked = jnp.where(cache_ok, cache_logits, NEG_FILL)
        recent_masked = jnp.where(recent_ok, newest_logits, NEG_FILL)
        row_max = jnp.maximum(lax.optimization_barrier(jnp.max(cache_masked, axis=-1)), lax.optimization_barrier(jnp.max(recent_masked, axis=-1)))[..., None]
        cache_weights = jnp.where(cache_ok, jnp.exp(cache_masked - row_max), 0.0)
        recent_weights = jnp.where(recent_ok, jnp.exp(recent_masked - row_max), 0.0)
        weight_sum = lax.optimization_barrier(jnp.sum(cache_weights, axis=-1)) + lax.optimization_barrier(jnp.sum(recent_weights, axis=-1))
        cache_lowered = lax.optimization_barrier(cache_weights.astype(jnp.bfloat16)).astype(jnp.float32)
        newest_lowered = lax.optimization_barrier(recent_weights.astype(jnp.bfloat16)).astype(jnp.float32)
        weighted_values = jnp.einsum('ufk,uke->ufe', cache_lowered, value_matrix) + jnp.einsum('wrx,xc->wrc', newest_lowered, newest_values)
        return (weighted_values / weight_sum[..., None]).astype(jnp.bfloat16)
    attended_rows = lax.map(attend_heads, jnp.arange(KEY_VALUE_HEADS * DECODE_STEPS, dtype=jnp.int32))
    attended_rows = attended_rows.reshape(KEY_VALUE_HEADS, DECODE_STEPS, BEAM_TOTAL, QUERIES_PER_KEY, HEAD_WIDTH).transpose(1, 2, 0, 3, 4).reshape(count_tokens, QUERY_HEADS * HEAD_WIDTH)
    attn_out = jnp.dot(attended_rows, out_weight, preferred_element_type=jnp.float32)
    residual = (flat_in + attn_out).astype(jnp.bfloat16)
    residual_wide = residual.astype(jnp.float32)
    mean_ffn = lax.optimization_barrier(jnp.mean(residual_wide * residual_wide, axis=1))
    inv_ffn = lax.rsqrt(mean_ffn + NORM_FLOOR)
    pre_ffn = (residual_wide * ffn_gain.astype(jnp.float32)).astype(jnp.bfloat16)
    logits = jnp.dot(pre_ffn, router_weight, preferred_element_type=jnp.float32) * inv_ffn[:, None]
    flat_routes = routes.reshape(count_tokens, 2)
    own_logit = jnp.take_along_axis(logits, flat_routes, axis=1)
    gate_share = 1.0 / (1.0 + jnp.exp(own_logit[:, ::-1] - own_logit))
    rank = expert_rank(routes).reshape(count_tokens, 2)
    rows_per_expert = DECODE_STEPS * CAP
    step_of = jnp.arange(count_tokens, dtype=jnp.int32) // BEAM_TOTAL
    row_id = (flat_routes * rows_per_expert + step_of[:, None] * CAP + rank).reshape(-1)
    token_ids = jnp.broadcast_to(jnp.arange(count_tokens, dtype=jnp.int32)[:, None], (count_tokens, 2)).reshape(-1)
    row_token = jnp.zeros((EXPERTS * rows_per_expert,), jnp.int32).at[row_id].set(token_ids)
    row_gate = jnp.zeros((EXPERTS * rows_per_expert,), jnp.float32).at[row_id].set(gate_share.reshape(-1))

    def run_expert(expert_index):
        rows_here = lax.dynamic_slice_in_dim(row_token, expert_index * rows_per_expert, rows_per_expert)
        pre_rows = pre_ffn[rows_here]
        scale_rows = inv_ffn[rows_here]
        weight_in = lax.dynamic_index_in_dim(expert_in, expert_index, axis=0, keepdims=False).reshape(MODEL_WIDTH, 2 * FF)
        weight_down = lax.dynamic_index_in_dim(expert_down, expert_index, axis=0, keepdims=False)
        expert_act = jnp.dot(pre_rows, weight_in, preferred_element_type=jnp.float32) * scale_rows[:, None]
        expert_hidden = (jax.nn.silu(expert_act[:, :FF]) * expert_act[:, FF:]).astype(jnp.bfloat16)
        return jnp.dot(expert_hidden, weight_down, preferred_element_type=jnp.float32)
    expert_result = lax.map(run_expert, jnp.arange(EXPERTS, dtype=jnp.int32)).reshape(EXPERTS * rows_per_expert, MODEL_WIDTH)
    mixture = jnp.zeros((count_tokens, MODEL_WIDTH), jnp.float32).at[row_token].add(expert_result * row_gate[:, None])
    return (residual_wide + mixture).astype(jnp.bfloat16).reshape(DECODE_STEPS, BEAM_TOTAL, MODEL_WIDTH)
```

```python
import math

import jax
import jax.numpy as jnp
from jax import lax
from jax.sharding import PartitionSpec as P

MODEL_WIDTH = 4096
HEAD_WIDTH = 128
QUERIES_PER_KEY = 4
EXPERTS = 8
BEAM_W = 8
GROUPS = 2
DECODE_STEPS = 4
BLOCK_POSITIONS = 128
BEAM_BLOCKS = 128
BEAM_TOTAL = 16
CAP = 6


NORM_FLOOR = 1e-05
ROPE_BASE = 1000000.0
NEG_FILL = -1e30


def exchange(value, axis, size, distance):
    pairs = [(index, index ^ distance) for index in range(size)]
    return jax.tree.map(lambda part: lax.ppermute(part, axis, pairs), value)


def butterfly(value, axis, size, join):
    distance = 1
    while distance < size:
        value = join(value, exchange(value, axis, size, distance))
        distance *= 2
    return value


def add_parts(first, second):
    return jax.tree.map(lambda one, two: one + two, first, second)


def gather_doubling(block, axis, size, dim):
    index = lax.axis_index(axis)
    distance = 1
    while distance < size:
        other = exchange(block, axis, size, distance)
        upper = (index // distance) % 2 == 1
        block = jnp.where(
            upper,
            jnp.concatenate([other, block], dim),
            jnp.concatenate([block, other], dim),
        )
        distance *= 2
    return block


def scatter_halving(value, axis, size, dim):
    index = lax.axis_index(axis)
    distance = size // 2
    while distance >= 1:
        half = value.shape[dim] // 2
        bit = (index // distance) % 2
        keep = lax.dynamic_slice_in_dim(value, bit * half, half, dim)
        send = lax.dynamic_slice_in_dim(value, (1 - bit) * half, half, dim)
        value = keep + exchange(send, axis, size, distance)
        distance //= 2
    return value


def rotate_pairs(vectors, positions):
    half_width = vectors.shape[-1] // 2
    exponents = jnp.arange(half_width, dtype=jnp.float32) * (2.0 / vectors.shape[-1])
    frequency = ROPE_BASE ** (-exponents)
    angles = positions.astype(jnp.float32)[..., None] * frequency
    cosine = jnp.cos(angles)
    sine_part = jnp.sin(angles)
    lower_half = vectors[..., :half_width]
    upper_half = vectors[..., half_width:]
    return jnp.concatenate(
        [
            lower_half * cosine - upper_half * sine_part,
            upper_half * cosine + lower_half * sine_part,
        ],
        axis=-1,
    )


def lineage(parents):
    steps_count, beam_count = parents.shape
    beam_ids = jnp.arange(beam_count, dtype=jnp.int32)
    line_rows = []
    anchor_rows = []
    for step_index in range(steps_count):
        current = beam_ids
        levels = [jnp.full((beam_count,), -1, jnp.int32) for level_index in range(steps_count)]
        for level_index in range(step_index, -1, -1):
            levels[level_index] = current
            current = parents[level_index][current]
        line_rows.append(jnp.stack(levels))
        anchor_rows.append(current)
    return (jnp.stack(line_rows), jnp.stack(anchor_rows))


def expert_rank(routes):
    steps_count, beam_count, pick_count = routes.shape
    onehot = (routes[..., None] == jnp.arange(EXPERTS, dtype=jnp.int32)).astype(jnp.int32)
    flat_hits = onehot.reshape(steps_count, beam_count * pick_count, EXPERTS)
    before = jnp.cumsum(flat_hits, axis=1) - flat_hits
    return jnp.sum(before * flat_hits, axis=-1).reshape(steps_count, beam_count, pick_count)


def head_total(partial_value, kv_size):
    return butterfly(partial_value, "kv", kv_size, add_parts)


def combine_parts(part_one, part_two):
    max_one, sum_one, vector_one = part_one
    max_two, sum_two, vector_two = part_two
    larger = jnp.maximum(max_one, max_two)
    scale_one = jnp.exp(max_one - larger)
    scale_two = jnp.exp(max_two - larger)
    return (
        larger,
        sum_one * scale_one + sum_two * scale_two,
        vector_one * scale_one[..., None] + vector_two * scale_two[..., None],
    )


def groups_to_beams(grouped):
    shaped = grouped.reshape((GROUPS, DECODE_STEPS, BEAM_W, QUERIES_PER_KEY) + grouped.shape[2:])
    shaped = jnp.moveaxis(shaped, 1, 0)
    return shaped.reshape((DECODE_STEPS, BEAM_TOTAL, QUERIES_PER_KEY) + grouped.shape[2:])


def body(
    hidden_in,
    attn_gain,
    ffn_gain,
    query_key_value_weight,
    out_weight,
    router_weight,
    expert_in,
    expert_down,
    kv_cache,
    lengths,
    tables,
    parents,
    routes,
    kv_size,
    blk_size,
):
    count_tokens = DECODE_STEPS * BEAM_TOTAL
    width_local = hidden_in.shape[2]
    heads_local = query_key_value_weight.shape[1]
    logit_scale = 1.0 / math.sqrt(HEAD_WIDTH)
    line_beams, anchor = lineage(parents)
    flat_in = hidden_in.reshape(count_tokens, width_local).astype(jnp.float32)
    pre_attn = (flat_in * attn_gain.astype(jnp.float32)).astype(jnp.bfloat16)
    partial_proj = jnp.dot(
        pre_attn,
        query_key_value_weight.reshape(width_local, -1),
        preferred_element_type=jnp.float32,
    )
    partial_sq = jnp.sum(flat_in * flat_in, axis=1)
    packed_proj = butterfly(
        jnp.concatenate([partial_proj, partial_sq[:, None]], axis=1), "blk", blk_size, add_parts
    )
    projected_rows = packed_proj[:, :-1]
    square_sum = packed_proj[:, -1]
    projected_rows = (
        projected_rows * lax.rsqrt(square_sum / MODEL_WIDTH + NORM_FLOOR)[:, None]
    ).reshape(DECODE_STEPS, BEAM_TOTAL, heads_local, QUERIES_PER_KEY + 2, HEAD_WIDTH)
    beam_groups = jnp.arange(BEAM_TOTAL, dtype=jnp.int32) // BEAM_W
    positions = lengths[beam_groups][None, :] + jnp.arange(DECODE_STEPS, dtype=jnp.int32)[:, None]
    queries = rotate_pairs(
        projected_rows[:, :, :, :QUERIES_PER_KEY], positions[:, :, None, None]
    ).astype(jnp.bfloat16)
    new_key = rotate_pairs(projected_rows[:, :, :, QUERIES_PER_KEY], positions[:, :, None]).astype(
        jnp.bfloat16
    )
    new_value = projected_rows[:, :, :, QUERIES_PER_KEY + 1].astype(jnp.bfloat16)
    slot_count = kv_cache.shape[0]
    slot_base = lax.axis_index("blk") * slot_count
    entry_ids = jnp.arange(BEAM_TOTAL * BEAM_BLOCKS, dtype=jnp.int32)
    slot_ids = slot_base + jnp.arange(slot_count, dtype=jnp.int32)
    slot_hits = tables.reshape(-1)[None, :] == slot_ids[:, None]
    entry_here = jnp.sum(jnp.where(slot_hits, entry_ids[None, :], 0), axis=1)
    owner_here = entry_here // BEAM_BLOCKS
    block_here = entry_here % BEAM_BLOCKS
    group_here = owner_here // BEAM_W
    live_keys = (
        block_here[:, None] * BLOCK_POSITIONS
        + jnp.arange(BLOCK_POSITIONS, dtype=jnp.int32)[None, :]
        < lengths[group_here][:, None]
    )
    anchor_groups = jnp.moveaxis(anchor.reshape(DECODE_STEPS, GROUPS, BEAM_W), 1, 0)
    anchor_query = jnp.broadcast_to(
        anchor_groups[..., None], (GROUPS, DECODE_STEPS, BEAM_W, QUERIES_PER_KEY)
    ).reshape(GROUPS, -1)
    query_match = anchor_query[group_here] == owner_here[:, None]
    group_hits = group_here[:, None] == jnp.arange(GROUPS, dtype=jnp.int32)[None, :]
    group_float = group_hits.astype(jnp.float32)
    recent_allowed = jnp.transpose(
        line_beams[:, :, :, None] == jnp.arange(BEAM_TOTAL, dtype=jnp.int32), (0, 2, 1, 3)
    ).reshape(DECODE_STEPS, BEAM_TOTAL, 1, count_tokens)
    is_first = lax.axis_index("blk") == 0
    query_head = queries[:, :, 0]
    query_groups = jnp.moveaxis(
        query_head.reshape(DECODE_STEPS, GROUPS, BEAM_W, QUERIES_PER_KEY, HEAD_WIDTH), 1, 0
    ).reshape(GROUPS, -1, HEAD_WIDTH)
    query_slots = query_groups[group_here]
    key_matrix = kv_cache[:, 0, 0]
    value_matrix = kv_cache[:, 1, 0]
    scores = (
        jnp.einsum("ptd,pqd->ptq", key_matrix, query_slots, preferred_element_type=jnp.float32)
        * logit_scale
    )
    allowed = live_keys[:, :, None] & query_match[:, None, :]
    masked = jnp.where(allowed, scores, NEG_FILL)
    slot_max = jnp.max(masked, axis=1)
    weights = jnp.where(allowed, jnp.exp(masked - slot_max[:, None, :]), 0.0)
    slot_sum = jnp.sum(weights, axis=1)
    slot_vector = jnp.einsum(
        "ptq,ptd->pqd",
        weights.astype(jnp.bfloat16),
        value_matrix,
        preferred_element_type=jnp.float32,
    )
    group_max = jnp.max(jnp.where(group_hits[:, :, None], slot_max[:, None, :], NEG_FILL), axis=0)
    rescale = jnp.exp(slot_max - group_max[group_here])
    group_sum = jnp.einsum(
        "pg,pq->gq", group_float, slot_sum * rescale, precision=lax.Precision.HIGHEST
    )
    group_vector = jnp.einsum(
        "pg,pqd->gqd",
        group_float,
        slot_vector * rescale[:, :, None],
        precision=lax.Precision.HIGHEST,
    )
    cache_max = groups_to_beams(group_max)
    cache_sum = groups_to_beams(group_sum)
    cache_vector = groups_to_beams(group_vector)
    newest_keys = new_key[:, :, 0].reshape(count_tokens, HEAD_WIDTH)
    newest_values = new_value[:, :, 0].reshape(count_tokens, HEAD_WIDTH)
    newest_logits = (
        jnp.einsum("sbqd,kd->sbqk", query_head, newest_keys, preferred_element_type=jnp.float32)
        * logit_scale
    )
    recent_masked = jnp.where(recent_allowed, newest_logits, NEG_FILL)
    recent_max = jnp.max(recent_masked, axis=-1)
    recent_weights = jnp.where(recent_allowed, jnp.exp(recent_masked - recent_max[..., None]), 0.0)
    recent_sum = jnp.sum(recent_weights, axis=-1)
    recent_vector = jnp.einsum(
        "sbqk,kd->sbqd",
        recent_weights.astype(jnp.bfloat16),
        newest_values,
        preferred_element_type=jnp.float32,
    )
    recent_max = jnp.where(is_first, recent_max, NEG_FILL)
    recent_sum = jnp.where(is_first, recent_sum, 0.0)
    recent_vector = jnp.where(is_first, recent_vector, 0.0)
    local_max, local_sum, local_vector = combine_parts(
        (cache_max, cache_sum, cache_vector), (recent_max, recent_sum, recent_vector)
    )
    max_heads = [local_max]
    sum_heads = [local_sum]
    vector_heads = [local_vector]
    part_max = jnp.stack(max_heads, axis=2)
    part_sum = jnp.stack(sum_heads, axis=2)
    part_vector = jnp.stack(vector_heads, axis=2)
    part_shape = part_max.shape
    vector_rows = part_vector.reshape(-1, HEAD_WIDTH)
    stat_rows = jnp.stack([part_max.reshape(-1), part_sum.reshape(-1)]).reshape(-1, HEAD_WIDTH)

    def packed_combine(first, second):
        def unpack(packed):
            stats = packed[vector_rows.shape[0] :].reshape(2, -1)
            return stats[0], stats[1], packed[: vector_rows.shape[0]]

        larger, total, vector = combine_parts(unpack(first), unpack(second))
        stats = jnp.stack([larger, total]).reshape(-1, HEAD_WIDTH)
        return jnp.concatenate([vector, stats], axis=0)

    whole_packed = butterfly(
        jnp.concatenate([vector_rows, stat_rows], axis=0), "blk", blk_size, packed_combine
    )
    whole_vector = whole_packed[: vector_rows.shape[0]].reshape(part_vector.shape)
    whole_sum = whole_packed[vector_rows.shape[0] :].reshape(2, -1)[1].reshape(part_shape)
    attended_rows = (
        (whole_vector / whole_sum[..., None]).astype(jnp.bfloat16).reshape(count_tokens, -1)
    )
    attn_partial = jnp.dot(attended_rows, out_weight, preferred_element_type=jnp.float32)
    attn_out = head_total(attn_partial, kv_size)
    residual = (flat_in + attn_out).astype(jnp.bfloat16)
    experts_local = expert_in.shape[0]
    ff_local = expert_in.shape[3]
    rows_per_expert = DECODE_STEPS * CAP
    rows_local = experts_local * rows_per_expert
    flat_routes = routes.reshape(count_tokens, 2)
    rank = expert_rank(routes).reshape(count_tokens, 2)
    step_of = jnp.arange(count_tokens, dtype=jnp.int32) // BEAM_TOTAL
    row_id = (flat_routes * rows_per_expert + step_of[:, None] * CAP + rank).reshape(-1)
    token_ids = jnp.broadcast_to(
        jnp.arange(count_tokens, dtype=jnp.int32)[:, None], (count_tokens, 2)
    ).reshape(-1)
    table_size = EXPERTS * rows_per_expert
    row_token_all = jnp.zeros((table_size,), jnp.int32).at[row_id].set(token_ids)
    row_live_all = jnp.zeros((table_size,), jnp.float32).at[row_id].set(1.0)
    row_other_all = (
        jnp.zeros((table_size,), jnp.int32).at[row_id].set(flat_routes[:, ::-1].reshape(-1))
    )
    row_start = lax.axis_index("kv") * rows_local
    row_token = lax.dynamic_slice_in_dim(row_token_all, row_start, rows_local)
    row_live = lax.dynamic_slice_in_dim(row_live_all, row_start, rows_local)
    row_other = lax.dynamic_slice_in_dim(row_other_all, row_start, rows_local)
    row_own = (row_start + jnp.arange(rows_local, dtype=jnp.int32)) // rows_per_expert
    in_flat = expert_in.reshape(experts_local, MODEL_WIDTH, 2 * ff_local)
    gain_wide = ffn_gain.astype(jnp.float32)
    full_rows = gather_doubling(residual, "blk", blk_size, 1)
    chosen = full_rows[row_token].astype(jnp.float32)
    pre_rows = (chosen * gain_wide).astype(jnp.bfloat16)
    sums_in = jnp.einsum(
        "erd,edf->erf",
        pre_rows.reshape(experts_local, rows_per_expert, MODEL_WIDTH),
        in_flat,
        preferred_element_type=jnp.float32,
    )
    sums_router = jnp.dot(pre_rows, router_weight, preferred_element_type=jnp.float32)
    sum_sq = jnp.sum(chosen * chosen, axis=1)
    inv_rows = lax.rsqrt(sum_sq / MODEL_WIDTH + NORM_FLOOR)
    expert_act = sums_in * inv_rows.reshape(experts_local, rows_per_expert)[:, :, None]
    expert_hidden = (jax.nn.silu(expert_act[..., :ff_local]) * expert_act[..., ff_local:]).astype(
        jnp.bfloat16
    )
    down_part = jnp.einsum(
        "erf,efd->erd", expert_hidden, expert_down, preferred_element_type=jnp.float32
    ).reshape(rows_local, MODEL_WIDTH)
    expert_result = scatter_halving(down_part, "blk", blk_size, 1)
    logits = sums_router * inv_rows[:, None]
    expert_ids = jnp.arange(EXPERTS, dtype=jnp.int32)
    own_logit = jnp.sum(jnp.where(row_own[:, None] == expert_ids[None, :], logits, 0.0), axis=1)
    other_logit = jnp.sum(jnp.where(row_other[:, None] == expert_ids[None, :], logits, 0.0), axis=1)
    gate_share = row_live / (1.0 + jnp.exp(other_logit - own_logit))
    weighted_values = expert_result * gate_share[:, None]
    placement = (row_token[None, :] == jnp.arange(count_tokens, dtype=jnp.int32)[:, None]).astype(
        jnp.float32
    )
    mixture_part = jnp.dot(placement, weighted_values, precision=lax.Precision.HIGHEST)
    mixture = head_total(mixture_part, kv_size)
    layer_out = (residual.astype(jnp.float32) + mixture).astype(jnp.bfloat16)
    return layer_out.reshape(DECODE_STEPS, BEAM_TOTAL, width_local)


def solution(mesh):
    placed = (
        P(None, None, "blk"),
        P("blk"),
        P(),
        P("blk", "kv", None),
        P("kv", "blk"),
        P(),
        P("kv", None, None, "blk"),
        P("kv", "blk", None),
        P("blk", None, "kv", None, None),
        P(),
        P(),
        P(),
        P(),
    )
    kv_size = mesh.shape["kv"]
    blk_size = mesh.shape["blk"]

    def sized(*arrays):
        return body(*arrays, kv_size, blk_size)

    return jax.shard_map(
        sized, mesh=mesh, in_specs=placed, out_specs=P(None, None, "blk"), check_vma=False
    )
```

```python
import math

import jax
import jax.numpy as jnp
from jax import lax
from jax.sharding import PartitionSpec as P

MODEL_WIDTH = 4096
HEAD_WIDTH = 128
QUERIES_PER_KEY = 4
EXPERTS = 8
BEAM_W = 8
GROUPS = 2
DECODE_STEPS = 4
BLOCK_POSITIONS = 128
BEAM_BLOCKS = 128
BEAM_TOTAL = 16
CAP = 6


NORM_FLOOR = 1e-05
ROPE_BASE = 1000000.0
NEG_FILL = -1e30
BLK_RADICES = (2, 4, 4)
SCATTER_RADICES = (4, 4, 2)
KV_RADICES = (8,)


def exchange(value, axis, size, distance):
    pairs = [(index, index ^ distance) for index in range(size)]
    return jax.tree.map(lambda part: lax.ppermute(part, axis, pairs), value)


def tree_join(parts, join):
    stride = 1
    while stride < len(parts):
        parts = [
            join(parts[place], parts[place + stride]) if place % (2 * stride) == 0 else parts[place]
            for place in range(len(parts))
        ]
        stride *= 2
    return parts[0]


def butterfly(value, axis, size, join, radices):
    distance = 1
    for radix in radices:
        parts = [value] + [
            exchange(value, axis, size, distance * offset) for offset in range(1, radix)
        ]
        value = tree_join(parts, join)
        distance *= radix
    assert distance == size
    return value


def add_parts(first, second):
    return jax.tree.map(lambda one, two: one + two, first, second)


def gather_doubling(block, axis, size, dim, radices):
    index = lax.axis_index(axis)
    distance = 1
    for radix in radices:
        place = (index // distance) % radix
        parts = [block] + [
            exchange(block, axis, size, distance * offset) for offset in range(1, radix)
        ]
        stacked = jnp.stack(parts)
        ordered = jnp.take(stacked, jnp.arange(radix, dtype=jnp.int32) ^ place, axis=0)
        block = jnp.concatenate([ordered[slot] for slot in range(radix)], dim)
        distance *= radix
    assert distance == size
    return block


def scatter_halving(value, axis, size, dim, radices):
    index = lax.axis_index(axis)
    distance = size
    for radix in radices:
        distance //= radix
        place = (index // distance) % radix
        piece = value.shape[dim] // radix
        received = [lax.dynamic_slice_in_dim(value, place * piece, piece, dim)]
        for offset in range(1, radix):
            send = lax.dynamic_slice_in_dim(value, (place ^ offset) * piece, piece, dim)
            received.append(exchange(send, axis, size, distance * offset))
        value = tree_join(received, add_parts)
    assert distance == 1
    return value


def rotate_pairs(vectors, positions):
    half_width = vectors.shape[-1] // 2
    exponents = jnp.arange(half_width, dtype=jnp.float32) * (2.0 / vectors.shape[-1])
    frequency = ROPE_BASE ** (-exponents)
    angles = positions.astype(jnp.float32)[..., None] * frequency
    cosine = jnp.cos(angles)
    sine_part = jnp.sin(angles)
    lower_half = vectors[..., :half_width]
    upper_half = vectors[..., half_width:]
    return jnp.concatenate(
        [
            lower_half * cosine - upper_half * sine_part,
            upper_half * cosine + lower_half * sine_part,
        ],
        axis=-1,
    )


def lineage(parents):
    steps_count, beam_count = parents.shape
    beam_ids = jnp.arange(beam_count, dtype=jnp.int32)
    line_rows = []
    anchor_rows = []
    for step_index in range(steps_count):
        current = beam_ids
        levels = [jnp.full((beam_count,), -1, jnp.int32) for level_index in range(steps_count)]
        for level_index in range(step_index, -1, -1):
            levels[level_index] = current
            current = parents[level_index][current]
        line_rows.append(jnp.stack(levels))
        anchor_rows.append(current)
    return (jnp.stack(line_rows), jnp.stack(anchor_rows))


def expert_rank(routes):
    steps_count, beam_count, pick_count = routes.shape
    onehot = (routes[..., None] == jnp.arange(EXPERTS, dtype=jnp.int32)).astype(jnp.int32)
    flat_hits = onehot.reshape(steps_count, beam_count * pick_count, EXPERTS)
    before = jnp.cumsum(flat_hits, axis=1) - flat_hits
    return jnp.sum(before * flat_hits, axis=-1).reshape(steps_count, beam_count, pick_count)


def head_total(partial_value, kv_size):
    return butterfly(partial_value, "kv", kv_size, add_parts, KV_RADICES)


def combine_parts(part_one, part_two):
    max_one, sum_one, vector_one = part_one
    max_two, sum_two, vector_two = part_two
    larger = jnp.maximum(max_one, max_two)
    scale_one = jnp.exp(max_one - larger)
    scale_two = jnp.exp(max_two - larger)
    return (
        larger,
        sum_one * scale_one + sum_two * scale_two,
        vector_one * scale_one[..., None] + vector_two * scale_two[..., None],
    )


def groups_to_beams(grouped):
    shaped = grouped.reshape((GROUPS, DECODE_STEPS, BEAM_W, QUERIES_PER_KEY) + grouped.shape[2:])
    shaped = jnp.moveaxis(shaped, 1, 0)
    return shaped.reshape((DECODE_STEPS, BEAM_TOTAL, QUERIES_PER_KEY) + grouped.shape[2:])


def body(
    hidden_in,
    attn_gain,
    ffn_gain,
    query_key_value_weight,
    out_weight,
    router_weight,
    expert_in,
    expert_down,
    kv_cache,
    lengths,
    tables,
    parents,
    routes,
    kv_size,
    blk_size,
):
    count_tokens = DECODE_STEPS * BEAM_TOTAL
    width_local = hidden_in.shape[2]
    heads_local = query_key_value_weight.shape[1]
    logit_scale = 1.0 / math.sqrt(HEAD_WIDTH)
    line_beams, anchor = lineage(parents)
    flat_in = hidden_in.reshape(count_tokens, width_local).astype(jnp.float32)
    pre_attn = (flat_in * attn_gain.astype(jnp.float32)).astype(jnp.bfloat16)
    partial_proj = jnp.dot(
        pre_attn,
        query_key_value_weight.reshape(width_local, -1),
        preferred_element_type=jnp.float32,
    )
    partial_sq = jnp.sum(flat_in * flat_in, axis=1)
    packed_proj = butterfly(
        jnp.concatenate([partial_proj, partial_sq[:, None]], axis=1), "blk", blk_size, add_parts, BLK_RADICES
    )
    projected_rows = packed_proj[:, :-1]
    square_sum = packed_proj[:, -1]
    projected_rows = (
        projected_rows * lax.rsqrt(square_sum / MODEL_WIDTH + NORM_FLOOR)[:, None]
    ).reshape(DECODE_STEPS, BEAM_TOTAL, heads_local, QUERIES_PER_KEY + 2, HEAD_WIDTH)
    beam_groups = jnp.arange(BEAM_TOTAL, dtype=jnp.int32) // BEAM_W
    positions = lengths[beam_groups][None, :] + jnp.arange(DECODE_STEPS, dtype=jnp.int32)[:, None]
    queries = rotate_pairs(
        projected_rows[:, :, :, :QUERIES_PER_KEY], positions[:, :, None, None]
    ).astype(jnp.bfloat16)
    new_key = rotate_pairs(projected_rows[:, :, :, QUERIES_PER_KEY], positions[:, :, None]).astype(
        jnp.bfloat16
    )
    new_value = projected_rows[:, :, :, QUERIES_PER_KEY + 1].astype(jnp.bfloat16)
    slot_count = kv_cache.shape[0]
    slot_base = lax.axis_index("blk") * slot_count
    entry_ids = jnp.arange(BEAM_TOTAL * BEAM_BLOCKS, dtype=jnp.int32)
    slot_ids = slot_base + jnp.arange(slot_count, dtype=jnp.int32)
    slot_hits = tables.reshape(-1)[None, :] == slot_ids[:, None]
    entry_here = jnp.sum(jnp.where(slot_hits, entry_ids[None, :], 0), axis=1)
    owner_here = entry_here // BEAM_BLOCKS
    block_here = entry_here % BEAM_BLOCKS
    group_here = owner_here // BEAM_W
    live_keys = (
        block_here[:, None] * BLOCK_POSITIONS
        + jnp.arange(BLOCK_POSITIONS, dtype=jnp.int32)[None, :]
        < lengths[group_here][:, None]
    )
    anchor_groups = jnp.moveaxis(anchor.reshape(DECODE_STEPS, GROUPS, BEAM_W), 1, 0)
    anchor_query = jnp.broadcast_to(
        anchor_groups[..., None], (GROUPS, DECODE_STEPS, BEAM_W, QUERIES_PER_KEY)
    ).reshape(GROUPS, -1)
    query_match = anchor_query[group_here] == owner_here[:, None]
    group_hits = group_here[:, None] == jnp.arange(GROUPS, dtype=jnp.int32)[None, :]
    group_float = group_hits.astype(jnp.float32)
    recent_allowed = jnp.transpose(
        line_beams[:, :, :, None] == jnp.arange(BEAM_TOTAL, dtype=jnp.int32), (0, 2, 1, 3)
    ).reshape(DECODE_STEPS, BEAM_TOTAL, 1, count_tokens)
    is_first = lax.axis_index("blk") == 0
    query_head = queries[:, :, 0]
    query_groups = jnp.moveaxis(
        query_head.reshape(DECODE_STEPS, GROUPS, BEAM_W, QUERIES_PER_KEY, HEAD_WIDTH), 1, 0
    ).reshape(GROUPS, -1, HEAD_WIDTH)
    query_slots = query_groups[group_here]
    key_matrix = kv_cache[:, 0, 0]
    value_matrix = kv_cache[:, 1, 0]
    scores = (
        jnp.einsum("ptd,pqd->ptq", key_matrix, query_slots, preferred_element_type=jnp.float32)
        * logit_scale
    )
    allowed = live_keys[:, :, None] & query_match[:, None, :]
    masked = jnp.where(allowed, scores, NEG_FILL)
    slot_max = jnp.max(masked, axis=1)
    weights = jnp.where(allowed, jnp.exp(masked - slot_max[:, None, :]), 0.0)
    slot_sum = jnp.sum(weights, axis=1)
    slot_vector = jnp.einsum(
        "ptq,ptd->pqd",
        weights.astype(jnp.bfloat16),
        value_matrix,
        preferred_element_type=jnp.float32,
    )
    group_max = jnp.max(jnp.where(group_hits[:, :, None], slot_max[:, None, :], NEG_FILL), axis=0)
    rescale = jnp.exp(slot_max - group_max[group_here])
    group_sum = jnp.einsum(
        "pg,pq->gq", group_float, slot_sum * rescale, precision=lax.Precision.HIGHEST
    )
    group_vector = jnp.einsum(
        "pg,pqd->gqd",
        group_float,
        slot_vector * rescale[:, :, None],
        precision=lax.Precision.HIGHEST,
    )
    cache_max = groups_to_beams(group_max)
    cache_sum = groups_to_beams(group_sum)
    cache_vector = groups_to_beams(group_vector)
    newest_keys = new_key[:, :, 0].reshape(count_tokens, HEAD_WIDTH)
    newest_values = new_value[:, :, 0].reshape(count_tokens, HEAD_WIDTH)
    newest_logits = (
        jnp.einsum("sbqd,kd->sbqk", query_head, newest_keys, preferred_element_type=jnp.float32)
        * logit_scale
    )
    recent_masked = jnp.where(recent_allowed, newest_logits, NEG_FILL)
    recent_max = jnp.max(recent_masked, axis=-1)
    recent_weights = jnp.where(recent_allowed, jnp.exp(recent_masked - recent_max[..., None]), 0.0)
    recent_sum = jnp.sum(recent_weights, axis=-1)
    recent_vector = jnp.einsum(
        "sbqk,kd->sbqd",
        recent_weights.astype(jnp.bfloat16),
        newest_values,
        preferred_element_type=jnp.float32,
    )
    recent_max = jnp.where(is_first, recent_max, NEG_FILL)
    recent_sum = jnp.where(is_first, recent_sum, 0.0)
    recent_vector = jnp.where(is_first, recent_vector, 0.0)
    local_max, local_sum, local_vector = combine_parts(
        (cache_max, cache_sum, cache_vector), (recent_max, recent_sum, recent_vector)
    )
    max_heads = [local_max]
    sum_heads = [local_sum]
    vector_heads = [local_vector]
    part_max = jnp.stack(max_heads, axis=2)
    part_sum = jnp.stack(sum_heads, axis=2)
    part_vector = jnp.stack(vector_heads, axis=2)
    part_shape = part_max.shape
    vector_rows = part_vector.reshape(-1, HEAD_WIDTH)
    stat_rows = jnp.stack([part_max.reshape(-1), part_sum.reshape(-1)]).reshape(-1, HEAD_WIDTH)

    def packed_combine(first, second):
        def unpack(packed):
            stats = packed[vector_rows.shape[0] :].reshape(2, -1)
            return stats[0], stats[1], packed[: vector_rows.shape[0]]

        larger, total, vector = combine_parts(unpack(first), unpack(second))
        stats = jnp.stack([larger, total]).reshape(-1, HEAD_WIDTH)
        return jnp.concatenate([vector, stats], axis=0)

    whole_packed = butterfly(
        jnp.concatenate([vector_rows, stat_rows], axis=0), "blk", blk_size, packed_combine, BLK_RADICES
    )
    whole_vector = whole_packed[: vector_rows.shape[0]].reshape(part_vector.shape)
    whole_sum = whole_packed[vector_rows.shape[0] :].reshape(2, -1)[1].reshape(part_shape)
    attended_rows = (
        (whole_vector / whole_sum[..., None]).astype(jnp.bfloat16).reshape(count_tokens, -1)
    )
    attn_partial = jnp.dot(attended_rows, out_weight, preferred_element_type=jnp.float32)
    attn_out = head_total(attn_partial, kv_size)
    residual = (flat_in + attn_out).astype(jnp.bfloat16)
    experts_local = expert_in.shape[0]
    ff_local = expert_in.shape[3]
    rows_per_expert = DECODE_STEPS * CAP
    rows_local = experts_local * rows_per_expert
    flat_routes = routes.reshape(count_tokens, 2)
    rank = expert_rank(routes).reshape(count_tokens, 2)
    step_of = jnp.arange(count_tokens, dtype=jnp.int32) // BEAM_TOTAL
    row_id = (flat_routes * rows_per_expert + step_of[:, None] * CAP + rank).reshape(-1)
    token_ids = jnp.broadcast_to(
        jnp.arange(count_tokens, dtype=jnp.int32)[:, None], (count_tokens, 2)
    ).reshape(-1)
    table_size = EXPERTS * rows_per_expert
    row_token_all = jnp.zeros((table_size,), jnp.int32).at[row_id].set(token_ids)
    row_live_all = jnp.zeros((table_size,), jnp.float32).at[row_id].set(1.0)
    row_other_all = (
        jnp.zeros((table_size,), jnp.int32).at[row_id].set(flat_routes[:, ::-1].reshape(-1))
    )
    row_start = lax.axis_index("kv") * rows_local
    row_token = lax.dynamic_slice_in_dim(row_token_all, row_start, rows_local)
    row_live = lax.dynamic_slice_in_dim(row_live_all, row_start, rows_local)
    row_other = lax.dynamic_slice_in_dim(row_other_all, row_start, rows_local)
    row_own = (row_start + jnp.arange(rows_local, dtype=jnp.int32)) // rows_per_expert
    in_flat = expert_in.reshape(experts_local, MODEL_WIDTH, 2 * ff_local)
    gain_wide = ffn_gain.astype(jnp.float32)
    full_rows = gather_doubling(residual, "blk", blk_size, 1, BLK_RADICES)
    chosen = full_rows[row_token].astype(jnp.float32)
    pre_rows = (chosen * gain_wide).astype(jnp.bfloat16)
    sums_in = jnp.einsum(
        "erd,edf->erf",
        pre_rows.reshape(experts_local, rows_per_expert, MODEL_WIDTH),
        in_flat,
        preferred_element_type=jnp.float32,
    )
    sums_router = jnp.dot(pre_rows, router_weight, preferred_element_type=jnp.float32)
    sum_sq = jnp.sum(chosen * chosen, axis=1)
    inv_rows = lax.rsqrt(sum_sq / MODEL_WIDTH + NORM_FLOOR)
    expert_act = sums_in * inv_rows.reshape(experts_local, rows_per_expert)[:, :, None]
    expert_hidden = (jax.nn.silu(expert_act[..., :ff_local]) * expert_act[..., ff_local:]).astype(
        jnp.bfloat16
    )
    down_part = jnp.einsum(
        "erf,efd->erd", expert_hidden, expert_down, preferred_element_type=jnp.float32
    ).reshape(rows_local, MODEL_WIDTH)
    expert_result = scatter_halving(down_part, "blk", blk_size, 1, SCATTER_RADICES)
    logits = sums_router * inv_rows[:, None]
    expert_ids = jnp.arange(EXPERTS, dtype=jnp.int32)
    own_logit = jnp.sum(jnp.where(row_own[:, None] == expert_ids[None, :], logits, 0.0), axis=1)
    other_logit = jnp.sum(jnp.where(row_other[:, None] == expert_ids[None, :], logits, 0.0), axis=1)
    gate_share = row_live / (1.0 + jnp.exp(other_logit - own_logit))
    weighted_values = expert_result * gate_share[:, None]
    placement = (row_token[None, :] == jnp.arange(count_tokens, dtype=jnp.int32)[:, None]).astype(
        jnp.float32
    )
    mixture_part = jnp.dot(placement, weighted_values, precision=lax.Precision.HIGHEST)
    mixture = head_total(mixture_part, kv_size)
    layer_out = (residual.astype(jnp.float32) + mixture).astype(jnp.bfloat16)
    return layer_out.reshape(DECODE_STEPS, BEAM_TOTAL, width_local)


def solution(mesh):
    placed = (
        P(None, None, "blk"),
        P("blk"),
        P(),
        P("blk", "kv", None),
        P("kv", "blk"),
        P(),
        P("kv", None, None, "blk"),
        P("kv", "blk", None),
        P("blk", None, "kv", None, None),
        P(),
        P(),
        P(),
        P(),
    )
    kv_size = mesh.shape["kv"]
    blk_size = mesh.shape["blk"]

    def sized(*arrays):
        return body(*arrays, kv_size, blk_size)

    return jax.shard_map(
        sized, mesh=mesh, in_specs=placed, out_specs=P(None, None, "blk"), check_vma=False
    )
```

```python
import math

import jax
import jax.numpy as jnp
from jax import lax
from jax.sharding import PartitionSpec as P

MODEL_WIDTH = 4096
HEAD_WIDTH = 128
QUERIES_PER_KEY = 4
EXPERTS = 8
BEAM_W = 8
GROUPS = 2
DECODE_STEPS = 4
BLOCK_POSITIONS = 128
BEAM_BLOCKS = 128
BEAM_TOTAL = 16
CAP = 6


NORM_FLOOR = 1e-05
ROPE_BASE = 1000000.0
NEG_FILL = -1e30
BLK_RADICES = (2, 4, 4)
SCATTER_RADICES = (4, 4, 2)
KV_RADICES = (2, 2, 2)


def exchange(value, axis, size, distance):
    pairs = [(index, index ^ distance) for index in range(size)]
    return jax.tree.map(lambda part: lax.ppermute(part, axis, pairs), value)


def tree_join(parts, join):
    stride = 1
    while stride < len(parts):
        parts = [
            join(parts[place], parts[place + stride]) if place % (2 * stride) == 0 else parts[place]
            for place in range(len(parts))
        ]
        stride *= 2
    return parts[0]


def butterfly(value, axis, size, join, radices):
    distance = 1
    for radix in radices:
        parts = [value] + [
            exchange(value, axis, size, distance * offset) for offset in range(1, radix)
        ]
        value = tree_join(parts, join)
        distance *= radix
    assert distance == size
    return value


def add_parts(first, second):
    return jax.tree.map(lambda one, two: one + two, first, second)


def gather_doubling(block, axis, size, dim, radices):
    index = lax.axis_index(axis)
    distance = 1
    for radix in radices:
        place = (index // distance) % radix
        parts = [block] + [
            exchange(block, axis, size, distance * offset) for offset in range(1, radix)
        ]
        stacked = jnp.stack(parts)
        ordered = jnp.take(stacked, jnp.arange(radix, dtype=jnp.int32) ^ place, axis=0)
        block = jnp.concatenate([ordered[slot] for slot in range(radix)], dim)
        distance *= radix
    assert distance == size
    return block


def scatter_halving(value, axis, size, dim, radices):
    index = lax.axis_index(axis)
    distance = size
    for radix in radices:
        distance //= radix
        place = (index // distance) % radix
        piece = value.shape[dim] // radix
        received = [lax.dynamic_slice_in_dim(value, place * piece, piece, dim)]
        for offset in range(1, radix):
            send = lax.dynamic_slice_in_dim(value, (place ^ offset) * piece, piece, dim)
            received.append(exchange(send, axis, size, distance * offset))
        value = tree_join(received, add_parts)
    assert distance == 1
    return value


def rotate_pairs(vectors, positions):
    half_width = vectors.shape[-1] // 2
    exponents = jnp.arange(half_width, dtype=jnp.float32) * (2.0 / vectors.shape[-1])
    frequency = ROPE_BASE ** (-exponents)
    angles = positions.astype(jnp.float32)[..., None] * frequency
    cosine = jnp.cos(angles)
    sine_part = jnp.sin(angles)
    lower_half = vectors[..., :half_width]
    upper_half = vectors[..., half_width:]
    return jnp.concatenate(
        [
            lower_half * cosine - upper_half * sine_part,
            upper_half * cosine + lower_half * sine_part,
        ],
        axis=-1,
    )


def lineage(parents):
    steps_count, beam_count = parents.shape
    beam_ids = jnp.arange(beam_count, dtype=jnp.int32)
    line_rows = []
    anchor_rows = []
    for step_index in range(steps_count):
        current = beam_ids
        levels = [jnp.full((beam_count,), -1, jnp.int32) for level_index in range(steps_count)]
        for level_index in range(step_index, -1, -1):
            levels[level_index] = current
            current = parents[level_index][current]
        line_rows.append(jnp.stack(levels))
        anchor_rows.append(current)
    return (jnp.stack(line_rows), jnp.stack(anchor_rows))


def expert_rank(routes):
    steps_count, beam_count, pick_count = routes.shape
    onehot = (routes[..., None] == jnp.arange(EXPERTS, dtype=jnp.int32)).astype(jnp.int32)
    flat_hits = onehot.reshape(steps_count, beam_count * pick_count, EXPERTS)
    before = jnp.cumsum(flat_hits, axis=1) - flat_hits
    return jnp.sum(before * flat_hits, axis=-1).reshape(steps_count, beam_count, pick_count)


def head_total(partial_value, kv_size):
    return butterfly(partial_value, "kv", kv_size, add_parts, KV_RADICES)


def combine_parts(part_one, part_two):
    max_one, sum_one, vector_one = part_one
    max_two, sum_two, vector_two = part_two
    larger = jnp.maximum(max_one, max_two)
    scale_one = jnp.exp(max_one - larger)
    scale_two = jnp.exp(max_two - larger)
    return (
        larger,
        sum_one * scale_one + sum_two * scale_two,
        vector_one * scale_one[..., None] + vector_two * scale_two[..., None],
    )


def groups_to_beams(grouped):
    shaped = grouped.reshape((GROUPS, DECODE_STEPS, BEAM_W, QUERIES_PER_KEY) + grouped.shape[2:])
    shaped = jnp.moveaxis(shaped, 1, 0)
    return shaped.reshape((DECODE_STEPS, BEAM_TOTAL, QUERIES_PER_KEY) + grouped.shape[2:])


def body(
    hidden_in,
    attn_gain,
    ffn_gain,
    query_key_value_weight,
    out_weight,
    router_weight,
    expert_in,
    expert_down,
    kv_cache,
    lengths,
    tables,
    parents,
    routes,
    kv_size,
    blk_size,
):
    count_tokens = DECODE_STEPS * BEAM_TOTAL
    width_local = hidden_in.shape[2]
    heads_local = query_key_value_weight.shape[1]
    logit_scale = 1.0 / math.sqrt(HEAD_WIDTH)
    line_beams, anchor = lineage(parents)
    flat_in = hidden_in.reshape(count_tokens, width_local).astype(jnp.float32)
    pre_attn = (flat_in * attn_gain.astype(jnp.float32)).astype(jnp.bfloat16)
    partial_proj = jnp.dot(
        pre_attn,
        query_key_value_weight.reshape(width_local, -1),
        preferred_element_type=jnp.float32,
    )
    partial_sq = jnp.sum(flat_in * flat_in, axis=1)
    packed_proj = butterfly(
        jnp.concatenate([partial_proj, partial_sq[:, None]], axis=1), "blk", blk_size, add_parts, BLK_RADICES
    )
    projected_rows = packed_proj[:, :-1]
    square_sum = packed_proj[:, -1]
    projected_rows = (
        projected_rows * lax.rsqrt(square_sum / MODEL_WIDTH + NORM_FLOOR)[:, None]
    ).reshape(DECODE_STEPS, BEAM_TOTAL, heads_local, QUERIES_PER_KEY + 2, HEAD_WIDTH)
    beam_groups = jnp.arange(BEAM_TOTAL, dtype=jnp.int32) // BEAM_W
    positions = lengths[beam_groups][None, :] + jnp.arange(DECODE_STEPS, dtype=jnp.int32)[:, None]
    queries = rotate_pairs(
        projected_rows[:, :, :, :QUERIES_PER_KEY], positions[:, :, None, None]
    ).astype(jnp.bfloat16)
    new_key = rotate_pairs(projected_rows[:, :, :, QUERIES_PER_KEY], positions[:, :, None]).astype(
        jnp.bfloat16
    )
    new_value = projected_rows[:, :, :, QUERIES_PER_KEY + 1].astype(jnp.bfloat16)
    slot_count = kv_cache.shape[0]
    slot_base = lax.axis_index("blk") * slot_count
    entry_ids = jnp.arange(BEAM_TOTAL * BEAM_BLOCKS, dtype=jnp.int32)
    slot_ids = slot_base + jnp.arange(slot_count, dtype=jnp.int32)
    slot_hits = tables.reshape(-1)[None, :] == slot_ids[:, None]
    entry_here = jnp.sum(jnp.where(slot_hits, entry_ids[None, :], 0), axis=1)
    owner_here = entry_here // BEAM_BLOCKS
    block_here = entry_here % BEAM_BLOCKS
    group_here = owner_here // BEAM_W
    live_keys = (
        block_here[:, None] * BLOCK_POSITIONS
        + jnp.arange(BLOCK_POSITIONS, dtype=jnp.int32)[None, :]
        < lengths[group_here][:, None]
    )
    anchor_groups = jnp.moveaxis(anchor.reshape(DECODE_STEPS, GROUPS, BEAM_W), 1, 0)
    anchor_query = jnp.broadcast_to(
        anchor_groups[..., None], (GROUPS, DECODE_STEPS, BEAM_W, QUERIES_PER_KEY)
    ).reshape(GROUPS, -1)
    query_match = anchor_query[group_here] == owner_here[:, None]
    group_hits = group_here[:, None] == jnp.arange(GROUPS, dtype=jnp.int32)[None, :]
    group_float = group_hits.astype(jnp.float32)
    recent_allowed = jnp.transpose(
        line_beams[:, :, :, None] == jnp.arange(BEAM_TOTAL, dtype=jnp.int32), (0, 2, 1, 3)
    ).reshape(DECODE_STEPS, BEAM_TOTAL, 1, count_tokens)
    is_first = lax.axis_index("blk") == 0
    query_head = queries[:, :, 0]
    query_groups = jnp.moveaxis(
        query_head.reshape(DECODE_STEPS, GROUPS, BEAM_W, QUERIES_PER_KEY, HEAD_WIDTH), 1, 0
    ).reshape(GROUPS, -1, HEAD_WIDTH)
    query_slots = query_groups[group_here]
    key_matrix = kv_cache[:, 0, 0]
    value_matrix = kv_cache[:, 1, 0]
    scores = (
        jnp.einsum("ptd,pqd->ptq", key_matrix, query_slots, preferred_element_type=jnp.float32)
        * logit_scale
    )
    allowed = live_keys[:, :, None] & query_match[:, None, :]
    masked = jnp.where(allowed, scores, NEG_FILL)
    slot_max = jnp.max(masked, axis=1)
    weights = jnp.where(allowed, jnp.exp(masked - slot_max[:, None, :]), 0.0)
    slot_sum = jnp.sum(weights, axis=1)
    slot_vector = jnp.einsum(
        "ptq,ptd->pqd",
        weights.astype(jnp.bfloat16),
        value_matrix,
        preferred_element_type=jnp.float32,
    )
    group_max = jnp.max(jnp.where(group_hits[:, :, None], slot_max[:, None, :], NEG_FILL), axis=0)
    rescale = jnp.exp(slot_max - group_max[group_here])
    group_sum = jnp.einsum(
        "pg,pq->gq", group_float, slot_sum * rescale, precision=lax.Precision.HIGHEST
    )
    group_vector = jnp.einsum(
        "pg,pqd->gqd",
        group_float,
        slot_vector * rescale[:, :, None],
        precision=lax.Precision.HIGHEST,
    )
    cache_max = groups_to_beams(group_max)
    cache_sum = groups_to_beams(group_sum)
    cache_vector = groups_to_beams(group_vector)
    newest_keys = new_key[:, :, 0].reshape(count_tokens, HEAD_WIDTH)
    newest_values = new_value[:, :, 0].reshape(count_tokens, HEAD_WIDTH)
    newest_logits = (
        jnp.einsum("sbqd,kd->sbqk", query_head, newest_keys, preferred_element_type=jnp.float32)
        * logit_scale
    )
    recent_masked = jnp.where(recent_allowed, newest_logits, NEG_FILL)
    recent_max = jnp.max(recent_masked, axis=-1)
    recent_weights = jnp.where(recent_allowed, jnp.exp(recent_masked - recent_max[..., None]), 0.0)
    recent_sum = jnp.sum(recent_weights, axis=-1)
    recent_vector = jnp.einsum(
        "sbqk,kd->sbqd",
        recent_weights.astype(jnp.bfloat16),
        newest_values,
        preferred_element_type=jnp.float32,
    )
    recent_max = jnp.where(is_first, recent_max, NEG_FILL)
    recent_sum = jnp.where(is_first, recent_sum, 0.0)
    recent_vector = jnp.where(is_first, recent_vector, 0.0)
    local_max, local_sum, local_vector = combine_parts(
        (cache_max, cache_sum, cache_vector), (recent_max, recent_sum, recent_vector)
    )
    max_heads = [local_max]
    sum_heads = [local_sum]
    vector_heads = [local_vector]
    part_max = jnp.stack(max_heads, axis=2)
    part_sum = jnp.stack(sum_heads, axis=2)
    part_vector = jnp.stack(vector_heads, axis=2)
    part_shape = part_max.shape
    vector_rows = part_vector.reshape(-1, HEAD_WIDTH)
    stat_rows = jnp.stack([part_max.reshape(-1), part_sum.reshape(-1)]).reshape(-1, HEAD_WIDTH)

    def packed_combine(first, second):
        def unpack(packed):
            stats = packed[vector_rows.shape[0] :].reshape(2, -1)
            return stats[0], stats[1], packed[: vector_rows.shape[0]]

        larger, total, vector = combine_parts(unpack(first), unpack(second))
        stats = jnp.stack([larger, total]).reshape(-1, HEAD_WIDTH)
        return jnp.concatenate([vector, stats], axis=0)

    whole_packed = butterfly(
        jnp.concatenate([vector_rows, stat_rows], axis=0), "blk", blk_size, packed_combine, BLK_RADICES
    )
    whole_vector = whole_packed[: vector_rows.shape[0]].reshape(part_vector.shape)
    whole_sum = whole_packed[vector_rows.shape[0] :].reshape(2, -1)[1].reshape(part_shape)
    attended_rows = (
        (whole_vector / whole_sum[..., None]).astype(jnp.bfloat16).reshape(count_tokens, -1)
    )
    attn_partial = jnp.dot(attended_rows, out_weight, preferred_element_type=jnp.float32)
    attn_out = head_total(attn_partial, kv_size)
    residual = (flat_in + attn_out).astype(jnp.bfloat16)
    experts_local = expert_in.shape[0]
    ff_local = expert_in.shape[3]
    rows_per_expert = DECODE_STEPS * CAP
    rows_local = experts_local * rows_per_expert
    flat_routes = routes.reshape(count_tokens, 2)
    rank = expert_rank(routes).reshape(count_tokens, 2)
    step_of = jnp.arange(count_tokens, dtype=jnp.int32) // BEAM_TOTAL
    row_id = (flat_routes * rows_per_expert + step_of[:, None] * CAP + rank).reshape(-1)
    token_ids = jnp.broadcast_to(
        jnp.arange(count_tokens, dtype=jnp.int32)[:, None], (count_tokens, 2)
    ).reshape(-1)
    table_size = EXPERTS * rows_per_expert
    row_token_all = jnp.zeros((table_size,), jnp.int32).at[row_id].set(token_ids)
    row_live_all = jnp.zeros((table_size,), jnp.float32).at[row_id].set(1.0)
    row_other_all = (
        jnp.zeros((table_size,), jnp.int32).at[row_id].set(flat_routes[:, ::-1].reshape(-1))
    )
    row_start = lax.axis_index("kv") * rows_local
    row_token = lax.dynamic_slice_in_dim(row_token_all, row_start, rows_local)
    row_live = lax.dynamic_slice_in_dim(row_live_all, row_start, rows_local)
    row_other = lax.dynamic_slice_in_dim(row_other_all, row_start, rows_local)
    row_own = (row_start + jnp.arange(rows_local, dtype=jnp.int32)) // rows_per_expert
    in_flat = expert_in.reshape(experts_local, MODEL_WIDTH, 2 * ff_local)
    gain_wide = ffn_gain.astype(jnp.float32)
    full_rows = jnp.moveaxis(
        lax.all_to_all(
            jnp.broadcast_to(residual[None], (blk_size,) + residual.shape), "blk", 0, 0, tiled=True
        ),
        0,
        1,
    ).reshape(residual.shape[0], -1)
    chosen = full_rows[row_token].astype(jnp.float32)
    pre_rows = (chosen * gain_wide).astype(jnp.bfloat16)
    sums_in = jnp.einsum(
        "erd,edf->erf",
        pre_rows.reshape(experts_local, rows_per_expert, MODEL_WIDTH),
        in_flat,
        preferred_element_type=jnp.float32,
    )
    sums_router = jnp.dot(pre_rows, router_weight, preferred_element_type=jnp.float32)
    sum_sq = jnp.sum(chosen * chosen, axis=1)
    inv_rows = lax.rsqrt(sum_sq / MODEL_WIDTH + NORM_FLOOR)
    expert_act = sums_in * inv_rows.reshape(experts_local, rows_per_expert)[:, :, None]
    expert_hidden = (jax.nn.silu(expert_act[..., :ff_local]) * expert_act[..., ff_local:]).astype(
        jnp.bfloat16
    )
    down_part = jnp.einsum(
        "erf,efd->erd", expert_hidden, expert_down, preferred_element_type=jnp.float32
    ).reshape(rows_local, MODEL_WIDTH)
    expert_pieces = jnp.moveaxis(down_part.reshape(rows_local, blk_size, -1), 1, 0)
    expert_result = jnp.sum(lax.all_to_all(expert_pieces, "blk", 0, 0, tiled=True), axis=0)
    logits = sums_router * inv_rows[:, None]
    expert_ids = jnp.arange(EXPERTS, dtype=jnp.int32)
    own_logit = jnp.sum(jnp.where(row_own[:, None] == expert_ids[None, :], logits, 0.0), axis=1)
    other_logit = jnp.sum(jnp.where(row_other[:, None] == expert_ids[None, :], logits, 0.0), axis=1)
    gate_share = row_live / (1.0 + jnp.exp(other_logit - own_logit))
    weighted_values = expert_result * gate_share[:, None]
    placement = (row_token[None, :] == jnp.arange(count_tokens, dtype=jnp.int32)[:, None]).astype(
        jnp.float32
    )
    mixture_part = jnp.dot(placement, weighted_values, precision=lax.Precision.HIGHEST)
    mixture = head_total(mixture_part, kv_size)
    layer_out = (residual.astype(jnp.float32) + mixture).astype(jnp.bfloat16)
    return layer_out.reshape(DECODE_STEPS, BEAM_TOTAL, width_local)


def solution(mesh):
    placed = (
        P(None, None, "blk"),
        P("blk"),
        P(),
        P("blk", "kv", None),
        P("kv", "blk"),
        P(),
        P("kv", None, None, "blk"),
        P("kv", "blk", None),
        P("blk", None, "kv", None, None),
        P(),
        P(),
        P(),
        P(),
    )
    kv_size = mesh.shape["kv"]
    blk_size = mesh.shape["blk"]

    def sized(*arrays):
        return body(*arrays, kv_size, blk_size)

    return jax.shard_map(
        sized, mesh=mesh, in_specs=placed, out_specs=P(None, None, "blk"), check_vma=False
    )
```

```python
import math

import jax
import jax.numpy as jnp
from jax import lax
from jax.sharding import PartitionSpec as P

MODEL_WIDTH = 4096
HEAD_WIDTH = 128
QUERIES_PER_KEY = 4
EXPERTS = 8
BEAM_W = 8
GROUPS = 2
DECODE_STEPS = 4
BLOCK_POSITIONS = 128
BEAM_BLOCKS = 128
BEAM_TOTAL = 16
CAP = 6


NORM_FLOOR = 1e-05
ROPE_BASE = 1000000.0
NEG_FILL = -1e30
BLK_RADICES = (2, 4, 4)
SCATTER_RADICES = (4, 4, 2)
KV_RADICES = (2, 2, 2)


def exchange(value, axis, size, distance):
    pairs = [(index, index ^ distance) for index in range(size)]
    return jax.tree.map(lambda part: lax.ppermute(part, axis, pairs), value)


def tree_join(parts, join):
    stride = 1
    while stride < len(parts):
        parts = [
            join(parts[place], parts[place + stride]) if place % (2 * stride) == 0 else parts[place]
            for place in range(len(parts))
        ]
        stride *= 2
    return parts[0]


def butterfly(value, axis, size, join, radices):
    distance = 1
    for radix in radices:
        parts = [value] + [
            exchange(value, axis, size, distance * offset) for offset in range(1, radix)
        ]
        value = tree_join(parts, join)
        distance *= radix
    assert distance == size
    return value


def add_parts(first, second):
    return jax.tree.map(lambda one, two: one + two, first, second)


def gather_doubling(block, axis, size, dim, radices):
    index = lax.axis_index(axis)
    distance = 1
    for radix in radices:
        place = (index // distance) % radix
        parts = [block] + [
            exchange(block, axis, size, distance * offset) for offset in range(1, radix)
        ]
        stacked = jnp.stack(parts)
        ordered = jnp.take(stacked, jnp.arange(radix, dtype=jnp.int32) ^ place, axis=0)
        block = jnp.concatenate([ordered[slot] for slot in range(radix)], dim)
        distance *= radix
    assert distance == size
    return block


def scatter_halving(value, axis, size, dim, radices):
    index = lax.axis_index(axis)
    distance = size
    for radix in radices:
        distance //= radix
        place = (index // distance) % radix
        piece = value.shape[dim] // radix
        received = [lax.dynamic_slice_in_dim(value, place * piece, piece, dim)]
        for offset in range(1, radix):
            send = lax.dynamic_slice_in_dim(value, (place ^ offset) * piece, piece, dim)
            received.append(exchange(send, axis, size, distance * offset))
        value = tree_join(received, add_parts)
    assert distance == 1
    return value


def rotate_pairs(vectors, positions):
    half_width = vectors.shape[-1] // 2
    exponents = jnp.arange(half_width, dtype=jnp.float32) * (2.0 / vectors.shape[-1])
    frequency = ROPE_BASE ** (-exponents)
    angles = positions.astype(jnp.float32)[..., None] * frequency
    cosine = jnp.cos(angles)
    sine_part = jnp.sin(angles)
    lower_half = vectors[..., :half_width]
    upper_half = vectors[..., half_width:]
    return jnp.concatenate(
        [
            lower_half * cosine - upper_half * sine_part,
            upper_half * cosine + lower_half * sine_part,
        ],
        axis=-1,
    )


def lookup(table, index):
    hits = index[..., None] == jnp.arange(table.shape[0], dtype=jnp.int32)
    shaped = hits.reshape(hits.shape + (1,) * (table.ndim - 1))
    return jnp.sum(jnp.where(shaped, table, jnp.zeros((), table.dtype)), axis=index.ndim)


def lineage(parents):
    steps_count, beam_count = parents.shape
    beam_ids = jnp.arange(beam_count, dtype=jnp.int32)
    line_rows = []
    anchor_rows = []
    for step_index in range(steps_count):
        current = beam_ids
        levels = [jnp.full((beam_count,), -1, jnp.int32) for level_index in range(steps_count)]
        for level_index in range(step_index, -1, -1):
            levels[level_index] = current
            current = lookup(parents[level_index], current)
        line_rows.append(jnp.stack(levels))
        anchor_rows.append(current)
    return (jnp.stack(line_rows), jnp.stack(anchor_rows))


def expert_rank(routes):
    steps_count, beam_count, pick_count = routes.shape
    onehot = (routes[..., None] == jnp.arange(EXPERTS, dtype=jnp.int32)).astype(jnp.int32)
    flat_hits = onehot.reshape(steps_count, beam_count * pick_count, EXPERTS)
    before = jnp.cumsum(flat_hits, axis=1) - flat_hits
    return jnp.sum(before * flat_hits, axis=-1).reshape(steps_count, beam_count, pick_count)


def head_total(partial_value, kv_size):
    return butterfly(partial_value, "kv", kv_size, add_parts, KV_RADICES)


def combine_parts(part_one, part_two):
    max_one, sum_one, vector_one = part_one
    max_two, sum_two, vector_two = part_two
    larger = jnp.maximum(max_one, max_two)
    scale_one = jnp.exp(max_one - larger)
    scale_two = jnp.exp(max_two - larger)
    return (
        larger,
        sum_one * scale_one + sum_two * scale_two,
        vector_one * scale_one[..., None] + vector_two * scale_two[..., None],
    )


def groups_to_beams(grouped):
    shaped = grouped.reshape((GROUPS, DECODE_STEPS, BEAM_W, QUERIES_PER_KEY) + grouped.shape[2:])
    shaped = jnp.moveaxis(shaped, 1, 0)
    return shaped.reshape((DECODE_STEPS, BEAM_TOTAL, QUERIES_PER_KEY) + grouped.shape[2:])


def body(
    hidden_in,
    attn_gain,
    ffn_gain,
    query_key_value_weight,
    out_weight,
    router_weight,
    expert_in,
    expert_down,
    kv_cache,
    lengths,
    tables,
    parents,
    routes,
    kv_size,
    blk_size,
):
    count_tokens = DECODE_STEPS * BEAM_TOTAL
    width_local = hidden_in.shape[2]
    heads_local = query_key_value_weight.shape[1]
    logit_scale = 1.0 / math.sqrt(HEAD_WIDTH)
    line_beams, anchor = lineage(parents)
    flat_in = hidden_in.reshape(count_tokens, width_local).astype(jnp.float32)
    pre_attn = (flat_in * attn_gain.astype(jnp.float32)).astype(jnp.bfloat16)
    partial_proj = jnp.dot(
        pre_attn,
        query_key_value_weight.reshape(width_local, -1),
        preferred_element_type=jnp.float32,
    )
    partial_sq = jnp.sum(flat_in * flat_in, axis=1)
    packed_proj = butterfly(
        jnp.concatenate([partial_proj, partial_sq[:, None]], axis=1), "blk", blk_size, add_parts, BLK_RADICES
    )
    projected_rows = packed_proj[:, :-1]
    square_sum = packed_proj[:, -1]
    projected_rows = (
        projected_rows * lax.rsqrt(square_sum / MODEL_WIDTH + NORM_FLOOR)[:, None]
    ).reshape(DECODE_STEPS, BEAM_TOTAL, heads_local, QUERIES_PER_KEY + 2, HEAD_WIDTH)
    beam_groups = jnp.arange(BEAM_TOTAL, dtype=jnp.int32) // BEAM_W
    positions = lookup(lengths, beam_groups)[None, :] + jnp.arange(DECODE_STEPS, dtype=jnp.int32)[:, None]
    queries = rotate_pairs(
        projected_rows[:, :, :, :QUERIES_PER_KEY], positions[:, :, None, None]
    ).astype(jnp.bfloat16)
    new_key = rotate_pairs(projected_rows[:, :, :, QUERIES_PER_KEY], positions[:, :, None]).astype(
        jnp.bfloat16
    )
    new_value = projected_rows[:, :, :, QUERIES_PER_KEY + 1].astype(jnp.bfloat16)
    slot_count = kv_cache.shape[0]
    slot_base = lax.axis_index("blk") * slot_count
    entry_ids = jnp.arange(BEAM_TOTAL * BEAM_BLOCKS, dtype=jnp.int32)
    slot_ids = slot_base + jnp.arange(slot_count, dtype=jnp.int32)
    slot_hits = tables.reshape(-1)[None, :] == slot_ids[:, None]
    entry_here = jnp.sum(jnp.where(slot_hits, entry_ids[None, :], 0), axis=1)
    owner_here = entry_here // BEAM_BLOCKS
    block_here = entry_here % BEAM_BLOCKS
    group_here = owner_here // BEAM_W
    live_keys = (
        block_here[:, None] * BLOCK_POSITIONS
        + jnp.arange(BLOCK_POSITIONS, dtype=jnp.int32)[None, :]
        < lookup(lengths, group_here)[:, None]
    )
    anchor_groups = jnp.moveaxis(anchor.reshape(DECODE_STEPS, GROUPS, BEAM_W), 1, 0)
    anchor_query = jnp.broadcast_to(
        anchor_groups[..., None], (GROUPS, DECODE_STEPS, BEAM_W, QUERIES_PER_KEY)
    ).reshape(GROUPS, -1)
    query_match = lookup(anchor_query, group_here) == owner_here[:, None]
    group_hits = group_here[:, None] == jnp.arange(GROUPS, dtype=jnp.int32)[None, :]
    group_float = group_hits.astype(jnp.float32)
    recent_allowed = jnp.transpose(
        line_beams[:, :, :, None] == jnp.arange(BEAM_TOTAL, dtype=jnp.int32), (0, 2, 1, 3)
    ).reshape(DECODE_STEPS, BEAM_TOTAL, 1, count_tokens)
    is_first = lax.axis_index("blk") == 0
    query_head = queries[:, :, 0]
    query_groups = jnp.moveaxis(
        query_head.reshape(DECODE_STEPS, GROUPS, BEAM_W, QUERIES_PER_KEY, HEAD_WIDTH), 1, 0
    ).reshape(GROUPS, -1, HEAD_WIDTH)
    query_slots = jnp.where((group_here == 0)[:, None, None], query_groups[0], query_groups[1])
    key_matrix = kv_cache[:, 0, 0]
    value_matrix = kv_cache[:, 1, 0]
    scores = (
        jnp.einsum("ptd,pqd->ptq", key_matrix, query_slots, preferred_element_type=jnp.float32)
        * logit_scale
    )
    allowed = live_keys[:, :, None] & query_match[:, None, :]
    masked = jnp.where(allowed, scores, NEG_FILL)
    slot_max = jnp.max(masked, axis=1)
    weights = jnp.where(allowed, jnp.exp(masked - slot_max[:, None, :]), 0.0)
    slot_sum = jnp.sum(weights, axis=1)
    slot_vector = jnp.einsum(
        "ptq,ptd->pqd",
        weights.astype(jnp.bfloat16),
        value_matrix,
        preferred_element_type=jnp.float32,
    )
    group_max = jnp.max(jnp.where(group_hits[:, :, None], slot_max[:, None, :], NEG_FILL), axis=0)
    rescale = jnp.exp(slot_max - jnp.where((group_here == 0)[:, None], group_max[0], group_max[1]))
    group_sum = jnp.einsum(
        "pg,pq->gq", group_float, slot_sum * rescale, precision=lax.Precision.HIGHEST
    )
    group_vector = jnp.einsum(
        "pg,pqd->gqd",
        group_float,
        slot_vector * rescale[:, :, None],
        precision=lax.Precision.HIGHEST,
    )
    cache_max = groups_to_beams(group_max)
    cache_sum = groups_to_beams(group_sum)
    cache_vector = groups_to_beams(group_vector)
    newest_keys = new_key[:, :, 0].reshape(count_tokens, HEAD_WIDTH)
    newest_values = new_value[:, :, 0].reshape(count_tokens, HEAD_WIDTH)
    newest_logits = (
        jnp.einsum("sbqd,kd->sbqk", query_head, newest_keys, preferred_element_type=jnp.float32)
        * logit_scale
    )
    recent_masked = jnp.where(recent_allowed, newest_logits, NEG_FILL)
    recent_max = jnp.max(recent_masked, axis=-1)
    recent_weights = jnp.where(recent_allowed, jnp.exp(recent_masked - recent_max[..., None]), 0.0)
    recent_sum = jnp.sum(recent_weights, axis=-1)
    recent_vector = jnp.einsum(
        "sbqk,kd->sbqd",
        recent_weights.astype(jnp.bfloat16),
        newest_values,
        preferred_element_type=jnp.float32,
    )
    recent_max = jnp.where(is_first, recent_max, NEG_FILL)
    recent_sum = jnp.where(is_first, recent_sum, 0.0)
    recent_vector = jnp.where(is_first, recent_vector, 0.0)
    local_max, local_sum, local_vector = combine_parts(
        (cache_max, cache_sum, cache_vector), (recent_max, recent_sum, recent_vector)
    )
    max_heads = [local_max]
    sum_heads = [local_sum]
    vector_heads = [local_vector]
    part_max = jnp.stack(max_heads, axis=2)
    part_sum = jnp.stack(sum_heads, axis=2)
    part_vector = jnp.stack(vector_heads, axis=2)
    part_shape = part_max.shape
    vector_rows = part_vector.reshape(-1, HEAD_WIDTH)
    stat_rows = jnp.stack([part_max.reshape(-1), part_sum.reshape(-1)]).reshape(-1, HEAD_WIDTH)

    def packed_combine(first, second):
        def unpack(packed):
            stats = packed[vector_rows.shape[0] :].reshape(2, -1)
            return stats[0], stats[1], packed[: vector_rows.shape[0]]

        larger, total, vector = combine_parts(unpack(first), unpack(second))
        stats = jnp.stack([larger, total]).reshape(-1, HEAD_WIDTH)
        return jnp.concatenate([vector, stats], axis=0)

    whole_packed = butterfly(
        jnp.concatenate([vector_rows, stat_rows], axis=0), "blk", blk_size, packed_combine, BLK_RADICES
    )
    whole_vector = whole_packed[: vector_rows.shape[0]].reshape(part_vector.shape)
    whole_sum = whole_packed[vector_rows.shape[0] :].reshape(2, -1)[1].reshape(part_shape)
    attended_rows = (
        (whole_vector / whole_sum[..., None]).astype(jnp.bfloat16).reshape(count_tokens, -1)
    )
    attn_partial = jnp.dot(attended_rows, out_weight, preferred_element_type=jnp.float32)
    attn_out = head_total(attn_partial, kv_size)
    residual = (flat_in + attn_out).astype(jnp.bfloat16)
    experts_local = expert_in.shape[0]
    ff_local = expert_in.shape[3]
    rows_per_expert = DECODE_STEPS * CAP
    rows_local = experts_local * rows_per_expert
    flat_routes = routes.reshape(count_tokens, 2)
    rank = expert_rank(routes).reshape(count_tokens, 2)
    step_of = jnp.arange(count_tokens, dtype=jnp.int32) // BEAM_TOTAL
    row_id = (flat_routes * rows_per_expert + step_of[:, None] * CAP + rank).reshape(-1)
    token_ids = jnp.broadcast_to(
        jnp.arange(count_tokens, dtype=jnp.int32)[:, None], (count_tokens, 2)
    ).reshape(-1)
    table_size = EXPERTS * rows_per_expert
    row_token_all = jnp.zeros((table_size,), jnp.int32).at[row_id].set(token_ids)
    row_live_all = jnp.zeros((table_size,), jnp.float32).at[row_id].set(1.0)
    row_other_all = (
        jnp.zeros((table_size,), jnp.int32).at[row_id].set(flat_routes[:, ::-1].reshape(-1))
    )
    row_start = lax.axis_index("kv") * rows_local
    row_token = lax.dynamic_slice_in_dim(row_token_all, row_start, rows_local)
    row_live = lax.dynamic_slice_in_dim(row_live_all, row_start, rows_local)
    row_other = lax.dynamic_slice_in_dim(row_other_all, row_start, rows_local)
    row_own = (row_start + jnp.arange(rows_local, dtype=jnp.int32)) // rows_per_expert
    in_flat = expert_in.reshape(experts_local, MODEL_WIDTH, 2 * ff_local)
    gain_wide = ffn_gain.astype(jnp.float32)
    full_rows = jnp.moveaxis(
        lax.all_to_all(
            jnp.broadcast_to(residual[None], (blk_size,) + residual.shape), "blk", 0, 0, tiled=True
        ),
        0,
        1,
    ).reshape(residual.shape[0], -1)
    chosen = full_rows[row_token].astype(jnp.float32)
    pre_rows = (chosen * gain_wide).astype(jnp.bfloat16)
    sums_in = jnp.einsum(
        "erd,edf->erf",
        pre_rows.reshape(experts_local, rows_per_expert, MODEL_WIDTH),
        in_flat,
        preferred_element_type=jnp.float32,
    )
    sums_router = jnp.dot(pre_rows, router_weight, preferred_element_type=jnp.float32)
    sum_sq = jnp.sum(chosen * chosen, axis=1)
    inv_rows = lax.rsqrt(sum_sq / MODEL_WIDTH + NORM_FLOOR)
    expert_act = sums_in * inv_rows.reshape(experts_local, rows_per_expert)[:, :, None]
    expert_hidden = (jax.nn.silu(expert_act[..., :ff_local]) * expert_act[..., ff_local:]).astype(
        jnp.bfloat16
    )
    down_part = jnp.einsum(
        "erf,efd->erd", expert_hidden, expert_down, preferred_element_type=jnp.float32
    ).reshape(rows_local, MODEL_WIDTH)
    expert_pieces = jnp.moveaxis(down_part.reshape(rows_local, blk_size, -1), 1, 0)
    expert_result = jnp.sum(lax.all_to_all(expert_pieces, "blk", 0, 0, tiled=True), axis=0)
    logits = sums_router * inv_rows[:, None]
    expert_ids = jnp.arange(EXPERTS, dtype=jnp.int32)
    own_logit = jnp.sum(jnp.where(row_own[:, None] == expert_ids[None, :], logits, 0.0), axis=1)
    other_logit = jnp.sum(jnp.where(row_other[:, None] == expert_ids[None, :], logits, 0.0), axis=1)
    gate_share = row_live / (1.0 + jnp.exp(other_logit - own_logit))
    weighted_values = expert_result * gate_share[:, None]
    placement = (row_token[None, :] == jnp.arange(count_tokens, dtype=jnp.int32)[:, None]).astype(
        jnp.float32
    )
    mixture_part = jnp.dot(placement, weighted_values, precision=lax.Precision.HIGHEST)
    mixture = head_total(mixture_part, kv_size)
    layer_out = (residual.astype(jnp.float32) + mixture).astype(jnp.bfloat16)
    return layer_out.reshape(DECODE_STEPS, BEAM_TOTAL, width_local)


def solution(mesh):
    placed = (
        P(None, None, "blk"),
        P("blk"),
        P(),
        P("blk", "kv", None),
        P("kv", "blk"),
        P(),
        P("kv", None, None, "blk"),
        P("kv", "blk", None),
        P("blk", None, "kv", None, None),
        P(),
        P(),
        P(),
        P(),
    )
    kv_size = mesh.shape["kv"]
    blk_size = mesh.shape["blk"]

    def sized(*arrays):
        return body(*arrays, kv_size, blk_size)

    return jax.shard_map(
        sized, mesh=mesh, in_specs=placed, out_specs=P(None, None, "blk"), check_vma=False
    )
```

```python
import functools
import math

import jax
import jax.numpy as jnp
from jax import lax
from jax.experimental import pallas as pl
from jax.experimental.pallas import tpu as pltpu
from jax.sharding import PartitionSpec as P

MODEL_WIDTH = 4096
HEAD_WIDTH = 128
QUERIES_PER_KEY = 4
EXPERTS = 8
BEAM_W = 8
GROUPS = 2
DECODE_STEPS = 4
BLOCK_POSITIONS = 128
BEAM_BLOCKS = 128
BEAM_TOTAL = 16
CAP = 6


NORM_FLOOR = 1e-05
ROPE_BASE = 1000000.0
NEG_FILL = -1e30
BLK_RADICES = (2, 4, 4)
SCATTER_RADICES = (4, 4, 2)
KV_RADICES = (2, 2, 2)


def exchange(value, axis, size, distance):
    pairs = [(index, index ^ distance) for index in range(size)]
    return jax.tree.map(lambda part: lax.ppermute(part, axis, pairs), value)


def tree_join(parts, join):
    stride = 1
    while stride < len(parts):
        parts = [
            join(parts[place], parts[place + stride]) if place % (2 * stride) == 0 else parts[place]
            for place in range(len(parts))
        ]
        stride *= 2
    return parts[0]


def butterfly(value, axis, size, join, radices):
    distance = 1
    for radix in radices:
        parts = [value] + [
            exchange(value, axis, size, distance * offset) for offset in range(1, radix)
        ]
        value = tree_join(parts, join)
        distance *= radix
    assert distance == size
    return value


def add_parts(first, second):
    return jax.tree.map(lambda one, two: one + two, first, second)


def gather_doubling(block, axis, size, dim, radices):
    index = lax.axis_index(axis)
    distance = 1
    for radix in radices:
        place = (index // distance) % radix
        parts = [block] + [
            exchange(block, axis, size, distance * offset) for offset in range(1, radix)
        ]
        stacked = jnp.stack(parts)
        ordered = jnp.take(stacked, jnp.arange(radix, dtype=jnp.int32) ^ place, axis=0)
        block = jnp.concatenate([ordered[slot] for slot in range(radix)], dim)
        distance *= radix
    assert distance == size
    return block


def scatter_halving(value, axis, size, dim, radices):
    index = lax.axis_index(axis)
    distance = size
    for radix in radices:
        distance //= radix
        place = (index // distance) % radix
        piece = value.shape[dim] // radix
        received = [lax.dynamic_slice_in_dim(value, place * piece, piece, dim)]
        for offset in range(1, radix):
            send = lax.dynamic_slice_in_dim(value, (place ^ offset) * piece, piece, dim)
            received.append(exchange(send, axis, size, distance * offset))
        value = tree_join(received, add_parts)
    assert distance == 1
    return value


def rotate_pairs(vectors, positions):
    half_width = vectors.shape[-1] // 2
    exponents = jnp.arange(half_width, dtype=jnp.float32) * (2.0 / vectors.shape[-1])
    frequency = ROPE_BASE ** (-exponents)
    angles = positions.astype(jnp.float32)[..., None] * frequency
    cosine = jnp.cos(angles)
    sine_part = jnp.sin(angles)
    lower_half = vectors[..., :half_width]
    upper_half = vectors[..., half_width:]
    return jnp.concatenate(
        [
            lower_half * cosine - upper_half * sine_part,
            upper_half * cosine + lower_half * sine_part,
        ],
        axis=-1,
    )


def slot_attention_kernel(group_ref, live_ref, owner_ref, used_ref, kv_ref, query_ref, anchor_ref,
                          vector_ref, max_ref, sum_ref, *, scale):
    vector_ref[...] = jnp.zeros(vector_ref.shape, jnp.float32)
    max_ref[...] = jnp.full(max_ref.shape, NEG_FILL, jnp.float32)
    sum_ref[...] = jnp.zeros(sum_ref.shape, jnp.float32)

    def visit(slot, carry):
        @pl.when(used_ref[slot] > 0)
        def _():
            group = group_ref[slot]
            keys = kv_ref[slot, 0]
            values = kv_ref[slot, 1]
            queries = query_ref[group]
            scores = lax.dot_general(
                queries, keys, (((1,), (1,)), ((), ())), preferred_element_type=jnp.float32
            ) * scale
            position = lax.broadcasted_iota(jnp.int32, scores.shape, 1)
            allowed = (position < live_ref[slot]) & (anchor_ref[group] == owner_ref[slot])
            masked = jnp.where(allowed, scores, NEG_FILL)
            old_max = max_ref[group]
            new_max = jnp.maximum(old_max, jnp.max(masked, axis=1, keepdims=True))
            weights = jnp.where(allowed, jnp.exp(masked - new_max), 0.0)
            keep = jnp.exp(old_max - new_max)
            sum_ref[group] = keep * sum_ref[group] + jnp.sum(weights, axis=1, keepdims=True)
            vector_ref[group] = keep * vector_ref[group] + jnp.dot(
                weights.astype(jnp.bfloat16), values, preferred_element_type=jnp.float32
            )
            max_ref[group] = new_max
        return carry

    lax.fori_loop(0, kv_ref.shape[0], visit, 0)


def slot_attention(group_here, live_here, owner_here, used_here, kv_pairs, query_groups, anchor_lanes, scale):
    groups, rows, width = query_groups.shape
    smem = pl.BlockSpec(memory_space=pltpu.SMEM)
    vmem = pl.BlockSpec(memory_space=pltpu.VMEM)
    shape = jax.ShapeDtypeStruct((groups, rows, width), jnp.float32)
    return pl.pallas_call(
        functools.partial(slot_attention_kernel, scale=scale),
        in_specs=[smem, smem, smem, smem, vmem, vmem, vmem],
        out_specs=[vmem, vmem, vmem],
        out_shape=[shape, shape, shape],
    )(group_here, live_here, owner_here, used_here, kv_pairs, query_groups, anchor_lanes)


def lookup(table, index):
    hits = index[..., None] == jnp.arange(table.shape[0], dtype=jnp.int32)
    shaped = hits.reshape(hits.shape + (1,) * (table.ndim - 1))
    return jnp.sum(jnp.where(shaped, table, jnp.zeros((), table.dtype)), axis=index.ndim)


def lineage(parents):
    steps_count, beam_count = parents.shape
    beam_ids = jnp.arange(beam_count, dtype=jnp.int32)
    line_rows = []
    anchor_rows = []
    for step_index in range(steps_count):
        current = beam_ids
        levels = [jnp.full((beam_count,), -1, jnp.int32) for level_index in range(steps_count)]
        for level_index in range(step_index, -1, -1):
            levels[level_index] = current
            current = lookup(parents[level_index], current)
        line_rows.append(jnp.stack(levels))
        anchor_rows.append(current)
    return (jnp.stack(line_rows), jnp.stack(anchor_rows))


def expert_rank(routes):
    steps_count, beam_count, pick_count = routes.shape
    onehot = (routes[..., None] == jnp.arange(EXPERTS, dtype=jnp.int32)).astype(jnp.int32)
    flat_hits = onehot.reshape(steps_count, beam_count * pick_count, EXPERTS)
    before = jnp.cumsum(flat_hits, axis=1) - flat_hits
    return jnp.sum(before * flat_hits, axis=-1).reshape(steps_count, beam_count, pick_count)


def head_total(partial_value, kv_size):
    return butterfly(partial_value, "kv", kv_size, add_parts, KV_RADICES)


def combine_parts(part_one, part_two):
    max_one, sum_one, vector_one = part_one
    max_two, sum_two, vector_two = part_two
    larger = jnp.maximum(max_one, max_two)
    scale_one = jnp.exp(max_one - larger)
    scale_two = jnp.exp(max_two - larger)
    return (
        larger,
        sum_one * scale_one + sum_two * scale_two,
        vector_one * scale_one[..., None] + vector_two * scale_two[..., None],
    )


def groups_to_beams(grouped):
    shaped = grouped.reshape((GROUPS, DECODE_STEPS, BEAM_W, QUERIES_PER_KEY) + grouped.shape[2:])
    shaped = jnp.moveaxis(shaped, 1, 0)
    return shaped.reshape((DECODE_STEPS, BEAM_TOTAL, QUERIES_PER_KEY) + grouped.shape[2:])


def body(
    hidden_in,
    attn_gain,
    ffn_gain,
    query_key_value_weight,
    out_weight,
    router_weight,
    expert_in,
    expert_down,
    kv_cache,
    lengths,
    tables,
    parents,
    routes,
    kv_size,
    blk_size,
):
    count_tokens = DECODE_STEPS * BEAM_TOTAL
    width_local = hidden_in.shape[2]
    heads_local = query_key_value_weight.shape[1]
    logit_scale = 1.0 / math.sqrt(HEAD_WIDTH)
    line_beams, anchor = lineage(parents)
    flat_in = hidden_in.reshape(count_tokens, width_local).astype(jnp.float32)
    pre_attn = (flat_in * attn_gain.astype(jnp.float32)).astype(jnp.bfloat16)
    partial_proj = jnp.dot(
        pre_attn,
        query_key_value_weight.reshape(width_local, -1),
        preferred_element_type=jnp.float32,
    )
    partial_sq = jnp.sum(flat_in * flat_in, axis=1)
    packed_proj = butterfly(
        jnp.concatenate([partial_proj, partial_sq[:, None]], axis=1), "blk", blk_size, add_parts, BLK_RADICES
    )
    projected_rows = packed_proj[:, :-1]
    square_sum = packed_proj[:, -1]
    projected_rows = (
        projected_rows * lax.rsqrt(square_sum / MODEL_WIDTH + NORM_FLOOR)[:, None]
    ).reshape(DECODE_STEPS, BEAM_TOTAL, heads_local, QUERIES_PER_KEY + 2, HEAD_WIDTH)
    beam_groups = jnp.arange(BEAM_TOTAL, dtype=jnp.int32) // BEAM_W
    positions = lookup(lengths, beam_groups)[None, :] + jnp.arange(DECODE_STEPS, dtype=jnp.int32)[:, None]
    queries = rotate_pairs(
        projected_rows[:, :, :, :QUERIES_PER_KEY], positions[:, :, None, None]
    ).astype(jnp.bfloat16)
    new_key = rotate_pairs(projected_rows[:, :, :, QUERIES_PER_KEY], positions[:, :, None]).astype(
        jnp.bfloat16
    )
    new_value = projected_rows[:, :, :, QUERIES_PER_KEY + 1].astype(jnp.bfloat16)
    slot_count = kv_cache.shape[0]
    slot_base = lax.axis_index("blk") * slot_count
    entry_ids = jnp.arange(BEAM_TOTAL * BEAM_BLOCKS, dtype=jnp.int32)
    slot_ids = slot_base + jnp.arange(slot_count, dtype=jnp.int32)
    slot_hits = tables.reshape(-1)[None, :] == slot_ids[:, None]
    entry_here = jnp.sum(jnp.where(slot_hits, entry_ids[None, :], 0), axis=1)
    owner_here = entry_here // BEAM_BLOCKS
    block_here = entry_here % BEAM_BLOCKS
    group_here = owner_here // BEAM_W
    anchor_groups = jnp.moveaxis(anchor.reshape(DECODE_STEPS, GROUPS, BEAM_W), 1, 0)
    anchor_query = jnp.broadcast_to(
        anchor_groups[..., None], (GROUPS, DECODE_STEPS, BEAM_W, QUERIES_PER_KEY)
    ).reshape(GROUPS, -1)
    recent_allowed = jnp.transpose(
        line_beams[:, :, :, None] == jnp.arange(BEAM_TOTAL, dtype=jnp.int32), (0, 2, 1, 3)
    ).reshape(DECODE_STEPS, BEAM_TOTAL, 1, count_tokens)
    is_first = lax.axis_index("blk") == 0
    query_head = queries[:, :, 0]
    query_groups = jnp.moveaxis(
        query_head.reshape(DECODE_STEPS, GROUPS, BEAM_W, QUERIES_PER_KEY, HEAD_WIDTH), 1, 0
    ).reshape(GROUPS, -1, HEAD_WIDTH)
    live_here = lookup(lengths, group_here) - block_here * BLOCK_POSITIONS
    query_match = lookup(anchor_query, group_here) == owner_here[:, None]
    used_here = (jnp.any(query_match, axis=1) & (live_here > 0)).astype(jnp.int32)
    anchor_lanes = jnp.broadcast_to(anchor_query[:, :, None], anchor_query.shape + (HEAD_WIDTH,))
    kv_pairs = kv_cache.reshape(slot_count, 2, BLOCK_POSITIONS, HEAD_WIDTH)
    vector_lanes, max_lanes, sum_lanes = slot_attention(
        group_here, live_here, owner_here, used_here, kv_pairs, query_groups, anchor_lanes, logit_scale
    )
    group_max = max_lanes[:, :, 0]
    group_sum = sum_lanes[:, :, 0]
    group_vector = vector_lanes
    cache_max = groups_to_beams(group_max)
    cache_sum = groups_to_beams(group_sum)
    cache_vector = groups_to_beams(group_vector)
    newest_keys = new_key[:, :, 0].reshape(count_tokens, HEAD_WIDTH)
    newest_values = new_value[:, :, 0].reshape(count_tokens, HEAD_WIDTH)
    newest_logits = (
        jnp.einsum("sbqd,kd->sbqk", query_head, newest_keys, preferred_element_type=jnp.float32)
        * logit_scale
    )
    recent_masked = jnp.where(recent_allowed, newest_logits, NEG_FILL)
    recent_max = jnp.max(recent_masked, axis=-1)
    recent_weights = jnp.where(recent_allowed, jnp.exp(recent_masked - recent_max[..., None]), 0.0)
    recent_sum = jnp.sum(recent_weights, axis=-1)
    recent_vector = jnp.einsum(
        "sbqk,kd->sbqd",
        recent_weights.astype(jnp.bfloat16),
        newest_values,
        preferred_element_type=jnp.float32,
    )
    recent_max = jnp.where(is_first, recent_max, NEG_FILL)
    recent_sum = jnp.where(is_first, recent_sum, 0.0)
    recent_vector = jnp.where(is_first, recent_vector, 0.0)
    local_max, local_sum, local_vector = combine_parts(
        (cache_max, cache_sum, cache_vector), (recent_max, recent_sum, recent_vector)
    )
    max_heads = [local_max]
    sum_heads = [local_sum]
    vector_heads = [local_vector]
    part_max = jnp.stack(max_heads, axis=2)
    part_sum = jnp.stack(sum_heads, axis=2)
    part_vector = jnp.stack(vector_heads, axis=2)
    part_shape = part_max.shape
    vector_rows = part_vector.reshape(-1, HEAD_WIDTH)
    stat_rows = jnp.stack([part_max.reshape(-1), part_sum.reshape(-1)]).reshape(-1, HEAD_WIDTH)

    def packed_combine(first, second):
        def unpack(packed):
            stats = packed[vector_rows.shape[0] :].reshape(2, -1)
            return stats[0], stats[1], packed[: vector_rows.shape[0]]

        larger, total, vector = combine_parts(unpack(first), unpack(second))
        stats = jnp.stack([larger, total]).reshape(-1, HEAD_WIDTH)
        return jnp.concatenate([vector, stats], axis=0)

    whole_packed = butterfly(
        jnp.concatenate([vector_rows, stat_rows], axis=0), "blk", blk_size, packed_combine, BLK_RADICES
    )
    whole_vector = whole_packed[: vector_rows.shape[0]].reshape(part_vector.shape)
    whole_sum = whole_packed[vector_rows.shape[0] :].reshape(2, -1)[1].reshape(part_shape)
    attended_rows = (
        (whole_vector / whole_sum[..., None]).astype(jnp.bfloat16).reshape(count_tokens, -1)
    )
    attn_partial = jnp.dot(attended_rows, out_weight, preferred_element_type=jnp.float32)
    attn_out = head_total(attn_partial, kv_size)
    residual = (flat_in + attn_out).astype(jnp.bfloat16)
    experts_local = expert_in.shape[0]
    ff_local = expert_in.shape[3]
    rows_per_expert = DECODE_STEPS * CAP
    rows_local = experts_local * rows_per_expert
    flat_routes = routes.reshape(count_tokens, 2)
    rank = expert_rank(routes).reshape(count_tokens, 2)
    step_of = jnp.arange(count_tokens, dtype=jnp.int32) // BEAM_TOTAL
    row_id = (flat_routes * rows_per_expert + step_of[:, None] * CAP + rank).reshape(-1)
    token_ids = jnp.broadcast_to(
        jnp.arange(count_tokens, dtype=jnp.int32)[:, None], (count_tokens, 2)
    ).reshape(-1)
    table_size = EXPERTS * rows_per_expert
    row_token_all = jnp.zeros((table_size,), jnp.int32).at[row_id].set(token_ids)
    row_live_all = jnp.zeros((table_size,), jnp.float32).at[row_id].set(1.0)
    row_other_all = (
        jnp.zeros((table_size,), jnp.int32).at[row_id].set(flat_routes[:, ::-1].reshape(-1))
    )
    row_start = lax.axis_index("kv") * rows_local
    row_token = lax.dynamic_slice_in_dim(row_token_all, row_start, rows_local)
    row_live = lax.dynamic_slice_in_dim(row_live_all, row_start, rows_local)
    row_other = lax.dynamic_slice_in_dim(row_other_all, row_start, rows_local)
    row_own = (row_start + jnp.arange(rows_local, dtype=jnp.int32)) // rows_per_expert
    in_flat = expert_in.reshape(experts_local, MODEL_WIDTH, 2 * ff_local)
    gain_wide = ffn_gain.astype(jnp.float32)
    full_rows = jnp.moveaxis(
        lax.all_to_all(
            jnp.broadcast_to(residual[None], (blk_size,) + residual.shape), "blk", 0, 0, tiled=True
        ),
        0,
        1,
    ).reshape(residual.shape[0], -1)
    chosen = full_rows[row_token].astype(jnp.float32)
    pre_rows = (chosen * gain_wide).astype(jnp.bfloat16)
    sums_in = jnp.einsum(
        "erd,edf->erf",
        pre_rows.reshape(experts_local, rows_per_expert, MODEL_WIDTH),
        in_flat,
        preferred_element_type=jnp.float32,
    )
    sums_router = jnp.dot(pre_rows, router_weight, preferred_element_type=jnp.float32)
    sum_sq = jnp.sum(chosen * chosen, axis=1)
    inv_rows = lax.rsqrt(sum_sq / MODEL_WIDTH + NORM_FLOOR)
    expert_act = sums_in * inv_rows.reshape(experts_local, rows_per_expert)[:, :, None]
    expert_hidden = (jax.nn.silu(expert_act[..., :ff_local]) * expert_act[..., ff_local:]).astype(
        jnp.bfloat16
    )
    down_part = jnp.einsum(
        "erf,efd->erd", expert_hidden, expert_down, preferred_element_type=jnp.float32
    ).reshape(rows_local, MODEL_WIDTH)
    expert_pieces = jnp.moveaxis(down_part.reshape(rows_local, blk_size, -1), 1, 0)
    expert_result = jnp.sum(lax.all_to_all(expert_pieces, "blk", 0, 0, tiled=True), axis=0)
    logits = sums_router * inv_rows[:, None]
    expert_ids = jnp.arange(EXPERTS, dtype=jnp.int32)
    own_logit = jnp.sum(jnp.where(row_own[:, None] == expert_ids[None, :], logits, 0.0), axis=1)
    other_logit = jnp.sum(jnp.where(row_other[:, None] == expert_ids[None, :], logits, 0.0), axis=1)
    gate_share = row_live / (1.0 + jnp.exp(other_logit - own_logit))
    weighted_values = expert_result * gate_share[:, None]
    placement = (row_token[None, :] == jnp.arange(count_tokens, dtype=jnp.int32)[:, None]).astype(
        jnp.float32
    )
    mixture_part = jnp.dot(placement, weighted_values, precision=lax.Precision.HIGHEST)
    mixture = head_total(mixture_part, kv_size)
    layer_out = (residual.astype(jnp.float32) + mixture).astype(jnp.bfloat16)
    return layer_out.reshape(DECODE_STEPS, BEAM_TOTAL, width_local)


def solution(mesh):
    placed = (
        P(None, None, "blk"),
        P("blk"),
        P(),
        P("blk", "kv", None),
        P("kv", "blk"),
        P(),
        P("kv", None, None, "blk"),
        P("kv", "blk", None),
        P("blk", None, "kv", None, None),
        P(),
        P(),
        P(),
        P(),
    )
    kv_size = mesh.shape["kv"]
    blk_size = mesh.shape["blk"]

    def sized(*arrays):
        return body(*arrays, kv_size, blk_size)

    return jax.shard_map(
        sized, mesh=mesh, in_specs=placed, out_specs=P(None, None, "blk"), check_vma=False
    )
```

```python
import functools
import math

import jax
import jax.numpy as jnp
from jax import lax
from jax.experimental import pallas as pl
from jax.experimental.pallas import tpu as pltpu
from jax.sharding import PartitionSpec as P

MODEL_WIDTH = 4096
HEAD_WIDTH = 128
QUERIES_PER_KEY = 4
EXPERTS = 8
BEAM_W = 8
GROUPS = 2
DECODE_STEPS = 4
BLOCK_POSITIONS = 128
BEAM_BLOCKS = 128
BEAM_TOTAL = 16
CAP = 6


NORM_FLOOR = 1e-05
ROPE_BASE = 1000000.0
NEG_FILL = -1e30
BLK_RADICES = (2, 4, 4)
SCATTER_RADICES = (4, 4, 2)
KV_RADICES = (2, 2, 2)


def exchange(value, axis, size, distance):
    pairs = [(index, index ^ distance) for index in range(size)]
    return jax.tree.map(lambda part: lax.ppermute(part, axis, pairs), value)


def tree_join(parts, join):
    stride = 1
    while stride < len(parts):
        parts = [
            join(parts[place], parts[place + stride]) if place % (2 * stride) == 0 else parts[place]
            for place in range(len(parts))
        ]
        stride *= 2
    return parts[0]


def butterfly(value, axis, size, join, radices):
    distance = 1
    for radix in radices:
        parts = [value] + [
            exchange(value, axis, size, distance * offset) for offset in range(1, radix)
        ]
        value = tree_join(parts, join)
        distance *= radix
    assert distance == size
    return value


def add_parts(first, second):
    return jax.tree.map(lambda one, two: one + two, first, second)


def gather_doubling(block, axis, size, dim, radices):
    index = lax.axis_index(axis)
    distance = 1
    for radix in radices:
        place = (index // distance) % radix
        parts = [block] + [
            exchange(block, axis, size, distance * offset) for offset in range(1, radix)
        ]
        stacked = jnp.stack(parts)
        ordered = jnp.take(stacked, jnp.arange(radix, dtype=jnp.int32) ^ place, axis=0)
        block = jnp.concatenate([ordered[slot] for slot in range(radix)], dim)
        distance *= radix
    assert distance == size
    return block


def scatter_halving(value, axis, size, dim, radices):
    index = lax.axis_index(axis)
    distance = size
    for radix in radices:
        distance //= radix
        place = (index // distance) % radix
        piece = value.shape[dim] // radix
        received = [lax.dynamic_slice_in_dim(value, place * piece, piece, dim)]
        for offset in range(1, radix):
            send = lax.dynamic_slice_in_dim(value, (place ^ offset) * piece, piece, dim)
            received.append(exchange(send, axis, size, distance * offset))
        value = tree_join(received, add_parts)
    assert distance == 1
    return value


def rotate_pairs(vectors, positions):
    half_width = vectors.shape[-1] // 2
    exponents = jnp.arange(half_width, dtype=jnp.float32) * (2.0 / vectors.shape[-1])
    frequency = ROPE_BASE ** (-exponents)
    angles = positions.astype(jnp.float32)[..., None] * frequency
    cosine = jnp.cos(angles)
    sine_part = jnp.sin(angles)
    lower_half = vectors[..., :half_width]
    upper_half = vectors[..., half_width:]
    return jnp.concatenate(
        [
            lower_half * cosine - upper_half * sine_part,
            upper_half * cosine + lower_half * sine_part,
        ],
        axis=-1,
    )


def slot_attention_kernel(group_ref, live_ref, owner_ref, used_ref, kv_ref, query_ref, anchor_ref,
                          vector_ref, max_ref, sum_ref, *, scale):
    vector_ref[...] = jnp.zeros(vector_ref.shape, jnp.float32)
    max_ref[...] = jnp.full(max_ref.shape, NEG_FILL, jnp.float32)
    sum_ref[...] = jnp.zeros(sum_ref.shape, jnp.float32)

    def visit(slot, carry):
        @pl.when(used_ref[slot] > 0)
        def _():
            group = group_ref[slot]
            keys = kv_ref[slot, 0]
            values = kv_ref[slot, 1]
            queries = query_ref[group]
            scores = lax.dot_general(
                queries, keys, (((1,), (1,)), ((), ())), preferred_element_type=jnp.float32
            ) * scale
            position = lax.broadcasted_iota(jnp.int32, scores.shape, 1)
            allowed = (position < live_ref[slot]) & (anchor_ref[group] == owner_ref[slot])
            masked = jnp.where(allowed, scores, NEG_FILL)
            old_max = max_ref[group]
            new_max = jnp.maximum(old_max, jnp.max(masked, axis=1, keepdims=True))
            weights = jnp.where(allowed, jnp.exp(masked - new_max), 0.0)
            keep = jnp.exp(old_max - new_max)
            sum_ref[group] = keep * sum_ref[group] + jnp.sum(weights, axis=1, keepdims=True)
            vector_ref[group] = keep * vector_ref[group] + jnp.dot(
                weights.astype(jnp.bfloat16), values, preferred_element_type=jnp.float32
            )
            max_ref[group] = new_max
        return carry

    lax.fori_loop(0, kv_ref.shape[0], visit, 0)


def slot_attention(group_here, live_here, owner_here, used_here, kv_pairs, query_groups, anchor_lanes, scale):
    groups, rows, width = query_groups.shape
    smem = pl.BlockSpec(memory_space=pltpu.SMEM)
    vmem = pl.BlockSpec(memory_space=pltpu.VMEM)
    shape = jax.ShapeDtypeStruct((groups, rows, width), jnp.float32)
    return pl.pallas_call(
        functools.partial(slot_attention_kernel, scale=scale),
        in_specs=[smem, smem, smem, smem, vmem, vmem, vmem],
        out_specs=[vmem, vmem, vmem],
        out_shape=[shape, shape, shape],
    )(group_here, live_here, owner_here, used_here, kv_pairs, query_groups, anchor_lanes)


def lookup(table, index):
    hits = index[..., None] == jnp.arange(table.shape[0], dtype=jnp.int32)
    shaped = hits.reshape(hits.shape + (1,) * (table.ndim - 1))
    return jnp.sum(jnp.where(shaped, table, jnp.zeros((), table.dtype)), axis=index.ndim)


def lineage(parents):
    steps_count, beam_count = parents.shape
    beam_ids = jnp.arange(beam_count, dtype=jnp.int32)
    line_rows = []
    anchor_rows = []
    for step_index in range(steps_count):
        current = beam_ids
        levels = [jnp.full((beam_count,), -1, jnp.int32) for level_index in range(steps_count)]
        for level_index in range(step_index, -1, -1):
            levels[level_index] = current
            current = lookup(parents[level_index], current)
        line_rows.append(jnp.stack(levels))
        anchor_rows.append(current)
    return (jnp.stack(line_rows), jnp.stack(anchor_rows))


def expert_rank(routes):
    steps_count, beam_count, pick_count = routes.shape
    onehot = (routes[..., None] == jnp.arange(EXPERTS, dtype=jnp.int32)).astype(jnp.int32)
    flat_hits = onehot.reshape(steps_count, beam_count * pick_count, EXPERTS)
    before = jnp.cumsum(flat_hits, axis=1) - flat_hits
    return jnp.sum(before * flat_hits, axis=-1).reshape(steps_count, beam_count, pick_count)


def head_total(partial_value, kv_size):
    return butterfly(partial_value, "kv", kv_size, add_parts, KV_RADICES)


def combine_parts(part_one, part_two):
    max_one, sum_one, vector_one = part_one
    max_two, sum_two, vector_two = part_two
    larger = jnp.maximum(max_one, max_two)
    scale_one = jnp.exp(max_one - larger)
    scale_two = jnp.exp(max_two - larger)
    return (
        larger,
        sum_one * scale_one + sum_two * scale_two,
        vector_one * scale_one[..., None] + vector_two * scale_two[..., None],
    )


def groups_to_beams(grouped):
    shaped = grouped.reshape((GROUPS, DECODE_STEPS, BEAM_W, QUERIES_PER_KEY) + grouped.shape[2:])
    shaped = jnp.moveaxis(shaped, 1, 0)
    return shaped.reshape((DECODE_STEPS, BEAM_TOTAL, QUERIES_PER_KEY) + grouped.shape[2:])


def body(
    hidden_in,
    attn_gain,
    ffn_gain,
    query_key_value_weight,
    out_weight,
    router_weight,
    expert_in,
    expert_down,
    kv_cache,
    lengths,
    tables,
    parents,
    routes,
    kv_size,
    blk_size,
):
    count_tokens = DECODE_STEPS * BEAM_TOTAL
    width_local = hidden_in.shape[2]
    heads_local = query_key_value_weight.shape[1]
    logit_scale = 1.0 / math.sqrt(HEAD_WIDTH)
    line_beams, anchor = lineage(parents)
    flat_in = hidden_in.reshape(count_tokens, width_local).astype(jnp.float32)
    pre_attn = (flat_in * attn_gain.astype(jnp.float32)).astype(jnp.bfloat16)
    partial_proj = jnp.dot(
        pre_attn,
        query_key_value_weight.reshape(width_local, -1),
        preferred_element_type=jnp.float32,
    )
    partial_sq = jnp.sum(flat_in * flat_in, axis=1)
    proj_rows = partial_proj.reshape(-1, HEAD_WIDTH)
    sq_rows = jnp.pad(partial_sq, (0, -partial_sq.shape[0] % HEAD_WIDTH)).reshape(-1, HEAD_WIDTH)
    stacked = jnp.concatenate([proj_rows, sq_rows], axis=0)
    chunk_rows = -(-stacked.shape[0] // (8 * blk_size)) * 8
    stacked = jnp.pad(stacked, ((0, chunk_rows * blk_size - stacked.shape[0]), (0, 0)))
    owned = jnp.sum(
        lax.all_to_all(stacked.reshape(blk_size, chunk_rows, HEAD_WIDTH), "blk", 0, 0, tiled=True),
        axis=0,
    )
    summed = lax.all_to_all(
        jnp.broadcast_to(owned[None], (blk_size,) + owned.shape), "blk", 0, 0, tiled=True
    ).reshape(-1, HEAD_WIDTH)
    projected_rows = summed[: proj_rows.shape[0]].reshape(partial_proj.shape)
    square_sum = summed[proj_rows.shape[0] :].reshape(-1)[: partial_sq.shape[0]]
    projected_rows = (
        projected_rows * lax.rsqrt(square_sum / MODEL_WIDTH + NORM_FLOOR)[:, None]
    ).reshape(DECODE_STEPS, BEAM_TOTAL, heads_local, QUERIES_PER_KEY + 2, HEAD_WIDTH)
    beam_groups = jnp.arange(BEAM_TOTAL, dtype=jnp.int32) // BEAM_W
    positions = lookup(lengths, beam_groups)[None, :] + jnp.arange(DECODE_STEPS, dtype=jnp.int32)[:, None]
    queries = rotate_pairs(
        projected_rows[:, :, :, :QUERIES_PER_KEY], positions[:, :, None, None]
    ).astype(jnp.bfloat16)
    new_key = rotate_pairs(projected_rows[:, :, :, QUERIES_PER_KEY], positions[:, :, None]).astype(
        jnp.bfloat16
    )
    new_value = projected_rows[:, :, :, QUERIES_PER_KEY + 1].astype(jnp.bfloat16)
    slot_count = kv_cache.shape[0]
    slot_base = lax.axis_index("blk") * slot_count
    entry_ids = jnp.arange(BEAM_TOTAL * BEAM_BLOCKS, dtype=jnp.int32)
    slot_ids = slot_base + jnp.arange(slot_count, dtype=jnp.int32)
    slot_hits = tables.reshape(-1)[None, :] == slot_ids[:, None]
    entry_here = jnp.sum(jnp.where(slot_hits, entry_ids[None, :], 0), axis=1)
    owner_here = entry_here // BEAM_BLOCKS
    block_here = entry_here % BEAM_BLOCKS
    group_here = owner_here // BEAM_W
    anchor_groups = jnp.moveaxis(anchor.reshape(DECODE_STEPS, GROUPS, BEAM_W), 1, 0)
    anchor_query = jnp.broadcast_to(
        anchor_groups[..., None], (GROUPS, DECODE_STEPS, BEAM_W, QUERIES_PER_KEY)
    ).reshape(GROUPS, -1)
    recent_allowed = jnp.transpose(
        line_beams[:, :, :, None] == jnp.arange(BEAM_TOTAL, dtype=jnp.int32), (0, 2, 1, 3)
    ).reshape(DECODE_STEPS, BEAM_TOTAL, 1, count_tokens)
    is_first = lax.axis_index("blk") == 0
    query_head = queries[:, :, 0]
    query_groups = jnp.moveaxis(
        query_head.reshape(DECODE_STEPS, GROUPS, BEAM_W, QUERIES_PER_KEY, HEAD_WIDTH), 1, 0
    ).reshape(GROUPS, -1, HEAD_WIDTH)
    live_here = lookup(lengths, group_here) - block_here * BLOCK_POSITIONS
    query_match = lookup(anchor_query, group_here) == owner_here[:, None]
    used_here = (jnp.any(query_match, axis=1) & (live_here > 0)).astype(jnp.int32)
    anchor_lanes = jnp.broadcast_to(anchor_query[:, :, None], anchor_query.shape + (HEAD_WIDTH,))
    kv_pairs = kv_cache.reshape(slot_count, 2, BLOCK_POSITIONS, HEAD_WIDTH)
    vector_lanes, max_lanes, sum_lanes = slot_attention(
        group_here, live_here, owner_here, used_here, kv_pairs, query_groups, anchor_lanes, logit_scale
    )
    group_max = max_lanes[:, :, 0]
    group_sum = sum_lanes[:, :, 0]
    group_vector = vector_lanes
    cache_max = groups_to_beams(group_max)
    cache_sum = groups_to_beams(group_sum)
    cache_vector = groups_to_beams(group_vector)
    newest_keys = new_key[:, :, 0].reshape(count_tokens, HEAD_WIDTH)
    newest_values = new_value[:, :, 0].reshape(count_tokens, HEAD_WIDTH)
    newest_logits = (
        jnp.einsum("sbqd,kd->sbqk", query_head, newest_keys, preferred_element_type=jnp.float32)
        * logit_scale
    )
    recent_masked = jnp.where(recent_allowed, newest_logits, NEG_FILL)
    recent_max = jnp.max(recent_masked, axis=-1)
    recent_weights = jnp.where(recent_allowed, jnp.exp(recent_masked - recent_max[..., None]), 0.0)
    recent_sum = jnp.sum(recent_weights, axis=-1)
    recent_vector = jnp.einsum(
        "sbqk,kd->sbqd",
        recent_weights.astype(jnp.bfloat16),
        newest_values,
        preferred_element_type=jnp.float32,
    )
    recent_max = jnp.where(is_first, recent_max, NEG_FILL)
    recent_sum = jnp.where(is_first, recent_sum, 0.0)
    recent_vector = jnp.where(is_first, recent_vector, 0.0)
    local_max, local_sum, local_vector = combine_parts(
        (cache_max, cache_sum, cache_vector), (recent_max, recent_sum, recent_vector)
    )
    max_heads = [local_max]
    sum_heads = [local_sum]
    vector_heads = [local_vector]
    part_max = jnp.stack(max_heads, axis=2)
    part_sum = jnp.stack(sum_heads, axis=2)
    part_vector = jnp.stack(vector_heads, axis=2)
    part_shape = part_max.shape
    vector_rows = part_vector.reshape(-1, HEAD_WIDTH)
    stat_rows = jnp.stack([part_max.reshape(-1), part_sum.reshape(-1)]).reshape(-1, HEAD_WIDTH)

    def packed_combine(first, second):
        def unpack(packed):
            stats = packed[vector_rows.shape[0] :].reshape(2, -1)
            return stats[0], stats[1], packed[: vector_rows.shape[0]]

        larger, total, vector = combine_parts(unpack(first), unpack(second))
        stats = jnp.stack([larger, total]).reshape(-1, HEAD_WIDTH)
        return jnp.concatenate([vector, stats], axis=0)

    whole_packed = butterfly(
        jnp.concatenate([vector_rows, stat_rows], axis=0), "blk", blk_size, packed_combine, BLK_RADICES
    )
    whole_vector = whole_packed[: vector_rows.shape[0]].reshape(part_vector.shape)
    whole_sum = whole_packed[vector_rows.shape[0] :].reshape(2, -1)[1].reshape(part_shape)
    attended_rows = (
        (whole_vector / whole_sum[..., None]).astype(jnp.bfloat16).reshape(count_tokens, -1)
    )
    attn_partial = jnp.dot(attended_rows, out_weight, preferred_element_type=jnp.float32)
    attn_out = head_total(attn_partial, kv_size)
    residual = (flat_in + attn_out).astype(jnp.bfloat16)
    experts_local = expert_in.shape[0]
    ff_local = expert_in.shape[3]
    rows_per_expert = DECODE_STEPS * CAP
    rows_local = experts_local * rows_per_expert
    flat_routes = routes.reshape(count_tokens, 2)
    rank = expert_rank(routes).reshape(count_tokens, 2)
    step_of = jnp.arange(count_tokens, dtype=jnp.int32) // BEAM_TOTAL
    row_id = (flat_routes * rows_per_expert + step_of[:, None] * CAP + rank).reshape(-1)
    token_ids = jnp.broadcast_to(
        jnp.arange(count_tokens, dtype=jnp.int32)[:, None], (count_tokens, 2)
    ).reshape(-1)
    table_size = EXPERTS * rows_per_expert
    row_token_all = jnp.zeros((table_size,), jnp.int32).at[row_id].set(token_ids)
    row_live_all = jnp.zeros((table_size,), jnp.float32).at[row_id].set(1.0)
    row_other_all = (
        jnp.zeros((table_size,), jnp.int32).at[row_id].set(flat_routes[:, ::-1].reshape(-1))
    )
    row_start = lax.axis_index("kv") * rows_local
    row_token = lax.dynamic_slice_in_dim(row_token_all, row_start, rows_local)
    row_live = lax.dynamic_slice_in_dim(row_live_all, row_start, rows_local)
    row_other = lax.dynamic_slice_in_dim(row_other_all, row_start, rows_local)
    row_own = (row_start + jnp.arange(rows_local, dtype=jnp.int32)) // rows_per_expert
    in_flat = expert_in.reshape(experts_local, MODEL_WIDTH, 2 * ff_local)
    gain_wide = ffn_gain.astype(jnp.float32)
    full_rows = jnp.moveaxis(
        lax.all_to_all(
            jnp.broadcast_to(residual[None], (blk_size,) + residual.shape), "blk", 0, 0, tiled=True
        ),
        0,
        1,
    ).reshape(residual.shape[0], -1)
    chosen = full_rows[row_token].astype(jnp.float32)
    pre_rows = (chosen * gain_wide).astype(jnp.bfloat16)
    sums_in = jnp.einsum(
        "erd,edf->erf",
        pre_rows.reshape(experts_local, rows_per_expert, MODEL_WIDTH),
        in_flat,
        preferred_element_type=jnp.float32,
    )
    sums_router = jnp.dot(pre_rows, router_weight, preferred_element_type=jnp.float32)
    sum_sq = jnp.sum(chosen * chosen, axis=1)
    inv_rows = lax.rsqrt(sum_sq / MODEL_WIDTH + NORM_FLOOR)
    expert_act = sums_in * inv_rows.reshape(experts_local, rows_per_expert)[:, :, None]
    expert_hidden = (jax.nn.silu(expert_act[..., :ff_local]) * expert_act[..., ff_local:]).astype(
        jnp.bfloat16
    )
    down_part = jnp.einsum(
        "erf,efd->erd", expert_hidden, expert_down, preferred_element_type=jnp.float32
    ).reshape(rows_local, MODEL_WIDTH)
    expert_pieces = jnp.moveaxis(down_part.reshape(rows_local, blk_size, -1), 1, 0)
    expert_result = jnp.sum(lax.all_to_all(expert_pieces, "blk", 0, 0, tiled=True), axis=0)
    logits = sums_router * inv_rows[:, None]
    expert_ids = jnp.arange(EXPERTS, dtype=jnp.int32)
    own_logit = jnp.sum(jnp.where(row_own[:, None] == expert_ids[None, :], logits, 0.0), axis=1)
    other_logit = jnp.sum(jnp.where(row_other[:, None] == expert_ids[None, :], logits, 0.0), axis=1)
    gate_share = row_live / (1.0 + jnp.exp(other_logit - own_logit))
    weighted_values = expert_result * gate_share[:, None]
    placement = (row_token[None, :] == jnp.arange(count_tokens, dtype=jnp.int32)[:, None]).astype(
        jnp.float32
    )
    mixture_part = jnp.dot(placement, weighted_values, precision=lax.Precision.HIGHEST)
    mixture = head_total(mixture_part, kv_size)
    layer_out = (residual.astype(jnp.float32) + mixture).astype(jnp.bfloat16)
    return layer_out.reshape(DECODE_STEPS, BEAM_TOTAL, width_local)


def solution(mesh):
    placed = (
        P(None, None, "blk"),
        P("blk"),
        P(),
        P("blk", "kv", None),
        P("kv", "blk"),
        P(),
        P("kv", None, None, "blk"),
        P("kv", "blk", None),
        P("blk", None, "kv", None, None),
        P(),
        P(),
        P(),
        P(),
    )
    kv_size = mesh.shape["kv"]
    blk_size = mesh.shape["blk"]

    def sized(*arrays):
        return body(*arrays, kv_size, blk_size)

    return jax.shard_map(
        sized, mesh=mesh, in_specs=placed, out_specs=P(None, None, "blk"), check_vma=False
    )
```

```python
import functools
import math

import jax
import jax.numpy as jnp
from jax import lax
from jax.experimental import pallas as pl
from jax.experimental.pallas import tpu as pltpu
from jax.sharding import PartitionSpec as P

MODEL_WIDTH = 4096
HEAD_WIDTH = 128
QUERIES_PER_KEY = 4
EXPERTS = 8
BEAM_W = 8
GROUPS = 2
DECODE_STEPS = 4
BLOCK_POSITIONS = 128
BEAM_BLOCKS = 128
BEAM_TOTAL = 16
CAP = 6


NORM_FLOOR = 1e-05
ROPE_BASE = 1000000.0
NEG_FILL = -1e30
BLK_RADICES = (2, 4, 4)
SCATTER_RADICES = (4, 4, 2)
KV_RADICES = (2, 2, 2)


def exchange(value, axis, size, distance):
    pairs = [(index, index ^ distance) for index in range(size)]
    return jax.tree.map(lambda part: lax.ppermute(part, axis, pairs), value)


def tree_join(parts, join):
    stride = 1
    while stride < len(parts):
        parts = [
            join(parts[place], parts[place + stride]) if place % (2 * stride) == 0 else parts[place]
            for place in range(len(parts))
        ]
        stride *= 2
    return parts[0]


def butterfly(value, axis, size, join, radices):
    distance = 1
    for radix in radices:
        parts = [value] + [
            exchange(value, axis, size, distance * offset) for offset in range(1, radix)
        ]
        value = tree_join(parts, join)
        distance *= radix
    assert distance == size
    return value


def add_parts(first, second):
    return jax.tree.map(lambda one, two: one + two, first, second)


def gather_doubling(block, axis, size, dim, radices):
    index = lax.axis_index(axis)
    distance = 1
    for radix in radices:
        place = (index // distance) % radix
        parts = [block] + [
            exchange(block, axis, size, distance * offset) for offset in range(1, radix)
        ]
        stacked = jnp.stack(parts)
        ordered = jnp.take(stacked, jnp.arange(radix, dtype=jnp.int32) ^ place, axis=0)
        block = jnp.concatenate([ordered[slot] for slot in range(radix)], dim)
        distance *= radix
    assert distance == size
    return block


def scatter_halving(value, axis, size, dim, radices):
    index = lax.axis_index(axis)
    distance = size
    for radix in radices:
        distance //= radix
        place = (index // distance) % radix
        piece = value.shape[dim] // radix
        received = [lax.dynamic_slice_in_dim(value, place * piece, piece, dim)]
        for offset in range(1, radix):
            send = lax.dynamic_slice_in_dim(value, (place ^ offset) * piece, piece, dim)
            received.append(exchange(send, axis, size, distance * offset))
        value = tree_join(received, add_parts)
    assert distance == 1
    return value


def rotate_pairs(vectors, positions):
    half_width = vectors.shape[-1] // 2
    exponents = jnp.arange(half_width, dtype=jnp.float32) * (2.0 / vectors.shape[-1])
    frequency = ROPE_BASE ** (-exponents)
    angles = positions.astype(jnp.float32)[..., None] * frequency
    cosine = jnp.cos(angles)
    sine_part = jnp.sin(angles)
    lower_half = vectors[..., :half_width]
    upper_half = vectors[..., half_width:]
    return jnp.concatenate(
        [
            lower_half * cosine - upper_half * sine_part,
            upper_half * cosine + lower_half * sine_part,
        ],
        axis=-1,
    )


def slot_attention_kernel(group_ref, live_ref, owner_ref, used_ref, kv_ref, query_ref, anchor_ref,
                          vector_ref, max_ref, sum_ref, *, scale):
    vector_ref[...] = jnp.zeros(vector_ref.shape, jnp.float32)
    max_ref[...] = jnp.full(max_ref.shape, NEG_FILL, jnp.float32)
    sum_ref[...] = jnp.zeros(sum_ref.shape, jnp.float32)

    def visit(slot, carry):
        @pl.when(used_ref[slot] > 0)
        def _():
            group = group_ref[slot]
            keys = kv_ref[slot, 0]
            values = kv_ref[slot, 1]
            queries = query_ref[group]
            scores = lax.dot_general(
                queries, keys, (((1,), (1,)), ((), ())), preferred_element_type=jnp.float32
            ) * scale
            position = lax.broadcasted_iota(jnp.int32, scores.shape, 1)
            allowed = (position < live_ref[slot]) & (anchor_ref[group] == owner_ref[slot])
            masked = jnp.where(allowed, scores, NEG_FILL)
            old_max = max_ref[group]
            new_max = jnp.maximum(old_max, jnp.max(masked, axis=1, keepdims=True))
            weights = jnp.where(allowed, jnp.exp(masked - new_max), 0.0)
            keep = jnp.exp(old_max - new_max)
            sum_ref[group] = keep * sum_ref[group] + jnp.sum(weights, axis=1, keepdims=True)
            vector_ref[group] = keep * vector_ref[group] + jnp.dot(
                weights.astype(jnp.bfloat16), values, preferred_element_type=jnp.float32
            )
            max_ref[group] = new_max
        return carry

    lax.fori_loop(0, kv_ref.shape[0], visit, 0)


def slot_attention(group_here, live_here, owner_here, used_here, kv_pairs, query_groups, anchor_lanes, scale):
    groups, rows, width = query_groups.shape
    smem = pl.BlockSpec(memory_space=pltpu.SMEM)
    vmem = pl.BlockSpec(memory_space=pltpu.VMEM)
    shape = jax.ShapeDtypeStruct((groups, rows, width), jnp.float32)
    return pl.pallas_call(
        functools.partial(slot_attention_kernel, scale=scale),
        in_specs=[smem, smem, smem, smem, vmem, vmem, vmem],
        out_specs=[vmem, vmem, vmem],
        out_shape=[shape, shape, shape],
    )(group_here, live_here, owner_here, used_here, kv_pairs, query_groups, anchor_lanes)


def lookup(table, index):
    hits = index[..., None] == jnp.arange(table.shape[0], dtype=jnp.int32)
    shaped = hits.reshape(hits.shape + (1,) * (table.ndim - 1))
    return jnp.sum(jnp.where(shaped, table, jnp.zeros((), table.dtype)), axis=index.ndim)


def lineage(parents):
    steps_count, beam_count = parents.shape
    beam_ids = jnp.arange(beam_count, dtype=jnp.int32)
    line_rows = []
    anchor_rows = []
    for step_index in range(steps_count):
        current = beam_ids
        levels = [jnp.full((beam_count,), -1, jnp.int32) for level_index in range(steps_count)]
        for level_index in range(step_index, -1, -1):
            levels[level_index] = current
            current = lookup(parents[level_index], current)
        line_rows.append(jnp.stack(levels))
        anchor_rows.append(current)
    return (jnp.stack(line_rows), jnp.stack(anchor_rows))


def expert_rank(routes):
    steps_count, beam_count, pick_count = routes.shape
    onehot = (routes[..., None] == jnp.arange(EXPERTS, dtype=jnp.int32)).astype(jnp.int32)
    flat_hits = onehot.reshape(steps_count, beam_count * pick_count, EXPERTS)
    before = jnp.cumsum(flat_hits, axis=1) - flat_hits
    return jnp.sum(before * flat_hits, axis=-1).reshape(steps_count, beam_count, pick_count)


def head_total(partial_value, kv_size):
    return butterfly(partial_value, "kv", kv_size, add_parts, KV_RADICES)


def combine_parts(part_one, part_two):
    max_one, sum_one, vector_one = part_one
    max_two, sum_two, vector_two = part_two
    larger = jnp.maximum(max_one, max_two)
    scale_one = jnp.exp(max_one - larger)
    scale_two = jnp.exp(max_two - larger)
    return (
        larger,
        sum_one * scale_one + sum_two * scale_two,
        vector_one * scale_one[..., None] + vector_two * scale_two[..., None],
    )


def groups_to_beams(grouped):
    shaped = grouped.reshape((GROUPS, DECODE_STEPS, BEAM_W, QUERIES_PER_KEY) + grouped.shape[2:])
    shaped = jnp.moveaxis(shaped, 1, 0)
    return shaped.reshape((DECODE_STEPS, BEAM_TOTAL, QUERIES_PER_KEY) + grouped.shape[2:])


def body(
    hidden_in,
    attn_gain,
    ffn_gain,
    query_key_value_weight,
    out_weight,
    router_weight,
    expert_in,
    expert_down,
    kv_cache,
    lengths,
    tables,
    parents,
    routes,
    kv_size,
    blk_size,
):
    count_tokens = DECODE_STEPS * BEAM_TOTAL
    width_local = hidden_in.shape[2]
    heads_local = query_key_value_weight.shape[1]
    logit_scale = 1.0 / math.sqrt(HEAD_WIDTH)
    line_beams, anchor = lineage(parents)
    flat_in = hidden_in.reshape(count_tokens, width_local).astype(jnp.float32)
    pre_attn = (flat_in * attn_gain.astype(jnp.float32)).astype(jnp.bfloat16)
    partial_proj = jnp.dot(
        pre_attn,
        query_key_value_weight.reshape(width_local, -1),
        preferred_element_type=jnp.float32,
    )
    partial_sq = jnp.sum(flat_in * flat_in, axis=1)
    proj_rows = partial_proj.reshape(-1, HEAD_WIDTH)
    sq_rows = jnp.pad(partial_sq, (0, -partial_sq.shape[0] % HEAD_WIDTH)).reshape(-1, HEAD_WIDTH)
    stacked = jnp.concatenate([proj_rows, sq_rows], axis=0)
    chunk_rows = -(-stacked.shape[0] // (8 * blk_size)) * 8
    stacked = jnp.pad(stacked, ((0, chunk_rows * blk_size - stacked.shape[0]), (0, 0)))
    owned = jnp.sum(
        lax.all_to_all(stacked.reshape(blk_size, chunk_rows, HEAD_WIDTH), "blk", 0, 0, tiled=True),
        axis=0,
    )
    summed = lax.all_to_all(
        jnp.broadcast_to(owned[None], (blk_size,) + owned.shape), "blk", 0, 0, tiled=True
    ).reshape(-1, HEAD_WIDTH)
    projected_rows = summed[: proj_rows.shape[0]].reshape(partial_proj.shape)
    square_sum = summed[proj_rows.shape[0] :].reshape(-1)[: partial_sq.shape[0]]
    projected_rows = (
        projected_rows * lax.rsqrt(square_sum / MODEL_WIDTH + NORM_FLOOR)[:, None]
    ).reshape(DECODE_STEPS, BEAM_TOTAL, heads_local, QUERIES_PER_KEY + 2, HEAD_WIDTH)
    beam_groups = jnp.arange(BEAM_TOTAL, dtype=jnp.int32) // BEAM_W
    positions = lookup(lengths, beam_groups)[None, :] + jnp.arange(DECODE_STEPS, dtype=jnp.int32)[:, None]
    queries = rotate_pairs(
        projected_rows[:, :, :, :QUERIES_PER_KEY], positions[:, :, None, None]
    ).astype(jnp.bfloat16)
    new_key = rotate_pairs(projected_rows[:, :, :, QUERIES_PER_KEY], positions[:, :, None]).astype(
        jnp.bfloat16
    )
    new_value = projected_rows[:, :, :, QUERIES_PER_KEY + 1].astype(jnp.bfloat16)
    slot_count = kv_cache.shape[0]
    slot_base = lax.axis_index("blk") * slot_count
    entry_ids = jnp.arange(BEAM_TOTAL * BEAM_BLOCKS, dtype=jnp.int32)
    slot_ids = slot_base + jnp.arange(slot_count, dtype=jnp.int32)
    slot_hits = tables.reshape(-1)[None, :] == slot_ids[:, None]
    entry_here = jnp.sum(jnp.where(slot_hits, entry_ids[None, :], 0), axis=1)
    owner_here = entry_here // BEAM_BLOCKS
    block_here = entry_here % BEAM_BLOCKS
    group_here = owner_here // BEAM_W
    anchor_groups = jnp.moveaxis(anchor.reshape(DECODE_STEPS, GROUPS, BEAM_W), 1, 0)
    anchor_query = jnp.broadcast_to(
        anchor_groups[..., None], (GROUPS, DECODE_STEPS, BEAM_W, QUERIES_PER_KEY)
    ).reshape(GROUPS, -1)
    recent_allowed = jnp.transpose(
        line_beams[:, :, :, None] == jnp.arange(BEAM_TOTAL, dtype=jnp.int32), (0, 2, 1, 3)
    ).reshape(DECODE_STEPS, BEAM_TOTAL, 1, count_tokens)
    is_first = lax.axis_index("blk") == 0
    query_head = queries[:, :, 0]
    query_groups = jnp.moveaxis(
        query_head.reshape(DECODE_STEPS, GROUPS, BEAM_W, QUERIES_PER_KEY, HEAD_WIDTH), 1, 0
    ).reshape(GROUPS, -1, HEAD_WIDTH)
    live_here = lookup(lengths, group_here) - block_here * BLOCK_POSITIONS
    query_match = lookup(anchor_query, group_here) == owner_here[:, None]
    used_here = (jnp.any(query_match, axis=1) & (live_here > 0)).astype(jnp.int32)
    anchor_lanes = jnp.broadcast_to(anchor_query[:, :, None], anchor_query.shape + (HEAD_WIDTH,))
    kv_pairs = kv_cache.reshape(slot_count, 2, BLOCK_POSITIONS, HEAD_WIDTH)
    vector_lanes, max_lanes, sum_lanes = slot_attention(
        group_here, live_here, owner_here, used_here, kv_pairs, query_groups, anchor_lanes, logit_scale
    )
    group_max = max_lanes[:, :, 0]
    group_sum = sum_lanes[:, :, 0]
    group_vector = vector_lanes
    cache_max = groups_to_beams(group_max)
    cache_sum = groups_to_beams(group_sum)
    cache_vector = groups_to_beams(group_vector)
    newest_keys = new_key[:, :, 0].reshape(count_tokens, HEAD_WIDTH)
    newest_values = new_value[:, :, 0].reshape(count_tokens, HEAD_WIDTH)
    newest_logits = (
        jnp.einsum("sbqd,kd->sbqk", query_head, newest_keys, preferred_element_type=jnp.float32)
        * logit_scale
    )
    recent_masked = jnp.where(recent_allowed, newest_logits, NEG_FILL)
    recent_max = jnp.max(recent_masked, axis=-1)
    recent_weights = jnp.where(recent_allowed, jnp.exp(recent_masked - recent_max[..., None]), 0.0)
    recent_sum = jnp.sum(recent_weights, axis=-1)
    recent_vector = jnp.einsum(
        "sbqk,kd->sbqd",
        recent_weights.astype(jnp.bfloat16),
        newest_values,
        preferred_element_type=jnp.float32,
    )
    recent_max = jnp.where(is_first, recent_max, NEG_FILL)
    recent_sum = jnp.where(is_first, recent_sum, 0.0)
    recent_vector = jnp.where(is_first, recent_vector, 0.0)
    local_max, local_sum, local_vector = combine_parts(
        (cache_max, cache_sum, cache_vector), (recent_max, recent_sum, recent_vector)
    )
    max_heads = [local_max]
    sum_heads = [local_sum]
    vector_heads = [local_vector]
    part_max = jnp.stack(max_heads, axis=2)
    part_sum = jnp.stack(sum_heads, axis=2)
    part_vector = jnp.stack(vector_heads, axis=2)
    query_rows = part_vector.reshape(-1, HEAD_WIDTH)
    row_count = query_rows.shape[0]
    packed_rows = jnp.concatenate(
        [
            query_rows,
            part_max.reshape(-1, 1),
            part_sum.reshape(-1, 1),
            jnp.zeros((row_count, HEAD_WIDTH - 2), jnp.float32),
        ],
        axis=1,
    ).reshape(blk_size, row_count // blk_size, 2 * HEAD_WIDTH)
    peer_rows = lax.all_to_all(packed_rows, "blk", 0, 0, tiled=True)
    peer_max = peer_rows[:, :, HEAD_WIDTH]
    peer_scale = jnp.exp(peer_max - jnp.max(peer_max, axis=0)[None])
    merged_sum = jnp.sum(peer_rows[:, :, HEAD_WIDTH + 1] * peer_scale, axis=0)
    merged_vector = jnp.sum(peer_rows[:, :, :HEAD_WIDTH] * peer_scale[:, :, None], axis=0)
    owned_rows = (merged_vector / merged_sum[:, None]).astype(jnp.bfloat16)
    attended_rows = lax.all_to_all(
        jnp.broadcast_to(owned_rows[None], (blk_size,) + owned_rows.shape), "blk", 0, 0, tiled=True
    ).reshape(count_tokens, -1)
    attn_partial = jnp.dot(attended_rows, out_weight, preferred_element_type=jnp.float32)
    attn_out = head_total(attn_partial, kv_size)
    residual = (flat_in + attn_out).astype(jnp.bfloat16)
    experts_local = expert_in.shape[0]
    ff_local = expert_in.shape[3]
    rows_per_expert = DECODE_STEPS * CAP
    rows_local = experts_local * rows_per_expert
    flat_routes = routes.reshape(count_tokens, 2)
    rank = expert_rank(routes).reshape(count_tokens, 2)
    step_of = jnp.arange(count_tokens, dtype=jnp.int32) // BEAM_TOTAL
    row_id = (flat_routes * rows_per_expert + step_of[:, None] * CAP + rank).reshape(-1)
    token_ids = jnp.broadcast_to(
        jnp.arange(count_tokens, dtype=jnp.int32)[:, None], (count_tokens, 2)
    ).reshape(-1)
    table_size = EXPERTS * rows_per_expert
    row_token_all = jnp.zeros((table_size,), jnp.int32).at[row_id].set(token_ids)
    row_live_all = jnp.zeros((table_size,), jnp.float32).at[row_id].set(1.0)
    row_other_all = (
        jnp.zeros((table_size,), jnp.int32).at[row_id].set(flat_routes[:, ::-1].reshape(-1))
    )
    row_start = lax.axis_index("kv") * rows_local
    row_token = lax.dynamic_slice_in_dim(row_token_all, row_start, rows_local)
    row_live = lax.dynamic_slice_in_dim(row_live_all, row_start, rows_local)
    row_other = lax.dynamic_slice_in_dim(row_other_all, row_start, rows_local)
    row_own = (row_start + jnp.arange(rows_local, dtype=jnp.int32)) // rows_per_expert
    in_flat = expert_in.reshape(experts_local, MODEL_WIDTH, 2 * ff_local)
    gain_wide = ffn_gain.astype(jnp.float32)
    full_rows = jnp.moveaxis(
        lax.all_to_all(
            jnp.broadcast_to(residual[None], (blk_size,) + residual.shape), "blk", 0, 0, tiled=True
        ),
        0,
        1,
    ).reshape(residual.shape[0], -1)
    chosen = full_rows[row_token].astype(jnp.float32)
    pre_rows = (chosen * gain_wide).astype(jnp.bfloat16)
    sums_in = jnp.einsum(
        "erd,edf->erf",
        pre_rows.reshape(experts_local, rows_per_expert, MODEL_WIDTH),
        in_flat,
        preferred_element_type=jnp.float32,
    )
    sums_router = jnp.dot(pre_rows, router_weight, preferred_element_type=jnp.float32)
    sum_sq = jnp.sum(chosen * chosen, axis=1)
    inv_rows = lax.rsqrt(sum_sq / MODEL_WIDTH + NORM_FLOOR)
    expert_act = sums_in * inv_rows.reshape(experts_local, rows_per_expert)[:, :, None]
    expert_hidden = (jax.nn.silu(expert_act[..., :ff_local]) * expert_act[..., ff_local:]).astype(
        jnp.bfloat16
    )
    down_part = jnp.einsum(
        "erf,efd->erd", expert_hidden, expert_down, preferred_element_type=jnp.float32
    ).reshape(rows_local, MODEL_WIDTH)
    expert_pieces = jnp.moveaxis(down_part.reshape(rows_local, blk_size, -1), 1, 0)
    expert_result = jnp.sum(lax.all_to_all(expert_pieces, "blk", 0, 0, tiled=True), axis=0)
    logits = sums_router * inv_rows[:, None]
    expert_ids = jnp.arange(EXPERTS, dtype=jnp.int32)
    own_logit = jnp.sum(jnp.where(row_own[:, None] == expert_ids[None, :], logits, 0.0), axis=1)
    other_logit = jnp.sum(jnp.where(row_other[:, None] == expert_ids[None, :], logits, 0.0), axis=1)
    gate_share = row_live / (1.0 + jnp.exp(other_logit - own_logit))
    weighted_values = expert_result * gate_share[:, None]
    placement = (row_token[None, :] == jnp.arange(count_tokens, dtype=jnp.int32)[:, None]).astype(
        jnp.float32
    )
    mixture_part = jnp.dot(placement, weighted_values, precision=lax.Precision.HIGHEST)
    mixture = head_total(mixture_part, kv_size)
    layer_out = (residual.astype(jnp.float32) + mixture).astype(jnp.bfloat16)
    return layer_out.reshape(DECODE_STEPS, BEAM_TOTAL, width_local)


def solution(mesh):
    placed = (
        P(None, None, "blk"),
        P("blk"),
        P(),
        P("blk", "kv", None),
        P("kv", "blk"),
        P(),
        P("kv", None, None, "blk"),
        P("kv", "blk", None),
        P("blk", None, "kv", None, None),
        P(),
        P(),
        P(),
        P(),
    )
    kv_size = mesh.shape["kv"]
    blk_size = mesh.shape["blk"]

    def sized(*arrays):
        return body(*arrays, kv_size, blk_size)

    return jax.shard_map(
        sized, mesh=mesh, in_specs=placed, out_specs=P(None, None, "blk"), check_vma=False
    )
```

```python
import functools
import math

import jax
import jax.numpy as jnp
from jax import lax
from jax.experimental import pallas as pl
from jax.experimental.pallas import tpu as pltpu
from jax.sharding import PartitionSpec as P

MODEL_WIDTH = 4096
HEAD_WIDTH = 128
QUERIES_PER_KEY = 4
EXPERTS = 8
BEAM_W = 8
GROUPS = 2
DECODE_STEPS = 4
BLOCK_POSITIONS = 128
BEAM_BLOCKS = 128
BEAM_TOTAL = 16
CAP = 6


NORM_FLOOR = 1e-05
ROPE_BASE = 1000000.0
NEG_FILL = -1e30
BLK_RADICES = (2, 4, 4)
SCATTER_RADICES = (4, 4, 2)
KV_RADICES = (2, 2, 2)


def exchange(value, axis, size, distance):
    pairs = [(index, index ^ distance) for index in range(size)]
    return jax.tree.map(lambda part: lax.ppermute(part, axis, pairs), value)


def tree_join(parts, join):
    stride = 1
    while stride < len(parts):
        parts = [
            join(parts[place], parts[place + stride]) if place % (2 * stride) == 0 else parts[place]
            for place in range(len(parts))
        ]
        stride *= 2
    return parts[0]


def butterfly(value, axis, size, join, radices):
    distance = 1
    for radix in radices:
        parts = [value] + [
            exchange(value, axis, size, distance * offset) for offset in range(1, radix)
        ]
        value = tree_join(parts, join)
        distance *= radix
    assert distance == size
    return value


def add_parts(first, second):
    return jax.tree.map(lambda one, two: one + two, first, second)


def gather_doubling(block, axis, size, dim, radices):
    index = lax.axis_index(axis)
    distance = 1
    for radix in radices:
        place = (index // distance) % radix
        parts = [block] + [
            exchange(block, axis, size, distance * offset) for offset in range(1, radix)
        ]
        stacked = jnp.stack(parts)
        ordered = jnp.take(stacked, jnp.arange(radix, dtype=jnp.int32) ^ place, axis=0)
        block = jnp.concatenate([ordered[slot] for slot in range(radix)], dim)
        distance *= radix
    assert distance == size
    return block


def scatter_halving(value, axis, size, dim, radices):
    index = lax.axis_index(axis)
    distance = size
    for radix in radices:
        distance //= radix
        place = (index // distance) % radix
        piece = value.shape[dim] // radix
        received = [lax.dynamic_slice_in_dim(value, place * piece, piece, dim)]
        for offset in range(1, radix):
            send = lax.dynamic_slice_in_dim(value, (place ^ offset) * piece, piece, dim)
            received.append(exchange(send, axis, size, distance * offset))
        value = tree_join(received, add_parts)
    assert distance == 1
    return value


def rotate_pairs(vectors, positions):
    half_width = vectors.shape[-1] // 2
    exponents = jnp.arange(half_width, dtype=jnp.float32) * (2.0 / vectors.shape[-1])
    frequency = ROPE_BASE ** (-exponents)
    angles = positions.astype(jnp.float32)[..., None] * frequency
    cosine = jnp.cos(angles)
    sine_part = jnp.sin(angles)
    lower_half = vectors[..., :half_width]
    upper_half = vectors[..., half_width:]
    return jnp.concatenate(
        [
            lower_half * cosine - upper_half * sine_part,
            upper_half * cosine + lower_half * sine_part,
        ],
        axis=-1,
    )


def slot_attention_kernel(group_ref, live_ref, owner_ref, used_ref, kv_ref, query_ref, anchor_ref,
                          vector_ref, max_ref, sum_ref, *, scale):
    vector_ref[...] = jnp.zeros(vector_ref.shape, jnp.float32)
    max_ref[...] = jnp.full(max_ref.shape, NEG_FILL, jnp.float32)
    sum_ref[...] = jnp.zeros(sum_ref.shape, jnp.float32)

    def visit(slot, carry):
        @pl.when(used_ref[slot] > 0)
        def _():
            group = group_ref[slot]
            keys = kv_ref[slot, 0]
            values = kv_ref[slot, 1]
            queries = query_ref[group]
            scores = lax.dot_general(
                queries, keys, (((1,), (1,)), ((), ())), preferred_element_type=jnp.float32
            ) * scale
            position = lax.broadcasted_iota(jnp.int32, scores.shape, 1)
            allowed = (position < live_ref[slot]) & (anchor_ref[group] == owner_ref[slot])
            masked = jnp.where(allowed, scores, NEG_FILL)
            old_max = max_ref[group]
            new_max = jnp.maximum(old_max, jnp.max(masked, axis=1, keepdims=True))
            weights = jnp.where(allowed, jnp.exp(masked - new_max), 0.0)
            keep = jnp.exp(old_max - new_max)
            sum_ref[group] = keep * sum_ref[group] + jnp.sum(weights, axis=1, keepdims=True)
            vector_ref[group] = keep * vector_ref[group] + jnp.dot(
                weights.astype(jnp.bfloat16), values, preferred_element_type=jnp.float32
            )
            max_ref[group] = new_max
        return carry

    lax.fori_loop(0, kv_ref.shape[0], visit, 0, unroll=4)


def slot_attention(group_here, live_here, owner_here, used_here, kv_pairs, query_groups, anchor_lanes, scale):
    groups, rows, width = query_groups.shape
    smem = pl.BlockSpec(memory_space=pltpu.SMEM)
    vmem = pl.BlockSpec(memory_space=pltpu.VMEM)
    shape = jax.ShapeDtypeStruct((groups, rows, width), jnp.float32)
    return pl.pallas_call(
        functools.partial(slot_attention_kernel, scale=scale),
        in_specs=[smem, smem, smem, smem, vmem, vmem, vmem],
        out_specs=[vmem, vmem, vmem],
        out_shape=[shape, shape, shape],
    )(group_here, live_here, owner_here, used_here, kv_pairs, query_groups, anchor_lanes)


def lookup(table, index):
    hits = index[..., None] == jnp.arange(table.shape[0], dtype=jnp.int32)
    shaped = hits.reshape(hits.shape + (1,) * (table.ndim - 1))
    return jnp.sum(jnp.where(shaped, table, jnp.zeros((), table.dtype)), axis=index.ndim)


def lineage(parents):
    steps_count, beam_count = parents.shape
    beam_ids = jnp.arange(beam_count, dtype=jnp.int32)
    line_rows = []
    anchor_rows = []
    for step_index in range(steps_count):
        current = beam_ids
        levels = [jnp.full((beam_count,), -1, jnp.int32) for level_index in range(steps_count)]
        for level_index in range(step_index, -1, -1):
            levels[level_index] = current
            current = lookup(parents[level_index], current)
        line_rows.append(jnp.stack(levels))
        anchor_rows.append(current)
    return (jnp.stack(line_rows), jnp.stack(anchor_rows))


def expert_rank(routes):
    steps_count, beam_count, pick_count = routes.shape
    onehot = (routes[..., None] == jnp.arange(EXPERTS, dtype=jnp.int32)).astype(jnp.int32)
    flat_hits = onehot.reshape(steps_count, beam_count * pick_count, EXPERTS)
    before = jnp.cumsum(flat_hits, axis=1) - flat_hits
    return jnp.sum(before * flat_hits, axis=-1).reshape(steps_count, beam_count, pick_count)


def head_total(partial_value, kv_size):
    return butterfly(partial_value, "kv", kv_size, add_parts, KV_RADICES)


def combine_parts(part_one, part_two):
    max_one, sum_one, vector_one = part_one
    max_two, sum_two, vector_two = part_two
    larger = jnp.maximum(max_one, max_two)
    scale_one = jnp.exp(max_one - larger)
    scale_two = jnp.exp(max_two - larger)
    return (
        larger,
        sum_one * scale_one + sum_two * scale_two,
        vector_one * scale_one[..., None] + vector_two * scale_two[..., None],
    )


def groups_to_beams(grouped):
    shaped = grouped.reshape((GROUPS, DECODE_STEPS, BEAM_W, QUERIES_PER_KEY) + grouped.shape[2:])
    shaped = jnp.moveaxis(shaped, 1, 0)
    return shaped.reshape((DECODE_STEPS, BEAM_TOTAL, QUERIES_PER_KEY) + grouped.shape[2:])


def body(
    hidden_in,
    attn_gain,
    ffn_gain,
    query_key_value_weight,
    out_weight,
    router_weight,
    expert_in,
    expert_down,
    kv_cache,
    lengths,
    tables,
    parents,
    routes,
    kv_size,
    blk_size,
):
    count_tokens = DECODE_STEPS * BEAM_TOTAL
    width_local = hidden_in.shape[2]
    heads_local = query_key_value_weight.shape[1]
    logit_scale = 1.0 / math.sqrt(HEAD_WIDTH)
    line_beams, anchor = lineage(parents)
    flat_in = hidden_in.reshape(count_tokens, width_local).astype(jnp.float32)
    pre_attn = (flat_in * attn_gain.astype(jnp.float32)).astype(jnp.bfloat16)
    partial_proj = jnp.dot(
        pre_attn,
        query_key_value_weight.reshape(width_local, -1),
        preferred_element_type=jnp.float32,
    )
    partial_sq = jnp.sum(flat_in * flat_in, axis=1)
    proj_rows = partial_proj.reshape(-1, HEAD_WIDTH)
    sq_rows = jnp.pad(partial_sq, (0, -partial_sq.shape[0] % HEAD_WIDTH)).reshape(-1, HEAD_WIDTH)
    stacked = jnp.concatenate([proj_rows, sq_rows], axis=0)
    chunk_rows = -(-stacked.shape[0] // (8 * blk_size)) * 8
    stacked = jnp.pad(stacked, ((0, chunk_rows * blk_size - stacked.shape[0]), (0, 0)))
    owned = jnp.sum(
        lax.all_to_all(stacked.reshape(blk_size, chunk_rows, HEAD_WIDTH), "blk", 0, 0, tiled=True),
        axis=0,
    )
    summed = lax.all_to_all(
        jnp.broadcast_to(owned[None], (blk_size,) + owned.shape), "blk", 0, 0, tiled=True
    ).reshape(-1, HEAD_WIDTH)
    projected_rows = summed[: proj_rows.shape[0]].reshape(partial_proj.shape)
    square_sum = summed[proj_rows.shape[0] :].reshape(-1)[: partial_sq.shape[0]]
    projected_rows = (
        projected_rows * lax.rsqrt(square_sum / MODEL_WIDTH + NORM_FLOOR)[:, None]
    ).reshape(DECODE_STEPS, BEAM_TOTAL, heads_local, QUERIES_PER_KEY + 2, HEAD_WIDTH)
    beam_groups = jnp.arange(BEAM_TOTAL, dtype=jnp.int32) // BEAM_W
    positions = lookup(lengths, beam_groups)[None, :] + jnp.arange(DECODE_STEPS, dtype=jnp.int32)[:, None]
    queries = rotate_pairs(
        projected_rows[:, :, :, :QUERIES_PER_KEY], positions[:, :, None, None]
    ).astype(jnp.bfloat16)
    new_key = rotate_pairs(projected_rows[:, :, :, QUERIES_PER_KEY], positions[:, :, None]).astype(
        jnp.bfloat16
    )
    new_value = projected_rows[:, :, :, QUERIES_PER_KEY + 1].astype(jnp.bfloat16)
    slot_count = kv_cache.shape[0]
    slot_base = lax.axis_index("blk") * slot_count
    entry_ids = jnp.arange(BEAM_TOTAL * BEAM_BLOCKS, dtype=jnp.int32)
    slot_ids = slot_base + jnp.arange(slot_count, dtype=jnp.int32)
    slot_hits = tables.reshape(-1)[None, :] == slot_ids[:, None]
    entry_here = jnp.sum(jnp.where(slot_hits, entry_ids[None, :], 0), axis=1)
    owner_here = entry_here // BEAM_BLOCKS
    block_here = entry_here % BEAM_BLOCKS
    group_here = owner_here // BEAM_W
    anchor_groups = jnp.moveaxis(anchor.reshape(DECODE_STEPS, GROUPS, BEAM_W), 1, 0)
    anchor_query = jnp.broadcast_to(
        anchor_groups[..., None], (GROUPS, DECODE_STEPS, BEAM_W, QUERIES_PER_KEY)
    ).reshape(GROUPS, -1)
    recent_allowed = jnp.transpose(
        line_beams[:, :, :, None] == jnp.arange(BEAM_TOTAL, dtype=jnp.int32), (0, 2, 1, 3)
    ).reshape(DECODE_STEPS, BEAM_TOTAL, 1, count_tokens)
    is_first = lax.axis_index("blk") == 0
    query_head = queries[:, :, 0]
    query_groups = jnp.moveaxis(
        query_head.reshape(DECODE_STEPS, GROUPS, BEAM_W, QUERIES_PER_KEY, HEAD_WIDTH), 1, 0
    ).reshape(GROUPS, -1, HEAD_WIDTH)
    live_here = lookup(lengths, group_here) - block_here * BLOCK_POSITIONS
    query_match = lookup(anchor_query, group_here) == owner_here[:, None]
    used_here = (jnp.any(query_match, axis=1) & (live_here > 0)).astype(jnp.int32)
    anchor_lanes = jnp.broadcast_to(anchor_query[:, :, None], anchor_query.shape + (HEAD_WIDTH,))
    kv_pairs = kv_cache.reshape(slot_count, 2, BLOCK_POSITIONS, HEAD_WIDTH)
    vector_lanes, max_lanes, sum_lanes = slot_attention(
        group_here, live_here, owner_here, used_here, kv_pairs, query_groups, anchor_lanes, logit_scale
    )
    group_max = max_lanes[:, :, 0]
    group_sum = sum_lanes[:, :, 0]
    group_vector = vector_lanes
    cache_max = groups_to_beams(group_max)
    cache_sum = groups_to_beams(group_sum)
    cache_vector = groups_to_beams(group_vector)
    newest_keys = new_key[:, :, 0].reshape(count_tokens, HEAD_WIDTH)
    newest_values = new_value[:, :, 0].reshape(count_tokens, HEAD_WIDTH)
    newest_logits = (
        jnp.einsum("sbqd,kd->sbqk", query_head, newest_keys, preferred_element_type=jnp.float32)
        * logit_scale
    )
    recent_masked = jnp.where(recent_allowed, newest_logits, NEG_FILL)
    recent_max = jnp.max(recent_masked, axis=-1)
    recent_weights = jnp.where(recent_allowed, jnp.exp(recent_masked - recent_max[..., None]), 0.0)
    recent_sum = jnp.sum(recent_weights, axis=-1)
    recent_vector = jnp.einsum(
        "sbqk,kd->sbqd",
        recent_weights.astype(jnp.bfloat16),
        newest_values,
        preferred_element_type=jnp.float32,
    )
    recent_max = jnp.where(is_first, recent_max, NEG_FILL)
    recent_sum = jnp.where(is_first, recent_sum, 0.0)
    recent_vector = jnp.where(is_first, recent_vector, 0.0)
    local_max, local_sum, local_vector = combine_parts(
        (cache_max, cache_sum, cache_vector), (recent_max, recent_sum, recent_vector)
    )
    max_heads = [local_max]
    sum_heads = [local_sum]
    vector_heads = [local_vector]
    part_max = jnp.stack(max_heads, axis=2)
    part_sum = jnp.stack(sum_heads, axis=2)
    part_vector = jnp.stack(vector_heads, axis=2)
    query_rows = part_vector.reshape(-1, HEAD_WIDTH)
    row_count = query_rows.shape[0]
    packed_rows = jnp.concatenate(
        [
            query_rows,
            part_max.reshape(-1, 1),
            part_sum.reshape(-1, 1),
            jnp.zeros((row_count, HEAD_WIDTH - 2), jnp.float32),
        ],
        axis=1,
    ).reshape(blk_size, row_count // blk_size, 2 * HEAD_WIDTH)
    peer_rows = lax.all_to_all(packed_rows, "blk", 0, 0, tiled=True)
    peer_max = peer_rows[:, :, HEAD_WIDTH]
    peer_scale = jnp.exp(peer_max - jnp.max(peer_max, axis=0)[None])
    merged_sum = jnp.sum(peer_rows[:, :, HEAD_WIDTH + 1] * peer_scale, axis=0)
    merged_vector = jnp.sum(peer_rows[:, :, :HEAD_WIDTH] * peer_scale[:, :, None], axis=0)
    owned_rows = (merged_vector / merged_sum[:, None]).astype(jnp.bfloat16)
    attended_rows = lax.all_to_all(
        jnp.broadcast_to(owned_rows[None], (blk_size,) + owned_rows.shape), "blk", 0, 0, tiled=True
    ).reshape(count_tokens, -1)
    attn_partial = jnp.dot(attended_rows, out_weight, preferred_element_type=jnp.float32)
    attn_out = head_total(attn_partial, kv_size)
    residual = (flat_in + attn_out).astype(jnp.bfloat16)
    experts_local = expert_in.shape[0]
    ff_local = expert_in.shape[3]
    rows_per_expert = DECODE_STEPS * CAP
    rows_local = experts_local * rows_per_expert
    flat_routes = routes.reshape(count_tokens, 2)
    rank = expert_rank(routes).reshape(count_tokens, 2)
    step_of = jnp.arange(count_tokens, dtype=jnp.int32) // BEAM_TOTAL
    row_id = (flat_routes * rows_per_expert + step_of[:, None] * CAP + rank).reshape(-1)
    token_ids = jnp.broadcast_to(
        jnp.arange(count_tokens, dtype=jnp.int32)[:, None], (count_tokens, 2)
    ).reshape(-1)
    table_size = EXPERTS * rows_per_expert
    row_token_all = jnp.zeros((table_size,), jnp.int32).at[row_id].set(token_ids)
    row_live_all = jnp.zeros((table_size,), jnp.float32).at[row_id].set(1.0)
    row_other_all = (
        jnp.zeros((table_size,), jnp.int32).at[row_id].set(flat_routes[:, ::-1].reshape(-1))
    )
    row_start = lax.axis_index("kv") * rows_local
    row_token = lax.dynamic_slice_in_dim(row_token_all, row_start, rows_local)
    row_live = lax.dynamic_slice_in_dim(row_live_all, row_start, rows_local)
    row_other = lax.dynamic_slice_in_dim(row_other_all, row_start, rows_local)
    row_own = (row_start + jnp.arange(rows_local, dtype=jnp.int32)) // rows_per_expert
    in_flat = expert_in.reshape(experts_local, MODEL_WIDTH, 2 * ff_local)
    gain_wide = ffn_gain.astype(jnp.float32)
    full_rows = jnp.moveaxis(
        lax.all_to_all(
            jnp.broadcast_to(residual[None], (blk_size,) + residual.shape), "blk", 0, 0, tiled=True
        ),
        0,
        1,
    ).reshape(residual.shape[0], -1)
    chosen = full_rows[row_token].astype(jnp.float32)
    pre_rows = (chosen * gain_wide).astype(jnp.bfloat16)
    sums_in = jnp.einsum(
        "erd,edf->erf",
        pre_rows.reshape(experts_local, rows_per_expert, MODEL_WIDTH),
        in_flat,
        preferred_element_type=jnp.float32,
    )
    sums_router = jnp.dot(pre_rows, router_weight, preferred_element_type=jnp.float32)
    sum_sq = jnp.sum(chosen * chosen, axis=1)
    inv_rows = lax.rsqrt(sum_sq / MODEL_WIDTH + NORM_FLOOR)
    expert_act = sums_in * inv_rows.reshape(experts_local, rows_per_expert)[:, :, None]
    expert_hidden = (jax.nn.silu(expert_act[..., :ff_local]) * expert_act[..., ff_local:]).astype(
        jnp.bfloat16
    )
    down_part = jnp.einsum(
        "erf,efd->erd", expert_hidden, expert_down, preferred_element_type=jnp.float32
    ).reshape(rows_local, MODEL_WIDTH)
    expert_pieces = jnp.moveaxis(down_part.reshape(rows_local, blk_size, -1), 1, 0)
    expert_result = jnp.sum(lax.all_to_all(expert_pieces, "blk", 0, 0, tiled=True), axis=0)
    logits = sums_router * inv_rows[:, None]
    expert_ids = jnp.arange(EXPERTS, dtype=jnp.int32)
    own_logit = jnp.sum(jnp.where(row_own[:, None] == expert_ids[None, :], logits, 0.0), axis=1)
    other_logit = jnp.sum(jnp.where(row_other[:, None] == expert_ids[None, :], logits, 0.0), axis=1)
    gate_share = row_live / (1.0 + jnp.exp(other_logit - own_logit))
    weighted_values = expert_result * gate_share[:, None]
    placement = (row_token[None, :] == jnp.arange(count_tokens, dtype=jnp.int32)[:, None]).astype(
        jnp.float32
    )
    mixture_part = jnp.dot(placement, weighted_values, precision=lax.Precision.HIGHEST)
    mixture = head_total(mixture_part, kv_size)
    layer_out = (residual.astype(jnp.float32) + mixture).astype(jnp.bfloat16)
    return layer_out.reshape(DECODE_STEPS, BEAM_TOTAL, width_local)


def solution(mesh):
    placed = (
        P(None, None, "blk"),
        P("blk"),
        P(),
        P("blk", "kv", None),
        P("kv", "blk"),
        P(),
        P("kv", None, None, "blk"),
        P("kv", "blk", None),
        P("blk", None, "kv", None, None),
        P(),
        P(),
        P(),
        P(),
    )
    kv_size = mesh.shape["kv"]
    blk_size = mesh.shape["blk"]

    def sized(*arrays):
        return body(*arrays, kv_size, blk_size)

    return jax.shard_map(
        sized, mesh=mesh, in_specs=placed, out_specs=P(None, None, "blk"), check_vma=False
    )
```

```python
import functools
import math

import jax
import jax.numpy as jnp
from jax import lax
from jax.experimental import pallas as pl
from jax.experimental.pallas import tpu as pltpu
from jax.sharding import PartitionSpec as P

MODEL_WIDTH = 4096
HEAD_WIDTH = 128
QUERIES_PER_KEY = 4
EXPERTS = 8
BEAM_W = 8
GROUPS = 2
DECODE_STEPS = 4
BLOCK_POSITIONS = 128
BEAM_BLOCKS = 128
BEAM_TOTAL = 16
CAP = 6


NORM_FLOOR = 1e-05
ROPE_BASE = 1000000.0
NEG_FILL = -1e30
BLK_RADICES = (2, 4, 4)
SCATTER_RADICES = (4, 4, 2)
KV_RADICES = (2, 2, 2)


def exchange(value, axis, size, distance):
    pairs = [(index, index ^ distance) for index in range(size)]
    return jax.tree.map(lambda part: lax.ppermute(part, axis, pairs), value)


def tree_join(parts, join):
    stride = 1
    while stride < len(parts):
        parts = [
            join(parts[place], parts[place + stride]) if place % (2 * stride) == 0 else parts[place]
            for place in range(len(parts))
        ]
        stride *= 2
    return parts[0]


def butterfly(value, axis, size, join, radices):
    distance = 1
    for radix in radices:
        parts = [value] + [
            exchange(value, axis, size, distance * offset) for offset in range(1, radix)
        ]
        value = tree_join(parts, join)
        distance *= radix
    assert distance == size
    return value


def add_parts(first, second):
    return jax.tree.map(lambda one, two: one + two, first, second)


def gather_doubling(block, axis, size, dim, radices):
    index = lax.axis_index(axis)
    distance = 1
    for radix in radices:
        place = (index // distance) % radix
        parts = [block] + [
            exchange(block, axis, size, distance * offset) for offset in range(1, radix)
        ]
        stacked = jnp.stack(parts)
        ordered = jnp.take(stacked, jnp.arange(radix, dtype=jnp.int32) ^ place, axis=0)
        block = jnp.concatenate([ordered[slot] for slot in range(radix)], dim)
        distance *= radix
    assert distance == size
    return block


def scatter_halving(value, axis, size, dim, radices):
    index = lax.axis_index(axis)
    distance = size
    for radix in radices:
        distance //= radix
        place = (index // distance) % radix
        piece = value.shape[dim] // radix
        received = [lax.dynamic_slice_in_dim(value, place * piece, piece, dim)]
        for offset in range(1, radix):
            send = lax.dynamic_slice_in_dim(value, (place ^ offset) * piece, piece, dim)
            received.append(exchange(send, axis, size, distance * offset))
        value = tree_join(received, add_parts)
    assert distance == 1
    return value


def rotate_pairs(vectors, positions):
    half_width = vectors.shape[-1] // 2
    exponents = jnp.arange(half_width, dtype=jnp.float32) * (2.0 / vectors.shape[-1])
    frequency = ROPE_BASE ** (-exponents)
    angles = positions.astype(jnp.float32)[..., None] * frequency
    cosine = jnp.cos(angles)
    sine_part = jnp.sin(angles)
    lower_half = vectors[..., :half_width]
    upper_half = vectors[..., half_width:]
    return jnp.concatenate(
        [
            lower_half * cosine - upper_half * sine_part,
            upper_half * cosine + lower_half * sine_part,
        ],
        axis=-1,
    )


def slot_attention_kernel(group_ref, live_ref, owner_ref, used_ref, kv_ref, query_ref, anchor_ref,
                          vector_ref, max_ref, sum_ref, *, scale):
    vector_ref[...] = jnp.zeros(vector_ref.shape, jnp.float32)
    max_ref[...] = jnp.full(max_ref.shape, NEG_FILL, jnp.float32)
    sum_ref[...] = jnp.zeros(sum_ref.shape, jnp.float32)

    def visit(slot, carry):
        @pl.when(used_ref[slot] > 0)
        def _():
            group = group_ref[slot]
            keys = kv_ref[slot, 0]
            values = kv_ref[slot, 1]
            queries = query_ref[group]
            scores = lax.dot_general(
                queries, keys, (((1,), (1,)), ((), ())), preferred_element_type=jnp.float32
            ) * scale
            position = lax.broadcasted_iota(jnp.int32, scores.shape, 1)
            allowed = (position < live_ref[slot]) & (anchor_ref[group] == owner_ref[slot])
            masked = jnp.where(allowed, scores, NEG_FILL)
            old_max = max_ref[group]
            new_max = jnp.maximum(old_max, jnp.max(masked, axis=1, keepdims=True))
            weights = jnp.where(allowed, jnp.exp(masked - new_max), 0.0)
            keep = jnp.exp(old_max - new_max)
            sum_ref[group] = keep * sum_ref[group] + jnp.sum(weights, axis=1, keepdims=True)
            vector_ref[group] = keep * vector_ref[group] + jnp.dot(
                weights.astype(jnp.bfloat16), values, preferred_element_type=jnp.float32
            )
            max_ref[group] = new_max
        return carry

    lax.fori_loop(0, kv_ref.shape[0], visit, 0, unroll=4)


def slot_attention(group_here, live_here, owner_here, used_here, kv_pairs, query_groups, anchor_lanes, scale):
    groups, rows, width = query_groups.shape
    smem = pl.BlockSpec(memory_space=pltpu.SMEM)
    vmem = pl.BlockSpec(memory_space=pltpu.VMEM)
    shape = jax.ShapeDtypeStruct((groups, rows, width), jnp.float32)
    return pl.pallas_call(
        functools.partial(slot_attention_kernel, scale=scale),
        in_specs=[smem, smem, smem, smem, vmem, vmem, vmem],
        out_specs=[vmem, vmem, vmem],
        out_shape=[shape, shape, shape],
    )(group_here, live_here, owner_here, used_here, kv_pairs, query_groups, anchor_lanes)


def lookup(table, index):
    hits = index[..., None] == jnp.arange(table.shape[0], dtype=jnp.int32)
    shaped = hits.reshape(hits.shape + (1,) * (table.ndim - 1))
    return jnp.sum(jnp.where(shaped, table, jnp.zeros((), table.dtype)), axis=index.ndim)


def lineage(parents):
    steps_count, beam_count = parents.shape
    beam_ids = jnp.arange(beam_count, dtype=jnp.int32)
    line_rows = []
    anchor_rows = []
    for step_index in range(steps_count):
        current = beam_ids
        levels = [jnp.full((beam_count,), -1, jnp.int32) for level_index in range(steps_count)]
        for level_index in range(step_index, -1, -1):
            levels[level_index] = current
            current = lookup(parents[level_index], current)
        line_rows.append(jnp.stack(levels))
        anchor_rows.append(current)
    return (jnp.stack(line_rows), jnp.stack(anchor_rows))


def expert_rank(routes):
    steps_count, beam_count, pick_count = routes.shape
    onehot = (routes[..., None] == jnp.arange(EXPERTS, dtype=jnp.int32)).astype(jnp.int32)
    flat_hits = onehot.reshape(steps_count, beam_count * pick_count, EXPERTS)
    before = jnp.cumsum(flat_hits, axis=1) - flat_hits
    return jnp.sum(before * flat_hits, axis=-1).reshape(steps_count, beam_count, pick_count)


def head_total(partial_value, kv_size):
    copies = jnp.broadcast_to(partial_value[None], (kv_size,) + partial_value.shape)
    return jnp.sum(lax.all_to_all(copies, "kv", 0, 0, tiled=True), axis=0)


def combine_parts(part_one, part_two):
    max_one, sum_one, vector_one = part_one
    max_two, sum_two, vector_two = part_two
    larger = jnp.maximum(max_one, max_two)
    scale_one = jnp.exp(max_one - larger)
    scale_two = jnp.exp(max_two - larger)
    return (
        larger,
        sum_one * scale_one + sum_two * scale_two,
        vector_one * scale_one[..., None] + vector_two * scale_two[..., None],
    )


def groups_to_beams(grouped):
    shaped = grouped.reshape((GROUPS, DECODE_STEPS, BEAM_W, QUERIES_PER_KEY) + grouped.shape[2:])
    shaped = jnp.moveaxis(shaped, 1, 0)
    return shaped.reshape((DECODE_STEPS, BEAM_TOTAL, QUERIES_PER_KEY) + grouped.shape[2:])


def body(
    hidden_in,
    attn_gain,
    ffn_gain,
    query_key_value_weight,
    out_weight,
    router_weight,
    expert_in,
    expert_down,
    kv_cache,
    lengths,
    tables,
    parents,
    routes,
    kv_size,
    blk_size,
):
    count_tokens = DECODE_STEPS * BEAM_TOTAL
    width_local = hidden_in.shape[2]
    heads_local = query_key_value_weight.shape[1]
    logit_scale = 1.0 / math.sqrt(HEAD_WIDTH)
    line_beams, anchor = lineage(parents)
    flat_in = hidden_in.reshape(count_tokens, width_local).astype(jnp.float32)
    pre_attn = (flat_in * attn_gain.astype(jnp.float32)).astype(jnp.bfloat16)
    partial_proj = jnp.dot(
        pre_attn,
        query_key_value_weight.reshape(width_local, -1),
        preferred_element_type=jnp.float32,
    )
    partial_sq = jnp.sum(flat_in * flat_in, axis=1)
    proj_rows = partial_proj.reshape(-1, HEAD_WIDTH)
    sq_rows = jnp.pad(partial_sq, (0, -partial_sq.shape[0] % HEAD_WIDTH)).reshape(-1, HEAD_WIDTH)
    stacked = jnp.concatenate([proj_rows, sq_rows], axis=0)
    chunk_rows = -(-stacked.shape[0] // (8 * blk_size)) * 8
    stacked = jnp.pad(stacked, ((0, chunk_rows * blk_size - stacked.shape[0]), (0, 0)))
    owned = jnp.sum(
        lax.all_to_all(stacked.reshape(blk_size, chunk_rows, HEAD_WIDTH), "blk", 0, 0, tiled=True),
        axis=0,
    )
    summed = lax.all_to_all(
        jnp.broadcast_to(owned[None], (blk_size,) + owned.shape), "blk", 0, 0, tiled=True
    ).reshape(-1, HEAD_WIDTH)
    projected_rows = summed[: proj_rows.shape[0]].reshape(partial_proj.shape)
    square_sum = summed[proj_rows.shape[0] :].reshape(-1)[: partial_sq.shape[0]]
    projected_rows = (
        projected_rows * lax.rsqrt(square_sum / MODEL_WIDTH + NORM_FLOOR)[:, None]
    ).reshape(DECODE_STEPS, BEAM_TOTAL, heads_local, QUERIES_PER_KEY + 2, HEAD_WIDTH)
    beam_groups = jnp.arange(BEAM_TOTAL, dtype=jnp.int32) // BEAM_W
    positions = lookup(lengths, beam_groups)[None, :] + jnp.arange(DECODE_STEPS, dtype=jnp.int32)[:, None]
    queries = rotate_pairs(
        projected_rows[:, :, :, :QUERIES_PER_KEY], positions[:, :, None, None]
    ).astype(jnp.bfloat16)
    new_key = rotate_pairs(projected_rows[:, :, :, QUERIES_PER_KEY], positions[:, :, None]).astype(
        jnp.bfloat16
    )
    new_value = projected_rows[:, :, :, QUERIES_PER_KEY + 1].astype(jnp.bfloat16)
    slot_count = kv_cache.shape[0]
    slot_base = lax.axis_index("blk") * slot_count
    entry_ids = jnp.arange(BEAM_TOTAL * BEAM_BLOCKS, dtype=jnp.int32)
    slot_ids = slot_base + jnp.arange(slot_count, dtype=jnp.int32)
    slot_hits = tables.reshape(-1)[None, :] == slot_ids[:, None]
    entry_here = jnp.sum(jnp.where(slot_hits, entry_ids[None, :], 0), axis=1)
    owner_here = entry_here // BEAM_BLOCKS
    block_here = entry_here % BEAM_BLOCKS
    group_here = owner_here // BEAM_W
    anchor_groups = jnp.moveaxis(anchor.reshape(DECODE_STEPS, GROUPS, BEAM_W), 1, 0)
    anchor_query = jnp.broadcast_to(
        anchor_groups[..., None], (GROUPS, DECODE_STEPS, BEAM_W, QUERIES_PER_KEY)
    ).reshape(GROUPS, -1)
    recent_allowed = jnp.transpose(
        line_beams[:, :, :, None] == jnp.arange(BEAM_TOTAL, dtype=jnp.int32), (0, 2, 1, 3)
    ).reshape(DECODE_STEPS, BEAM_TOTAL, 1, count_tokens)
    is_first = lax.axis_index("blk") == 0
    query_head = queries[:, :, 0]
    query_groups = jnp.moveaxis(
        query_head.reshape(DECODE_STEPS, GROUPS, BEAM_W, QUERIES_PER_KEY, HEAD_WIDTH), 1, 0
    ).reshape(GROUPS, -1, HEAD_WIDTH)
    live_here = lookup(lengths, group_here) - block_here * BLOCK_POSITIONS
    query_match = lookup(anchor_query, group_here) == owner_here[:, None]
    used_here = (jnp.any(query_match, axis=1) & (live_here > 0)).astype(jnp.int32)
    anchor_lanes = jnp.broadcast_to(anchor_query[:, :, None], anchor_query.shape + (HEAD_WIDTH,))
    kv_pairs = kv_cache.reshape(slot_count, 2, BLOCK_POSITIONS, HEAD_WIDTH)
    vector_lanes, max_lanes, sum_lanes = slot_attention(
        group_here, live_here, owner_here, used_here, kv_pairs, query_groups, anchor_lanes, logit_scale
    )
    group_max = max_lanes[:, :, 0]
    group_sum = sum_lanes[:, :, 0]
    group_vector = vector_lanes
    cache_max = groups_to_beams(group_max)
    cache_sum = groups_to_beams(group_sum)
    cache_vector = groups_to_beams(group_vector)
    newest_keys = new_key[:, :, 0].reshape(count_tokens, HEAD_WIDTH)
    newest_values = new_value[:, :, 0].reshape(count_tokens, HEAD_WIDTH)
    newest_logits = (
        jnp.einsum("sbqd,kd->sbqk", query_head, newest_keys, preferred_element_type=jnp.float32)
        * logit_scale
    )
    recent_masked = jnp.where(recent_allowed, newest_logits, NEG_FILL)
    recent_max = jnp.max(recent_masked, axis=-1)
    recent_weights = jnp.where(recent_allowed, jnp.exp(recent_masked - recent_max[..., None]), 0.0)
    recent_sum = jnp.sum(recent_weights, axis=-1)
    recent_vector = jnp.einsum(
        "sbqk,kd->sbqd",
        recent_weights.astype(jnp.bfloat16),
        newest_values,
        preferred_element_type=jnp.float32,
    )
    recent_max = jnp.where(is_first, recent_max, NEG_FILL)
    recent_sum = jnp.where(is_first, recent_sum, 0.0)
    recent_vector = jnp.where(is_first, recent_vector, 0.0)
    local_max, local_sum, local_vector = combine_parts(
        (cache_max, cache_sum, cache_vector), (recent_max, recent_sum, recent_vector)
    )
    max_heads = [local_max]
    sum_heads = [local_sum]
    vector_heads = [local_vector]
    part_max = jnp.stack(max_heads, axis=2)
    part_sum = jnp.stack(sum_heads, axis=2)
    part_vector = jnp.stack(vector_heads, axis=2)
    query_rows = part_vector.reshape(-1, HEAD_WIDTH)
    row_count = query_rows.shape[0]
    packed_rows = jnp.concatenate(
        [
            query_rows,
            part_max.reshape(-1, 1),
            part_sum.reshape(-1, 1),
            jnp.zeros((row_count, HEAD_WIDTH - 2), jnp.float32),
        ],
        axis=1,
    ).reshape(blk_size, row_count // blk_size, 2 * HEAD_WIDTH)
    peer_rows = lax.all_to_all(packed_rows, "blk", 0, 0, tiled=True)
    peer_max = peer_rows[:, :, HEAD_WIDTH]
    peer_scale = jnp.exp(peer_max - jnp.max(peer_max, axis=0)[None])
    merged_sum = jnp.sum(peer_rows[:, :, HEAD_WIDTH + 1] * peer_scale, axis=0)
    merged_vector = jnp.sum(peer_rows[:, :, :HEAD_WIDTH] * peer_scale[:, :, None], axis=0)
    owned_rows = (merged_vector / merged_sum[:, None]).astype(jnp.bfloat16)
    attended_rows = lax.all_to_all(
        jnp.broadcast_to(owned_rows[None], (blk_size,) + owned_rows.shape), "blk", 0, 0, tiled=True
    ).reshape(count_tokens, -1)
    attn_partial = jnp.dot(attended_rows, out_weight, preferred_element_type=jnp.float32)
    attn_out = head_total(attn_partial, kv_size)
    residual = (flat_in + attn_out).astype(jnp.bfloat16)
    experts_local = expert_in.shape[0]
    ff_local = expert_in.shape[3]
    rows_per_expert = DECODE_STEPS * CAP
    rows_local = experts_local * rows_per_expert
    flat_routes = routes.reshape(count_tokens, 2)
    rank = expert_rank(routes).reshape(count_tokens, 2)
    step_of = jnp.arange(count_tokens, dtype=jnp.int32) // BEAM_TOTAL
    row_id = (flat_routes * rows_per_expert + step_of[:, None] * CAP + rank).reshape(-1)
    token_ids = jnp.broadcast_to(
        jnp.arange(count_tokens, dtype=jnp.int32)[:, None], (count_tokens, 2)
    ).reshape(-1)
    table_size = EXPERTS * rows_per_expert
    row_token_all = jnp.zeros((table_size,), jnp.int32).at[row_id].set(token_ids)
    row_live_all = jnp.zeros((table_size,), jnp.float32).at[row_id].set(1.0)
    row_other_all = (
        jnp.zeros((table_size,), jnp.int32).at[row_id].set(flat_routes[:, ::-1].reshape(-1))
    )
    row_start = lax.axis_index("kv") * rows_local
    row_token = lax.dynamic_slice_in_dim(row_token_all, row_start, rows_local)
    row_live = lax.dynamic_slice_in_dim(row_live_all, row_start, rows_local)
    row_other = lax.dynamic_slice_in_dim(row_other_all, row_start, rows_local)
    row_own = (row_start + jnp.arange(rows_local, dtype=jnp.int32)) // rows_per_expert
    in_flat = expert_in.reshape(experts_local, MODEL_WIDTH, 2 * ff_local)
    gain_wide = ffn_gain.astype(jnp.float32)
    full_rows = jnp.moveaxis(
        lax.all_to_all(
            jnp.broadcast_to(residual[None], (blk_size,) + residual.shape), "blk", 0, 0, tiled=True
        ),
        0,
        1,
    ).reshape(residual.shape[0], -1)
    chosen = full_rows[row_token].astype(jnp.float32)
    pre_rows = (chosen * gain_wide).astype(jnp.bfloat16)
    sums_in = jnp.einsum(
        "erd,edf->erf",
        pre_rows.reshape(experts_local, rows_per_expert, MODEL_WIDTH),
        in_flat,
        preferred_element_type=jnp.float32,
    )
    sums_router = jnp.dot(pre_rows, router_weight, preferred_element_type=jnp.float32)
    sum_sq = jnp.sum(chosen * chosen, axis=1)
    inv_rows = lax.rsqrt(sum_sq / MODEL_WIDTH + NORM_FLOOR)
    expert_act = sums_in * inv_rows.reshape(experts_local, rows_per_expert)[:, :, None]
    expert_hidden = (jax.nn.silu(expert_act[..., :ff_local]) * expert_act[..., ff_local:]).astype(
        jnp.bfloat16
    )
    down_part = jnp.einsum(
        "erf,efd->erd", expert_hidden, expert_down, preferred_element_type=jnp.float32
    ).reshape(rows_local, MODEL_WIDTH)
    expert_pieces = jnp.moveaxis(down_part.reshape(rows_local, blk_size, -1), 1, 0)
    expert_result = jnp.sum(lax.all_to_all(expert_pieces, "blk", 0, 0, tiled=True), axis=0)
    logits = sums_router * inv_rows[:, None]
    expert_ids = jnp.arange(EXPERTS, dtype=jnp.int32)
    own_logit = jnp.sum(jnp.where(row_own[:, None] == expert_ids[None, :], logits, 0.0), axis=1)
    other_logit = jnp.sum(jnp.where(row_other[:, None] == expert_ids[None, :], logits, 0.0), axis=1)
    gate_share = row_live / (1.0 + jnp.exp(other_logit - own_logit))
    weighted_values = expert_result * gate_share[:, None]
    placement = (row_token[None, :] == jnp.arange(count_tokens, dtype=jnp.int32)[:, None]).astype(
        jnp.float32
    )
    mixture_part = jnp.dot(placement, weighted_values, precision=lax.Precision.HIGHEST)
    mixture = head_total(mixture_part, kv_size)
    layer_out = (residual.astype(jnp.float32) + mixture).astype(jnp.bfloat16)
    return layer_out.reshape(DECODE_STEPS, BEAM_TOTAL, width_local)


def solution(mesh):
    placed = (
        P(None, None, "blk"),
        P("blk"),
        P(),
        P("blk", "kv", None),
        P("kv", "blk"),
        P(),
        P("kv", None, None, "blk"),
        P("kv", "blk", None),
        P("blk", None, "kv", None, None),
        P(),
        P(),
        P(),
        P(),
    )
    kv_size = mesh.shape["kv"]
    blk_size = mesh.shape["blk"]

    def sized(*arrays):
        return body(*arrays, kv_size, blk_size)

    return jax.shard_map(
        sized, mesh=mesh, in_specs=placed, out_specs=P(None, None, "blk"), check_vma=False
    )
```

```python
import functools
import math

import jax
import jax.numpy as jnp
from jax import lax
from jax.experimental import pallas as pl
from jax.experimental.pallas import tpu as pltpu
from jax.sharding import PartitionSpec as P

MODEL_WIDTH = 4096
HEAD_WIDTH = 128
QUERIES_PER_KEY = 4
EXPERTS = 8
BEAM_W = 8
GROUPS = 2
DECODE_STEPS = 4
BLOCK_POSITIONS = 128
BEAM_BLOCKS = 128
BEAM_TOTAL = 16
CAP = 6


NORM_FLOOR = 1e-05
ROPE_BASE = 1000000.0
NEG_FILL = -1e30
BLK_RADICES = (2, 4, 4)
SCATTER_RADICES = (4, 4, 2)
KV_RADICES = (2, 4)


def exchange(value, axis, size, distance):
    pairs = [(index, index ^ distance) for index in range(size)]
    return jax.tree.map(lambda part: lax.ppermute(part, axis, pairs), value)


def tree_join(parts, join):
    stride = 1
    while stride < len(parts):
        parts = [
            join(parts[place], parts[place + stride]) if place % (2 * stride) == 0 else parts[place]
            for place in range(len(parts))
        ]
        stride *= 2
    return parts[0]


def butterfly(value, axis, size, join, radices):
    distance = 1
    for radix in radices:
        parts = [value] + [
            exchange(value, axis, size, distance * offset) for offset in range(1, radix)
        ]
        value = tree_join(parts, join)
        distance *= radix
    assert distance == size
    return value


def add_parts(first, second):
    return jax.tree.map(lambda one, two: one + two, first, second)


def gather_doubling(block, axis, size, dim, radices):
    index = lax.axis_index(axis)
    distance = 1
    for radix in radices:
        place = (index // distance) % radix
        parts = [block] + [
            exchange(block, axis, size, distance * offset) for offset in range(1, radix)
        ]
        stacked = jnp.stack(parts)
        ordered = jnp.take(stacked, jnp.arange(radix, dtype=jnp.int32) ^ place, axis=0)
        block = jnp.concatenate([ordered[slot] for slot in range(radix)], dim)
        distance *= radix
    assert distance == size
    return block


def scatter_halving(value, axis, size, dim, radices):
    index = lax.axis_index(axis)
    distance = size
    for radix in radices:
        distance //= radix
        place = (index // distance) % radix
        piece = value.shape[dim] // radix
        received = [lax.dynamic_slice_in_dim(value, place * piece, piece, dim)]
        for offset in range(1, radix):
            send = lax.dynamic_slice_in_dim(value, (place ^ offset) * piece, piece, dim)
            received.append(exchange(send, axis, size, distance * offset))
        value = tree_join(received, add_parts)
    assert distance == 1
    return value


def rotate_pairs(vectors, positions):
    half_width = vectors.shape[-1] // 2
    exponents = jnp.arange(half_width, dtype=jnp.float32) * (2.0 / vectors.shape[-1])
    frequency = ROPE_BASE ** (-exponents)
    angles = positions.astype(jnp.float32)[..., None] * frequency
    cosine = jnp.cos(angles)
    sine_part = jnp.sin(angles)
    lower_half = vectors[..., :half_width]
    upper_half = vectors[..., half_width:]
    return jnp.concatenate(
        [
            lower_half * cosine - upper_half * sine_part,
            upper_half * cosine + lower_half * sine_part,
        ],
        axis=-1,
    )


def slot_attention_kernel(group_ref, live_ref, owner_ref, used_ref, kv_ref, query_ref, anchor_ref,
                          vector_ref, max_ref, sum_ref, *, scale):
    vector_ref[...] = jnp.zeros(vector_ref.shape, jnp.float32)
    max_ref[...] = jnp.full(max_ref.shape, NEG_FILL, jnp.float32)
    sum_ref[...] = jnp.zeros(sum_ref.shape, jnp.float32)

    def visit(slot, carry):
        @pl.when(used_ref[slot] > 0)
        def _():
            group = group_ref[slot]
            keys = kv_ref[slot, 0]
            values = kv_ref[slot, 1]
            queries = query_ref[group]
            scores = lax.dot_general(
                queries, keys, (((1,), (1,)), ((), ())), preferred_element_type=jnp.float32
            ) * scale
            position = lax.broadcasted_iota(jnp.int32, scores.shape, 1)
            allowed = (position < live_ref[slot]) & (anchor_ref[group] == owner_ref[slot])
            masked = jnp.where(allowed, scores, NEG_FILL)
            old_max = max_ref[group]
            new_max = jnp.maximum(old_max, jnp.max(masked, axis=1, keepdims=True))
            weights = jnp.where(allowed, jnp.exp(masked - new_max), 0.0)
            keep = jnp.exp(old_max - new_max)
            sum_ref[group] = keep * sum_ref[group] + jnp.sum(weights, axis=1, keepdims=True)
            vector_ref[group] = keep * vector_ref[group] + jnp.dot(
                weights.astype(jnp.bfloat16), values, preferred_element_type=jnp.float32
            )
            max_ref[group] = new_max
        return carry

    lax.fori_loop(0, kv_ref.shape[0], visit, 0)


def slot_attention(group_here, live_here, owner_here, used_here, kv_pairs, query_groups, anchor_lanes, scale):
    groups, rows, width = query_groups.shape
    smem = pl.BlockSpec(memory_space=pltpu.SMEM)
    vmem = pl.BlockSpec(memory_space=pltpu.VMEM)
    shape = jax.ShapeDtypeStruct((groups, rows, width), jnp.float32)
    return pl.pallas_call(
        functools.partial(slot_attention_kernel, scale=scale),
        in_specs=[smem, smem, smem, smem, vmem, vmem, vmem],
        out_specs=[vmem, vmem, vmem],
        out_shape=[shape, shape, shape],
    )(group_here, live_here, owner_here, used_here, kv_pairs, query_groups, anchor_lanes)


def lookup(table, index):
    hits = index[..., None] == jnp.arange(table.shape[0], dtype=jnp.int32)
    shaped = hits.reshape(hits.shape + (1,) * (table.ndim - 1))
    return jnp.sum(jnp.where(shaped, table, jnp.zeros((), table.dtype)), axis=index.ndim)


def lineage(parents):
    steps_count, beam_count = parents.shape
    beam_ids = jnp.arange(beam_count, dtype=jnp.int32)
    line_rows = []
    anchor_rows = []
    for step_index in range(steps_count):
        current = beam_ids
        levels = [jnp.full((beam_count,), -1, jnp.int32) for level_index in range(steps_count)]
        for level_index in range(step_index, -1, -1):
            levels[level_index] = current
            current = lookup(parents[level_index], current)
        line_rows.append(jnp.stack(levels))
        anchor_rows.append(current)
    return (jnp.stack(line_rows), jnp.stack(anchor_rows))


def expert_rank(routes):
    steps_count, beam_count, pick_count = routes.shape
    onehot = (routes[..., None] == jnp.arange(EXPERTS, dtype=jnp.int32)).astype(jnp.int32)
    flat_hits = onehot.reshape(steps_count, beam_count * pick_count, EXPERTS)
    before = jnp.cumsum(flat_hits, axis=1) - flat_hits
    return jnp.sum(before * flat_hits, axis=-1).reshape(steps_count, beam_count, pick_count)


def head_total(partial_value, kv_size):
    return butterfly(partial_value, "kv", kv_size, add_parts, KV_RADICES)


def combine_parts(part_one, part_two):
    max_one, sum_one, vector_one = part_one
    max_two, sum_two, vector_two = part_two
    larger = jnp.maximum(max_one, max_two)
    scale_one = jnp.exp(max_one - larger)
    scale_two = jnp.exp(max_two - larger)
    return (
        larger,
        sum_one * scale_one + sum_two * scale_two,
        vector_one * scale_one[..., None] + vector_two * scale_two[..., None],
    )


def groups_to_beams(grouped):
    shaped = grouped.reshape((GROUPS, DECODE_STEPS, BEAM_W, QUERIES_PER_KEY) + grouped.shape[2:])
    shaped = jnp.moveaxis(shaped, 1, 0)
    return shaped.reshape((DECODE_STEPS, BEAM_TOTAL, QUERIES_PER_KEY) + grouped.shape[2:])


def body(
    hidden_in,
    attn_gain,
    ffn_gain,
    query_key_value_weight,
    out_weight,
    router_weight,
    expert_in,
    expert_down,
    kv_cache,
    lengths,
    tables,
    parents,
    routes,
    kv_size,
    blk_size,
):
    count_tokens = DECODE_STEPS * BEAM_TOTAL
    width_local = hidden_in.shape[2]
    heads_local = query_key_value_weight.shape[1]
    logit_scale = 1.0 / math.sqrt(HEAD_WIDTH)
    line_beams, anchor = lineage(parents)
    flat_in = hidden_in.reshape(count_tokens, width_local).astype(jnp.float32)
    pre_attn = (flat_in * attn_gain.astype(jnp.float32)).astype(jnp.bfloat16)
    partial_proj = jnp.dot(
        pre_attn,
        query_key_value_weight.reshape(width_local, -1),
        preferred_element_type=jnp.float32,
    )
    partial_sq = jnp.sum(flat_in * flat_in, axis=1)
    proj_rows = partial_proj.reshape(-1, HEAD_WIDTH)
    sq_rows = jnp.pad(partial_sq, (0, -partial_sq.shape[0] % HEAD_WIDTH)).reshape(-1, HEAD_WIDTH)
    stacked = jnp.concatenate([proj_rows, sq_rows], axis=0)
    chunk_rows = -(-stacked.shape[0] // (8 * blk_size)) * 8
    stacked = jnp.pad(stacked, ((0, chunk_rows * blk_size - stacked.shape[0]), (0, 0)))
    owned = jnp.sum(
        lax.all_to_all(stacked.reshape(blk_size, chunk_rows, HEAD_WIDTH), "blk", 0, 0, tiled=True),
        axis=0,
    )
    summed = lax.all_to_all(
        jnp.broadcast_to(owned[None], (blk_size,) + owned.shape), "blk", 0, 0, tiled=True
    ).reshape(-1, HEAD_WIDTH)
    projected_rows = summed[: proj_rows.shape[0]].reshape(partial_proj.shape)
    square_sum = summed[proj_rows.shape[0] :].reshape(-1)[: partial_sq.shape[0]]
    projected_rows = (
        projected_rows * lax.rsqrt(square_sum / MODEL_WIDTH + NORM_FLOOR)[:, None]
    ).reshape(DECODE_STEPS, BEAM_TOTAL, heads_local, QUERIES_PER_KEY + 2, HEAD_WIDTH)
    beam_groups = jnp.arange(BEAM_TOTAL, dtype=jnp.int32) // BEAM_W
    positions = lookup(lengths, beam_groups)[None, :] + jnp.arange(DECODE_STEPS, dtype=jnp.int32)[:, None]
    queries = rotate_pairs(
        projected_rows[:, :, :, :QUERIES_PER_KEY], positions[:, :, None, None]
    ).astype(jnp.bfloat16)
    new_key = rotate_pairs(projected_rows[:, :, :, QUERIES_PER_KEY], positions[:, :, None]).astype(
        jnp.bfloat16
    )
    new_value = projected_rows[:, :, :, QUERIES_PER_KEY + 1].astype(jnp.bfloat16)
    slot_count = kv_cache.shape[0]
    slot_base = lax.axis_index("blk") * slot_count
    entry_ids = jnp.arange(BEAM_TOTAL * BEAM_BLOCKS, dtype=jnp.int32)
    slot_ids = slot_base + jnp.arange(slot_count, dtype=jnp.int32)
    slot_hits = tables.reshape(-1)[None, :] == slot_ids[:, None]
    entry_here = jnp.sum(jnp.where(slot_hits, entry_ids[None, :], 0), axis=1)
    owner_here = entry_here // BEAM_BLOCKS
    block_here = entry_here % BEAM_BLOCKS
    group_here = owner_here // BEAM_W
    anchor_groups = jnp.moveaxis(anchor.reshape(DECODE_STEPS, GROUPS, BEAM_W), 1, 0)
    anchor_query = jnp.broadcast_to(
        anchor_groups[..., None], (GROUPS, DECODE_STEPS, BEAM_W, QUERIES_PER_KEY)
    ).reshape(GROUPS, -1)
    recent_allowed = jnp.transpose(
        line_beams[:, :, :, None] == jnp.arange(BEAM_TOTAL, dtype=jnp.int32), (0, 2, 1, 3)
    ).reshape(DECODE_STEPS, BEAM_TOTAL, 1, count_tokens)
    is_first = lax.axis_index("blk") == 0
    query_head = queries[:, :, 0]
    query_groups = jnp.moveaxis(
        query_head.reshape(DECODE_STEPS, GROUPS, BEAM_W, QUERIES_PER_KEY, HEAD_WIDTH), 1, 0
    ).reshape(GROUPS, -1, HEAD_WIDTH)
    live_here = lookup(lengths, group_here) - block_here * BLOCK_POSITIONS
    query_match = lookup(anchor_query, group_here) == owner_here[:, None]
    used_here = (jnp.any(query_match, axis=1) & (live_here > 0)).astype(jnp.int32)
    anchor_lanes = jnp.broadcast_to(anchor_query[:, :, None], anchor_query.shape + (HEAD_WIDTH,))
    kv_pairs = kv_cache.reshape(slot_count, 2, BLOCK_POSITIONS, HEAD_WIDTH)
    vector_lanes, max_lanes, sum_lanes = slot_attention(
        group_here, live_here, owner_here, used_here, kv_pairs, query_groups, anchor_lanes, logit_scale
    )
    group_max = max_lanes[:, :, 0]
    group_sum = sum_lanes[:, :, 0]
    group_vector = vector_lanes
    cache_max = groups_to_beams(group_max)
    cache_sum = groups_to_beams(group_sum)
    cache_vector = groups_to_beams(group_vector)
    newest_keys = new_key[:, :, 0].reshape(count_tokens, HEAD_WIDTH)
    newest_values = new_value[:, :, 0].reshape(count_tokens, HEAD_WIDTH)
    newest_logits = (
        jnp.einsum("sbqd,kd->sbqk", query_head, newest_keys, preferred_element_type=jnp.float32)
        * logit_scale
    )
    recent_masked = jnp.where(recent_allowed, newest_logits, NEG_FILL)
    recent_max = jnp.max(recent_masked, axis=-1)
    recent_weights = jnp.where(recent_allowed, jnp.exp(recent_masked - recent_max[..., None]), 0.0)
    recent_sum = jnp.sum(recent_weights, axis=-1)
    recent_vector = jnp.einsum(
        "sbqk,kd->sbqd",
        recent_weights.astype(jnp.bfloat16),
        newest_values,
        preferred_element_type=jnp.float32,
    )
    recent_max = jnp.where(is_first, recent_max, NEG_FILL)
    recent_sum = jnp.where(is_first, recent_sum, 0.0)
    recent_vector = jnp.where(is_first, recent_vector, 0.0)
    local_max, local_sum, local_vector = combine_parts(
        (cache_max, cache_sum, cache_vector), (recent_max, recent_sum, recent_vector)
    )
    max_heads = [local_max]
    sum_heads = [local_sum]
    vector_heads = [local_vector]
    part_max = jnp.stack(max_heads, axis=2)
    part_sum = jnp.stack(sum_heads, axis=2)
    part_vector = jnp.stack(vector_heads, axis=2)
    query_rows = part_vector.reshape(-1, HEAD_WIDTH)
    row_count = query_rows.shape[0]
    packed_rows = jnp.concatenate(
        [
            query_rows,
            part_max.reshape(-1, 1),
            part_sum.reshape(-1, 1),
            jnp.zeros((row_count, HEAD_WIDTH - 2), jnp.float32),
        ],
        axis=1,
    ).reshape(blk_size, row_count // blk_size, 2 * HEAD_WIDTH)
    peer_rows = lax.all_to_all(packed_rows, "blk", 0, 0, tiled=True)
    peer_max = peer_rows[:, :, HEAD_WIDTH]
    peer_scale = jnp.exp(peer_max - jnp.max(peer_max, axis=0)[None])
    merged_sum = jnp.sum(peer_rows[:, :, HEAD_WIDTH + 1] * peer_scale, axis=0)
    merged_vector = jnp.sum(peer_rows[:, :, :HEAD_WIDTH] * peer_scale[:, :, None], axis=0)
    owned_rows = (merged_vector / merged_sum[:, None]).astype(jnp.bfloat16)
    attended_rows = lax.all_to_all(
        jnp.broadcast_to(owned_rows[None], (blk_size,) + owned_rows.shape), "blk", 0, 0, tiled=True
    ).reshape(count_tokens, -1)
    attn_partial = jnp.dot(attended_rows, out_weight, preferred_element_type=jnp.float32)
    attn_out = head_total(attn_partial, kv_size)
    residual = (flat_in + attn_out).astype(jnp.bfloat16)
    experts_local = expert_in.shape[0]
    ff_local = expert_in.shape[3]
    rows_per_expert = DECODE_STEPS * CAP
    rows_local = experts_local * rows_per_expert
    flat_routes = routes.reshape(count_tokens, 2)
    rank = expert_rank(routes).reshape(count_tokens, 2)
    step_of = jnp.arange(count_tokens, dtype=jnp.int32) // BEAM_TOTAL
    row_id = (flat_routes * rows_per_expert + step_of[:, None] * CAP + rank).reshape(-1)
    token_ids = jnp.broadcast_to(
        jnp.arange(count_tokens, dtype=jnp.int32)[:, None], (count_tokens, 2)
    ).reshape(-1)
    table_size = EXPERTS * rows_per_expert
    row_token_all = jnp.zeros((table_size,), jnp.int32).at[row_id].set(token_ids)
    row_live_all = jnp.zeros((table_size,), jnp.float32).at[row_id].set(1.0)
    row_other_all = (
        jnp.zeros((table_size,), jnp.int32).at[row_id].set(flat_routes[:, ::-1].reshape(-1))
    )
    row_start = lax.axis_index("kv") * rows_local
    row_token = lax.dynamic_slice_in_dim(row_token_all, row_start, rows_local)
    row_live = lax.dynamic_slice_in_dim(row_live_all, row_start, rows_local)
    row_other = lax.dynamic_slice_in_dim(row_other_all, row_start, rows_local)
    row_own = (row_start + jnp.arange(rows_local, dtype=jnp.int32)) // rows_per_expert
    in_flat = expert_in.reshape(experts_local, MODEL_WIDTH, 2 * ff_local)
    gain_wide = ffn_gain.astype(jnp.float32)
    full_rows = jnp.moveaxis(
        lax.all_to_all(
            jnp.broadcast_to(residual[None], (blk_size,) + residual.shape), "blk", 0, 0, tiled=True
        ),
        0,
        1,
    ).reshape(residual.shape[0], -1)
    chosen = full_rows[row_token].astype(jnp.float32)
    pre_rows = (chosen * gain_wide).astype(jnp.bfloat16)
    sums_in = jnp.einsum(
        "erd,edf->erf",
        pre_rows.reshape(experts_local, rows_per_expert, MODEL_WIDTH),
        in_flat,
        preferred_element_type=jnp.float32,
    )
    sums_router = jnp.dot(pre_rows, router_weight, preferred_element_type=jnp.float32)
    sum_sq = jnp.sum(chosen * chosen, axis=1)
    inv_rows = lax.rsqrt(sum_sq / MODEL_WIDTH + NORM_FLOOR)
    expert_act = sums_in * inv_rows.reshape(experts_local, rows_per_expert)[:, :, None]
    expert_hidden = (jax.nn.silu(expert_act[..., :ff_local]) * expert_act[..., ff_local:]).astype(
        jnp.bfloat16
    )
    down_part = jnp.einsum(
        "erf,efd->erd", expert_hidden, expert_down, preferred_element_type=jnp.float32
    ).reshape(rows_local, MODEL_WIDTH)
    expert_pieces = jnp.moveaxis(down_part.reshape(rows_local, blk_size, -1), 1, 0)
    expert_result = jnp.sum(lax.all_to_all(expert_pieces, "blk", 0, 0, tiled=True), axis=0)
    logits = sums_router * inv_rows[:, None]
    expert_ids = jnp.arange(EXPERTS, dtype=jnp.int32)
    own_logit = jnp.sum(jnp.where(row_own[:, None] == expert_ids[None, :], logits, 0.0), axis=1)
    other_logit = jnp.sum(jnp.where(row_other[:, None] == expert_ids[None, :], logits, 0.0), axis=1)
    gate_share = row_live / (1.0 + jnp.exp(other_logit - own_logit))
    weighted_values = expert_result * gate_share[:, None]
    placement = (row_token[None, :] == jnp.arange(count_tokens, dtype=jnp.int32)[:, None]).astype(
        jnp.float32
    )
    mixture_part = jnp.dot(placement, weighted_values, precision=lax.Precision.HIGHEST)
    mixture = head_total(mixture_part, kv_size)
    layer_out = (residual.astype(jnp.float32) + mixture).astype(jnp.bfloat16)
    return layer_out.reshape(DECODE_STEPS, BEAM_TOTAL, width_local)


def solution(mesh):
    placed = (
        P(None, None, "blk"),
        P("blk"),
        P(),
        P("blk", "kv", None),
        P("kv", "blk"),
        P(),
        P("kv", None, None, "blk"),
        P("kv", "blk", None),
        P("blk", None, "kv", None, None),
        P(),
        P(),
        P(),
        P(),
    )
    kv_size = mesh.shape["kv"]
    blk_size = mesh.shape["blk"]

    def sized(*arrays):
        return body(*arrays, kv_size, blk_size)

    return jax.shard_map(
        sized, mesh=mesh, in_specs=placed, out_specs=P(None, None, "blk"), check_vma=False
    )
```

```python
import functools
import math

import jax
import jax.numpy as jnp
from jax import lax
from jax.experimental import pallas as pl
from jax.experimental.pallas import tpu as pltpu
from jax.sharding import PartitionSpec as P

MODEL_WIDTH = 4096
HEAD_WIDTH = 128
QUERIES_PER_KEY = 4
EXPERTS = 8
BEAM_W = 8
GROUPS = 2
DECODE_STEPS = 4
BLOCK_POSITIONS = 128
BEAM_BLOCKS = 128
BEAM_TOTAL = 16
CAP = 6


NORM_FLOOR = 1e-05
ROPE_BASE = 1000000.0
NEG_FILL = -1e30
BLK_RADICES = (2, 4, 4)
SCATTER_RADICES = (4, 4, 2)
KV_RADICES = (2, 4)


def exchange(value, axis, size, distance):
    pairs = [(index, index ^ distance) for index in range(size)]
    return jax.tree.map(lambda part: lax.ppermute(part, axis, pairs), value)


def tree_join(parts, join):
    stride = 1
    while stride < len(parts):
        parts = [
            join(parts[place], parts[place + stride]) if place % (2 * stride) == 0 else parts[place]
            for place in range(len(parts))
        ]
        stride *= 2
    return parts[0]


def butterfly(value, axis, size, join, radices):
    distance = 1
    for radix in radices:
        parts = [value] + [
            exchange(value, axis, size, distance * offset) for offset in range(1, radix)
        ]
        value = tree_join(parts, join)
        distance *= radix
    assert distance == size
    return value


def add_parts(first, second):
    return jax.tree.map(lambda one, two: one + two, first, second)


def gather_doubling(block, axis, size, dim, radices):
    index = lax.axis_index(axis)
    distance = 1
    for radix in radices:
        place = (index // distance) % radix
        parts = [block] + [
            exchange(block, axis, size, distance * offset) for offset in range(1, radix)
        ]
        stacked = jnp.stack(parts)
        ordered = jnp.take(stacked, jnp.arange(radix, dtype=jnp.int32) ^ place, axis=0)
        block = jnp.concatenate([ordered[slot] for slot in range(radix)], dim)
        distance *= radix
    assert distance == size
    return block


def scatter_halving(value, axis, size, dim, radices):
    index = lax.axis_index(axis)
    distance = size
    for radix in radices:
        distance //= radix
        place = (index // distance) % radix
        piece = value.shape[dim] // radix
        received = [lax.dynamic_slice_in_dim(value, place * piece, piece, dim)]
        for offset in range(1, radix):
            send = lax.dynamic_slice_in_dim(value, (place ^ offset) * piece, piece, dim)
            received.append(exchange(send, axis, size, distance * offset))
        value = tree_join(received, add_parts)
    assert distance == 1
    return value


def rotate_pairs(vectors, positions):
    half_width = vectors.shape[-1] // 2
    exponents = jnp.arange(half_width, dtype=jnp.float32) * (2.0 / vectors.shape[-1])
    frequency = ROPE_BASE ** (-exponents)
    angles = positions.astype(jnp.float32)[..., None] * frequency
    cosine = jnp.cos(angles)
    sine_part = jnp.sin(angles)
    lower_half = vectors[..., :half_width]
    upper_half = vectors[..., half_width:]
    return jnp.concatenate(
        [
            lower_half * cosine - upper_half * sine_part,
            upper_half * cosine + lower_half * sine_part,
        ],
        axis=-1,
    )


def slot_attention_kernel(group_ref, live_ref, owner_ref, used_ref, kv_ref, query_ref, anchor_ref,
                          vector_ref, max_ref, sum_ref, *, scale):
    vector_ref[...] = jnp.zeros(vector_ref.shape, jnp.float32)
    max_ref[...] = jnp.full(max_ref.shape, NEG_FILL, jnp.float32)
    sum_ref[...] = jnp.zeros(sum_ref.shape, jnp.float32)

    def accumulate(slot, whole):
        group = group_ref[slot]
        keys = kv_ref[slot, 0]
        values = kv_ref[slot, 1]
        queries = query_ref[group]
        scores = lax.dot_general(
            queries, keys, (((1,), (1,)), ((), ())), preferred_element_type=jnp.float32
        ) * scale
        allowed = anchor_ref[group] == owner_ref[slot]
        if not whole:
            position = lax.broadcasted_iota(jnp.int32, scores.shape, 1)
            allowed = allowed & (position < live_ref[slot])
        masked = jnp.where(allowed, scores, NEG_FILL)
        old_max = max_ref[group]
        new_max = jnp.maximum(old_max, jnp.max(masked, axis=1, keepdims=True))
        weights = jnp.where(allowed, jnp.exp(masked - new_max), 0.0)
        keep = jnp.exp(old_max - new_max)
        sum_ref[group] = keep * sum_ref[group] + jnp.sum(weights, axis=1, keepdims=True)
        vector_ref[group] = keep * vector_ref[group] + jnp.dot(
            weights.astype(jnp.bfloat16), values, preferred_element_type=jnp.float32
        )
        max_ref[group] = new_max

    def visit(slot, carry):
        used = used_ref[slot] > 0
        whole = live_ref[slot] >= kv_ref.shape[2]

        @pl.when(used & whole)
        def _():
            accumulate(slot, True)

        @pl.when(used & jnp.logical_not(whole))
        def _():
            accumulate(slot, False)

        return carry

    lax.fori_loop(0, kv_ref.shape[0], visit, 0)


def slot_attention(group_here, live_here, owner_here, used_here, kv_pairs, query_groups, anchor_lanes, scale):
    groups, rows, width = query_groups.shape
    smem = pl.BlockSpec(memory_space=pltpu.SMEM)
    vmem = pl.BlockSpec(memory_space=pltpu.VMEM)
    shape = jax.ShapeDtypeStruct((groups, rows, width), jnp.float32)
    return pl.pallas_call(
        functools.partial(slot_attention_kernel, scale=scale),
        in_specs=[smem, smem, smem, smem, vmem, vmem, vmem],
        out_specs=[vmem, vmem, vmem],
        out_shape=[shape, shape, shape],
    )(group_here, live_here, owner_here, used_here, kv_pairs, query_groups, anchor_lanes)


def lookup(table, index):
    hits = index[..., None] == jnp.arange(table.shape[0], dtype=jnp.int32)
    shaped = hits.reshape(hits.shape + (1,) * (table.ndim - 1))
    return jnp.sum(jnp.where(shaped, table, jnp.zeros((), table.dtype)), axis=index.ndim)


def lineage(parents):
    steps_count, beam_count = parents.shape
    beam_ids = jnp.arange(beam_count, dtype=jnp.int32)
    line_rows = []
    anchor_rows = []
    for step_index in range(steps_count):
        current = beam_ids
        levels = [jnp.full((beam_count,), -1, jnp.int32) for level_index in range(steps_count)]
        for level_index in range(step_index, -1, -1):
            levels[level_index] = current
            current = lookup(parents[level_index], current)
        line_rows.append(jnp.stack(levels))
        anchor_rows.append(current)
    return (jnp.stack(line_rows), jnp.stack(anchor_rows))


def expert_rank(routes):
    steps_count, beam_count, pick_count = routes.shape
    onehot = (routes[..., None] == jnp.arange(EXPERTS, dtype=jnp.int32)).astype(jnp.int32)
    flat_hits = onehot.reshape(steps_count, beam_count * pick_count, EXPERTS)
    before = jnp.cumsum(flat_hits, axis=1) - flat_hits
    return jnp.sum(before * flat_hits, axis=-1).reshape(steps_count, beam_count, pick_count)


def head_total(partial_value, kv_size):
    return butterfly(partial_value, "kv", kv_size, add_parts, KV_RADICES)


def combine_parts(part_one, part_two):
    max_one, sum_one, vector_one = part_one
    max_two, sum_two, vector_two = part_two
    larger = jnp.maximum(max_one, max_two)
    scale_one = jnp.exp(max_one - larger)
    scale_two = jnp.exp(max_two - larger)
    return (
        larger,
        sum_one * scale_one + sum_two * scale_two,
        vector_one * scale_one[..., None] + vector_two * scale_two[..., None],
    )


def groups_to_beams(grouped):
    shaped = grouped.reshape((GROUPS, DECODE_STEPS, BEAM_W, QUERIES_PER_KEY) + grouped.shape[2:])
    shaped = jnp.moveaxis(shaped, 1, 0)
    return shaped.reshape((DECODE_STEPS, BEAM_TOTAL, QUERIES_PER_KEY) + grouped.shape[2:])


def body(
    hidden_in,
    attn_gain,
    ffn_gain,
    query_key_value_weight,
    out_weight,
    router_weight,
    expert_in,
    expert_down,
    kv_cache,
    lengths,
    tables,
    parents,
    routes,
    kv_size,
    blk_size,
):
    count_tokens = DECODE_STEPS * BEAM_TOTAL
    width_local = hidden_in.shape[2]
    heads_local = query_key_value_weight.shape[1]
    logit_scale = 1.0 / math.sqrt(HEAD_WIDTH)
    line_beams, anchor = lineage(parents)
    flat_in = hidden_in.reshape(count_tokens, width_local).astype(jnp.float32)
    pre_attn = (flat_in * attn_gain.astype(jnp.float32)).astype(jnp.bfloat16)
    partial_proj = jnp.dot(
        pre_attn,
        query_key_value_weight.reshape(width_local, -1),
        preferred_element_type=jnp.float32,
    )
    partial_sq = jnp.sum(flat_in * flat_in, axis=1)
    proj_rows = partial_proj.reshape(-1, HEAD_WIDTH)
    sq_rows = jnp.pad(partial_sq, (0, -partial_sq.shape[0] % HEAD_WIDTH)).reshape(-1, HEAD_WIDTH)
    stacked = jnp.concatenate([proj_rows, sq_rows], axis=0)
    chunk_rows = -(-stacked.shape[0] // (8 * blk_size)) * 8
    stacked = jnp.pad(stacked, ((0, chunk_rows * blk_size - stacked.shape[0]), (0, 0)))
    owned = jnp.sum(
        lax.all_to_all(stacked.reshape(blk_size, chunk_rows, HEAD_WIDTH), "blk", 0, 0, tiled=True),
        axis=0,
    )
    summed = lax.all_to_all(
        jnp.broadcast_to(owned[None], (blk_size,) + owned.shape), "blk", 0, 0, tiled=True
    ).reshape(-1, HEAD_WIDTH)
    projected_rows = summed[: proj_rows.shape[0]].reshape(partial_proj.shape)
    square_sum = summed[proj_rows.shape[0] :].reshape(-1)[: partial_sq.shape[0]]
    projected_rows = (
        projected_rows * lax.rsqrt(square_sum / MODEL_WIDTH + NORM_FLOOR)[:, None]
    ).reshape(DECODE_STEPS, BEAM_TOTAL, heads_local, QUERIES_PER_KEY + 2, HEAD_WIDTH)
    beam_groups = jnp.arange(BEAM_TOTAL, dtype=jnp.int32) // BEAM_W
    positions = lookup(lengths, beam_groups)[None, :] + jnp.arange(DECODE_STEPS, dtype=jnp.int32)[:, None]
    queries = rotate_pairs(
        projected_rows[:, :, :, :QUERIES_PER_KEY], positions[:, :, None, None]
    ).astype(jnp.bfloat16)
    new_key = rotate_pairs(projected_rows[:, :, :, QUERIES_PER_KEY], positions[:, :, None]).astype(
        jnp.bfloat16
    )
    new_value = projected_rows[:, :, :, QUERIES_PER_KEY + 1].astype(jnp.bfloat16)
    slot_count = kv_cache.shape[0]
    slot_base = lax.axis_index("blk") * slot_count
    entry_ids = jnp.arange(BEAM_TOTAL * BEAM_BLOCKS, dtype=jnp.int32)
    slot_ids = slot_base + jnp.arange(slot_count, dtype=jnp.int32)
    slot_hits = tables.reshape(-1)[None, :] == slot_ids[:, None]
    entry_here = jnp.sum(jnp.where(slot_hits, entry_ids[None, :], 0), axis=1)
    owner_here = entry_here // BEAM_BLOCKS
    block_here = entry_here % BEAM_BLOCKS
    group_here = owner_here // BEAM_W
    anchor_groups = jnp.moveaxis(anchor.reshape(DECODE_STEPS, GROUPS, BEAM_W), 1, 0)
    anchor_query = jnp.broadcast_to(
        anchor_groups[..., None], (GROUPS, DECODE_STEPS, BEAM_W, QUERIES_PER_KEY)
    ).reshape(GROUPS, -1)
    recent_allowed = jnp.transpose(
        line_beams[:, :, :, None] == jnp.arange(BEAM_TOTAL, dtype=jnp.int32), (0, 2, 1, 3)
    ).reshape(DECODE_STEPS, BEAM_TOTAL, 1, count_tokens)
    is_first = lax.axis_index("blk") == 0
    query_head = queries[:, :, 0]
    query_groups = jnp.moveaxis(
        query_head.reshape(DECODE_STEPS, GROUPS, BEAM_W, QUERIES_PER_KEY, HEAD_WIDTH), 1, 0
    ).reshape(GROUPS, -1, HEAD_WIDTH)
    live_here = lookup(lengths, group_here) - block_here * BLOCK_POSITIONS
    query_match = lookup(anchor_query, group_here) == owner_here[:, None]
    used_here = (jnp.any(query_match, axis=1) & (live_here > 0)).astype(jnp.int32)
    anchor_lanes = jnp.broadcast_to(anchor_query[:, :, None], anchor_query.shape + (HEAD_WIDTH,))
    kv_pairs = kv_cache.reshape(slot_count, 2, BLOCK_POSITIONS, HEAD_WIDTH)
    vector_lanes, max_lanes, sum_lanes = slot_attention(
        group_here, live_here, owner_here, used_here, kv_pairs, query_groups, anchor_lanes, logit_scale
    )
    group_max = max_lanes[:, :, 0]
    group_sum = sum_lanes[:, :, 0]
    group_vector = vector_lanes
    cache_max = groups_to_beams(group_max)
    cache_sum = groups_to_beams(group_sum)
    cache_vector = groups_to_beams(group_vector)
    newest_keys = new_key[:, :, 0].reshape(count_tokens, HEAD_WIDTH)
    newest_values = new_value[:, :, 0].reshape(count_tokens, HEAD_WIDTH)
    newest_logits = (
        jnp.einsum("sbqd,kd->sbqk", query_head, newest_keys, preferred_element_type=jnp.float32)
        * logit_scale
    )
    recent_masked = jnp.where(recent_allowed, newest_logits, NEG_FILL)
    recent_max = jnp.max(recent_masked, axis=-1)
    recent_weights = jnp.where(recent_allowed, jnp.exp(recent_masked - recent_max[..., None]), 0.0)
    recent_sum = jnp.sum(recent_weights, axis=-1)
    recent_vector = jnp.einsum(
        "sbqk,kd->sbqd",
        recent_weights.astype(jnp.bfloat16),
        newest_values,
        preferred_element_type=jnp.float32,
    )
    recent_max = jnp.where(is_first, recent_max, NEG_FILL)
    recent_sum = jnp.where(is_first, recent_sum, 0.0)
    recent_vector = jnp.where(is_first, recent_vector, 0.0)
    local_max, local_sum, local_vector = combine_parts(
        (cache_max, cache_sum, cache_vector), (recent_max, recent_sum, recent_vector)
    )
    max_heads = [local_max]
    sum_heads = [local_sum]
    vector_heads = [local_vector]
    part_max = jnp.stack(max_heads, axis=2)
    part_sum = jnp.stack(sum_heads, axis=2)
    part_vector = jnp.stack(vector_heads, axis=2)
    query_rows = part_vector.reshape(-1, HEAD_WIDTH)
    row_count = query_rows.shape[0]
    packed_rows = jnp.concatenate(
        [
            query_rows,
            part_max.reshape(-1, 1),
            part_sum.reshape(-1, 1),
            jnp.zeros((row_count, HEAD_WIDTH - 2), jnp.float32),
        ],
        axis=1,
    ).reshape(blk_size, row_count // blk_size, 2 * HEAD_WIDTH)
    peer_rows = lax.all_to_all(packed_rows, "blk", 0, 0, tiled=True)
    peer_max = peer_rows[:, :, HEAD_WIDTH]
    peer_scale = jnp.exp(peer_max - jnp.max(peer_max, axis=0)[None])
    merged_sum = jnp.sum(peer_rows[:, :, HEAD_WIDTH + 1] * peer_scale, axis=0)
    merged_vector = jnp.sum(peer_rows[:, :, :HEAD_WIDTH] * peer_scale[:, :, None], axis=0)
    owned_rows = (merged_vector / merged_sum[:, None]).astype(jnp.bfloat16)
    attended_rows = lax.all_to_all(
        jnp.broadcast_to(owned_rows[None], (blk_size,) + owned_rows.shape), "blk", 0, 0, tiled=True
    ).reshape(count_tokens, -1)
    attn_partial = jnp.dot(attended_rows, out_weight, preferred_element_type=jnp.float32)
    attn_out = head_total(attn_partial, kv_size)
    residual = (flat_in + attn_out).astype(jnp.bfloat16)
    experts_local = expert_in.shape[0]
    ff_local = expert_in.shape[3]
    rows_per_expert = DECODE_STEPS * CAP
    rows_local = experts_local * rows_per_expert
    flat_routes = routes.reshape(count_tokens, 2)
    rank = expert_rank(routes).reshape(count_tokens, 2)
    step_of = jnp.arange(count_tokens, dtype=jnp.int32) // BEAM_TOTAL
    row_id = (flat_routes * rows_per_expert + step_of[:, None] * CAP + rank).reshape(-1)
    token_ids = jnp.broadcast_to(
        jnp.arange(count_tokens, dtype=jnp.int32)[:, None], (count_tokens, 2)
    ).reshape(-1)
    table_size = EXPERTS * rows_per_expert
    row_token_all = jnp.zeros((table_size,), jnp.int32).at[row_id].set(token_ids)
    row_live_all = jnp.zeros((table_size,), jnp.float32).at[row_id].set(1.0)
    row_other_all = (
        jnp.zeros((table_size,), jnp.int32).at[row_id].set(flat_routes[:, ::-1].reshape(-1))
    )
    row_start = lax.axis_index("kv") * rows_local
    row_token = lax.dynamic_slice_in_dim(row_token_all, row_start, rows_local)
    row_live = lax.dynamic_slice_in_dim(row_live_all, row_start, rows_local)
    row_other = lax.dynamic_slice_in_dim(row_other_all, row_start, rows_local)
    row_own = (row_start + jnp.arange(rows_local, dtype=jnp.int32)) // rows_per_expert
    in_flat = expert_in.reshape(experts_local, MODEL_WIDTH, 2 * ff_local)
    gain_wide = ffn_gain.astype(jnp.float32)
    full_rows = jnp.moveaxis(
        lax.all_to_all(
            jnp.broadcast_to(residual[None], (blk_size,) + residual.shape), "blk", 0, 0, tiled=True
        ),
        0,
        1,
    ).reshape(residual.shape[0], -1)
    chosen = full_rows[row_token].astype(jnp.float32)
    pre_rows = (chosen * gain_wide).astype(jnp.bfloat16)
    sums_in = jnp.einsum(
        "erd,edf->erf",
        pre_rows.reshape(experts_local, rows_per_expert, MODEL_WIDTH),
        in_flat,
        preferred_element_type=jnp.float32,
    )
    sums_router = jnp.dot(pre_rows, router_weight, preferred_element_type=jnp.float32)
    sum_sq = jnp.sum(chosen * chosen, axis=1)
    inv_rows = lax.rsqrt(sum_sq / MODEL_WIDTH + NORM_FLOOR)
    expert_act = sums_in * inv_rows.reshape(experts_local, rows_per_expert)[:, :, None]
    expert_hidden = (jax.nn.silu(expert_act[..., :ff_local]) * expert_act[..., ff_local:]).astype(
        jnp.bfloat16
    )
    down_part = jnp.einsum(
        "erf,efd->erd", expert_hidden, expert_down, preferred_element_type=jnp.float32
    ).reshape(rows_local, MODEL_WIDTH)
    expert_pieces = jnp.moveaxis(down_part.reshape(rows_local, blk_size, -1), 1, 0)
    expert_result = jnp.sum(lax.all_to_all(expert_pieces, "blk", 0, 0, tiled=True), axis=0)
    logits = sums_router * inv_rows[:, None]
    expert_ids = jnp.arange(EXPERTS, dtype=jnp.int32)
    own_logit = jnp.sum(jnp.where(row_own[:, None] == expert_ids[None, :], logits, 0.0), axis=1)
    other_logit = jnp.sum(jnp.where(row_other[:, None] == expert_ids[None, :], logits, 0.0), axis=1)
    gate_share = row_live / (1.0 + jnp.exp(other_logit - own_logit))
    weighted_values = expert_result * gate_share[:, None]
    placement = (row_token[None, :] == jnp.arange(count_tokens, dtype=jnp.int32)[:, None]).astype(
        jnp.float32
    )
    mixture_part = jnp.dot(placement, weighted_values, precision=lax.Precision.HIGHEST)
    mixture = head_total(mixture_part, kv_size)
    layer_out = (residual.astype(jnp.float32) + mixture).astype(jnp.bfloat16)
    return layer_out.reshape(DECODE_STEPS, BEAM_TOTAL, width_local)


def solution(mesh):
    placed = (
        P(None, None, "blk"),
        P("blk"),
        P(),
        P("blk", "kv", None),
        P("kv", "blk"),
        P(),
        P("kv", None, None, "blk"),
        P("kv", "blk", None),
        P("blk", None, "kv", None, None),
        P(),
        P(),
        P(),
        P(),
    )
    kv_size = mesh.shape["kv"]
    blk_size = mesh.shape["blk"]

    def sized(*arrays):
        return body(*arrays, kv_size, blk_size)

    return jax.shard_map(
        sized, mesh=mesh, in_specs=placed, out_specs=P(None, None, "blk"), check_vma=False
    )
```

```python
import functools
import math

import jax
import jax.numpy as jnp
from jax import lax
from jax.experimental import pallas as pl
from jax.experimental.pallas import tpu as pltpu
from jax.sharding import PartitionSpec as P

MODEL_WIDTH = 4096
HEAD_WIDTH = 128
QUERIES_PER_KEY = 4
EXPERTS = 8
BEAM_W = 8
GROUPS = 2
DECODE_STEPS = 4
BLOCK_POSITIONS = 128
BEAM_BLOCKS = 128
BEAM_TOTAL = 16
CAP = 6


NORM_FLOOR = 1e-05
ROPE_BASE = 1000000.0
NEG_FILL = -1e30
BLK_RADICES = (2, 4, 4)
SCATTER_RADICES = (4, 4, 2)
KV_RADICES = (2, 4)


def exchange(value, axis, size, distance):
    pairs = [(index, index ^ distance) for index in range(size)]
    return jax.tree.map(lambda part: lax.ppermute(part, axis, pairs), value)


def tree_join(parts, join):
    stride = 1
    while stride < len(parts):
        parts = [
            join(parts[place], parts[place + stride]) if place % (2 * stride) == 0 else parts[place]
            for place in range(len(parts))
        ]
        stride *= 2
    return parts[0]


def butterfly(value, axis, size, join, radices):
    distance = 1
    for radix in radices:
        parts = [value] + [
            exchange(value, axis, size, distance * offset) for offset in range(1, radix)
        ]
        value = tree_join(parts, join)
        distance *= radix
    assert distance == size
    return value


def add_parts(first, second):
    return jax.tree.map(lambda one, two: one + two, first, second)


def gather_doubling(block, axis, size, dim, radices):
    index = lax.axis_index(axis)
    distance = 1
    for radix in radices:
        place = (index // distance) % radix
        parts = [block] + [
            exchange(block, axis, size, distance * offset) for offset in range(1, radix)
        ]
        stacked = jnp.stack(parts)
        ordered = jnp.take(stacked, jnp.arange(radix, dtype=jnp.int32) ^ place, axis=0)
        block = jnp.concatenate([ordered[slot] for slot in range(radix)], dim)
        distance *= radix
    assert distance == size
    return block


def scatter_halving(value, axis, size, dim, radices):
    index = lax.axis_index(axis)
    distance = size
    for radix in radices:
        distance //= radix
        place = (index // distance) % radix
        piece = value.shape[dim] // radix
        received = [lax.dynamic_slice_in_dim(value, place * piece, piece, dim)]
        for offset in range(1, radix):
            send = lax.dynamic_slice_in_dim(value, (place ^ offset) * piece, piece, dim)
            received.append(exchange(send, axis, size, distance * offset))
        value = tree_join(received, add_parts)
    assert distance == 1
    return value


def rotate_pairs(vectors, positions):
    half_width = vectors.shape[-1] // 2
    exponents = jnp.arange(half_width, dtype=jnp.float32) * (2.0 / vectors.shape[-1])
    frequency = ROPE_BASE ** (-exponents)
    angles = positions.astype(jnp.float32)[..., None] * frequency
    cosine = jnp.cos(angles)
    sine_part = jnp.sin(angles)
    lower_half = vectors[..., :half_width]
    upper_half = vectors[..., half_width:]
    return jnp.concatenate(
        [
            lower_half * cosine - upper_half * sine_part,
            upper_half * cosine + lower_half * sine_part,
        ],
        axis=-1,
    )


def slot_attention_kernel(group_ref, live_ref, owner_ref, used_ref, kv_ref, query_ref, anchor_ref,
                          vector_ref, max_ref, sum_ref, *, scale):
    vector_ref[...] = jnp.zeros(vector_ref.shape, jnp.float32)
    max_ref[...] = jnp.full(max_ref.shape, NEG_FILL, jnp.float32)
    sum_ref[...] = jnp.zeros(sum_ref.shape, jnp.float32)

    def accumulate(slot, whole):
        group = group_ref[slot]
        keys = kv_ref[slot, 0]
        values = kv_ref[slot, 1]
        queries = query_ref[group]
        scores = lax.dot_general(
            queries, keys, (((1,), (1,)), ((), ())), preferred_element_type=jnp.float32
        ) * scale
        allowed = anchor_ref[group] == owner_ref[slot]
        if not whole:
            position = lax.broadcasted_iota(jnp.int32, scores.shape, 1)
            allowed = allowed & (position < live_ref[slot])
        masked = jnp.where(allowed, scores, NEG_FILL)
        old_max = max_ref[group]
        new_max = jnp.maximum(old_max, jnp.max(masked, axis=1, keepdims=True))
        weights = jnp.where(allowed, jnp.exp(masked - new_max), 0.0)
        keep = jnp.exp(old_max - new_max)
        sum_ref[group] = keep * sum_ref[group] + jnp.sum(weights, axis=1, keepdims=True)
        vector_ref[group] = keep * vector_ref[group] + jnp.dot(
            weights.astype(jnp.bfloat16), values, preferred_element_type=jnp.float32
        )
        max_ref[group] = new_max

    def visit(slot, carry):
        used = used_ref[slot] > 0
        whole = live_ref[slot] >= kv_ref.shape[2]

        @pl.when(used & whole)
        def _():
            accumulate(slot, True)

        @pl.when(used & jnp.logical_not(whole))
        def _():
            accumulate(slot, False)

        return carry

    lax.fori_loop(0, kv_ref.shape[0], visit, 0)


def slot_attention(group_here, live_here, owner_here, used_here, kv_pairs, query_groups, anchor_lanes, scale):
    groups, rows, width = query_groups.shape
    smem = pl.BlockSpec(memory_space=pltpu.SMEM)
    vmem = pl.BlockSpec(memory_space=pltpu.VMEM)
    shape = jax.ShapeDtypeStruct((groups, rows, width), jnp.float32)
    return pl.pallas_call(
        functools.partial(slot_attention_kernel, scale=scale),
        in_specs=[smem, smem, smem, smem, vmem, vmem, vmem],
        out_specs=[vmem, vmem, vmem],
        out_shape=[shape, shape, shape],
    )(group_here, live_here, owner_here, used_here, kv_pairs, query_groups, anchor_lanes)


def lookup(table, index):
    hits = index[..., None] == jnp.arange(table.shape[0], dtype=jnp.int32)
    shaped = hits.reshape(hits.shape + (1,) * (table.ndim - 1))
    return jnp.sum(jnp.where(shaped, table, jnp.zeros((), table.dtype)), axis=index.ndim)


def lineage(parents):
    steps_count, beam_count = parents.shape
    beam_ids = jnp.arange(beam_count, dtype=jnp.int32)
    line_rows = []
    anchor_rows = []
    for step_index in range(steps_count):
        current = beam_ids
        levels = [jnp.full((beam_count,), -1, jnp.int32) for level_index in range(steps_count)]
        for level_index in range(step_index, -1, -1):
            levels[level_index] = current
            current = lookup(parents[level_index], current)
        line_rows.append(jnp.stack(levels))
        anchor_rows.append(current)
    return (jnp.stack(line_rows), jnp.stack(anchor_rows))


def expert_rank(routes):
    steps_count, beam_count, pick_count = routes.shape
    onehot = (routes[..., None] == jnp.arange(EXPERTS, dtype=jnp.int32)).astype(jnp.int32)
    flat_hits = onehot.reshape(steps_count, beam_count * pick_count, EXPERTS)
    before = jnp.cumsum(flat_hits, axis=1) - flat_hits
    return jnp.sum(before * flat_hits, axis=-1).reshape(steps_count, beam_count, pick_count)


def head_total(partial_value, kv_size):
    return butterfly(partial_value, "kv", kv_size, add_parts, KV_RADICES)


def combine_parts(part_one, part_two):
    max_one, sum_one, vector_one = part_one
    max_two, sum_two, vector_two = part_two
    larger = jnp.maximum(max_one, max_two)
    scale_one = jnp.exp(max_one - larger)
    scale_two = jnp.exp(max_two - larger)
    return (
        larger,
        sum_one * scale_one + sum_two * scale_two,
        vector_one * scale_one[..., None] + vector_two * scale_two[..., None],
    )


def groups_to_beams(grouped):
    shaped = grouped.reshape((GROUPS, DECODE_STEPS, BEAM_W, QUERIES_PER_KEY) + grouped.shape[2:])
    shaped = jnp.moveaxis(shaped, 1, 0)
    return shaped.reshape((DECODE_STEPS, BEAM_TOTAL, QUERIES_PER_KEY) + grouped.shape[2:])


def body(
    hidden_in,
    attn_gain,
    ffn_gain,
    query_key_value_weight,
    out_weight,
    router_weight,
    expert_in,
    expert_down,
    kv_cache,
    lengths,
    tables,
    parents,
    routes,
    kv_size,
    blk_size,
):
    count_tokens = DECODE_STEPS * BEAM_TOTAL
    width_local = hidden_in.shape[2]
    heads_local = query_key_value_weight.shape[1]
    logit_scale = 1.0 / math.sqrt(HEAD_WIDTH)
    line_beams, anchor = lineage(parents)
    flat_in = hidden_in.reshape(count_tokens, width_local).astype(jnp.float32)
    pre_attn = (flat_in * attn_gain.astype(jnp.float32)).astype(jnp.bfloat16)
    partial_proj = jnp.dot(
        pre_attn,
        query_key_value_weight.reshape(width_local, -1),
        preferred_element_type=jnp.float32,
    )
    partial_sq = jnp.sum(flat_in * flat_in, axis=1)
    proj_rows = partial_proj.reshape(-1, HEAD_WIDTH)
    sq_rows = jnp.pad(partial_sq, (0, -partial_sq.shape[0] % HEAD_WIDTH)).reshape(-1, HEAD_WIDTH)
    stacked = jnp.concatenate([proj_rows, sq_rows], axis=0)
    chunk_rows = -(-stacked.shape[0] // (8 * blk_size)) * 8
    stacked = jnp.pad(stacked, ((0, chunk_rows * blk_size - stacked.shape[0]), (0, 0)))
    owned = jnp.sum(
        lax.all_to_all(stacked.reshape(blk_size, chunk_rows, HEAD_WIDTH), "blk", 0, 0, tiled=True),
        axis=0,
    )
    summed = lax.all_to_all(
        jnp.broadcast_to(owned[None], (blk_size,) + owned.shape), "blk", 0, 0, tiled=True
    ).reshape(-1, HEAD_WIDTH)
    projected_rows = summed[: proj_rows.shape[0]].reshape(partial_proj.shape)
    square_sum = summed[proj_rows.shape[0] :].reshape(-1)[: partial_sq.shape[0]]
    projected_rows = (
        projected_rows * lax.rsqrt(square_sum / MODEL_WIDTH + NORM_FLOOR)[:, None]
    ).reshape(DECODE_STEPS, BEAM_TOTAL, heads_local, QUERIES_PER_KEY + 2, HEAD_WIDTH)
    beam_groups = jnp.arange(BEAM_TOTAL, dtype=jnp.int32) // BEAM_W
    positions = lookup(lengths, beam_groups)[None, :] + jnp.arange(DECODE_STEPS, dtype=jnp.int32)[:, None]
    queries = rotate_pairs(
        projected_rows[:, :, :, :QUERIES_PER_KEY], positions[:, :, None, None]
    ).astype(jnp.bfloat16)
    new_key = rotate_pairs(projected_rows[:, :, :, QUERIES_PER_KEY], positions[:, :, None]).astype(
        jnp.bfloat16
    )
    new_value = projected_rows[:, :, :, QUERIES_PER_KEY + 1].astype(jnp.bfloat16)
    slot_count = kv_cache.shape[0]
    slot_base = lax.axis_index("blk") * slot_count
    entry_ids = jnp.arange(BEAM_TOTAL * BEAM_BLOCKS, dtype=jnp.int32)
    slot_ids = slot_base + jnp.arange(slot_count, dtype=jnp.int32)
    slot_hits = tables.reshape(-1)[None, :] == slot_ids[:, None]
    entry_here = jnp.sum(jnp.where(slot_hits, entry_ids[None, :], 0), axis=1)
    owner_here = entry_here // BEAM_BLOCKS
    block_here = entry_here % BEAM_BLOCKS
    group_here = owner_here // BEAM_W
    anchor_groups = jnp.moveaxis(anchor.reshape(DECODE_STEPS, GROUPS, BEAM_W), 1, 0)
    anchor_query = jnp.broadcast_to(
        anchor_groups[..., None], (GROUPS, DECODE_STEPS, BEAM_W, QUERIES_PER_KEY)
    ).reshape(GROUPS, -1)
    recent_allowed = jnp.transpose(
        line_beams[:, :, :, None] == jnp.arange(BEAM_TOTAL, dtype=jnp.int32), (0, 2, 1, 3)
    ).reshape(DECODE_STEPS, BEAM_TOTAL, 1, count_tokens)
    is_first = lax.axis_index("blk") == 0
    query_head = queries[:, :, 0]
    query_groups = jnp.moveaxis(
        query_head.reshape(DECODE_STEPS, GROUPS, BEAM_W, QUERIES_PER_KEY, HEAD_WIDTH), 1, 0
    ).reshape(GROUPS, -1, HEAD_WIDTH)
    live_here = lookup(lengths, group_here) - block_here * BLOCK_POSITIONS
    query_match = lookup(anchor_query, group_here) == owner_here[:, None]
    used_here = (jnp.any(query_match, axis=1) & (live_here > 0)).astype(jnp.int32)
    anchor_lanes = jnp.broadcast_to(anchor_query[:, :, None], anchor_query.shape + (HEAD_WIDTH,))
    kv_pairs = kv_cache.reshape(slot_count, 2, BLOCK_POSITIONS, HEAD_WIDTH)
    vector_lanes, max_lanes, sum_lanes = slot_attention(
        group_here, live_here, owner_here, used_here, kv_pairs, query_groups, anchor_lanes, logit_scale
    )
    group_max = max_lanes[:, :, 0]
    group_sum = sum_lanes[:, :, 0]
    group_vector = vector_lanes
    cache_max = groups_to_beams(group_max)
    cache_sum = groups_to_beams(group_sum)
    cache_vector = groups_to_beams(group_vector)
    newest_keys = new_key[:, :, 0].reshape(count_tokens, HEAD_WIDTH)
    newest_values = new_value[:, :, 0].reshape(count_tokens, HEAD_WIDTH)
    newest_logits = (
        jnp.einsum("sbqd,kd->sbqk", query_head, newest_keys, preferred_element_type=jnp.float32)
        * logit_scale
    )
    recent_masked = jnp.where(recent_allowed, newest_logits, NEG_FILL)
    recent_max = jnp.max(recent_masked, axis=-1)
    recent_weights = jnp.where(recent_allowed, jnp.exp(recent_masked - recent_max[..., None]), 0.0)
    recent_sum = jnp.sum(recent_weights, axis=-1)
    recent_vector = jnp.einsum(
        "sbqk,kd->sbqd",
        recent_weights.astype(jnp.bfloat16),
        newest_values,
        preferred_element_type=jnp.float32,
    )
    recent_max = jnp.where(is_first, recent_max, NEG_FILL)
    recent_sum = jnp.where(is_first, recent_sum, 0.0)
    recent_vector = jnp.where(is_first, recent_vector, 0.0)
    local_max, local_sum, local_vector = combine_parts(
        (cache_max, cache_sum, cache_vector), (recent_max, recent_sum, recent_vector)
    )
    max_heads = [local_max]
    sum_heads = [local_sum]
    vector_heads = [local_vector]
    part_max = jnp.stack(max_heads, axis=2)
    part_sum = jnp.stack(sum_heads, axis=2)
    part_vector = jnp.stack(vector_heads, axis=2)
    part_shape = part_max.shape
    vector_rows = part_vector.reshape(-1, HEAD_WIDTH)
    stat_rows = jnp.stack([part_max.reshape(-1), part_sum.reshape(-1)]).reshape(-1, HEAD_WIDTH)

    def packed_combine(first, second):
        def unpack(packed):
            stats = packed[vector_rows.shape[0] :].reshape(2, -1)
            return stats[0], stats[1], packed[: vector_rows.shape[0]]

        larger, total, vector = combine_parts(unpack(first), unpack(second))
        stats = jnp.stack([larger, total]).reshape(-1, HEAD_WIDTH)
        return jnp.concatenate([vector, stats], axis=0)

    whole_packed = butterfly(
        jnp.concatenate([vector_rows, stat_rows], axis=0), "blk", blk_size, packed_combine, BLK_RADICES
    )
    whole_vector = whole_packed[: vector_rows.shape[0]].reshape(part_vector.shape)
    whole_sum = whole_packed[vector_rows.shape[0] :].reshape(2, -1)[1].reshape(part_shape)
    attended_rows = (
        (whole_vector / whole_sum[..., None]).astype(jnp.bfloat16).reshape(count_tokens, -1)
    )
    attn_partial = jnp.dot(attended_rows, out_weight, preferred_element_type=jnp.float32)
    attn_out = head_total(attn_partial, kv_size)
    residual = (flat_in + attn_out).astype(jnp.bfloat16)
    experts_local = expert_in.shape[0]
    ff_local = expert_in.shape[3]
    rows_per_expert = DECODE_STEPS * CAP
    rows_local = experts_local * rows_per_expert
    flat_routes = routes.reshape(count_tokens, 2)
    rank = expert_rank(routes).reshape(count_tokens, 2)
    step_of = jnp.arange(count_tokens, dtype=jnp.int32) // BEAM_TOTAL
    row_id = (flat_routes * rows_per_expert + step_of[:, None] * CAP + rank).reshape(-1)
    token_ids = jnp.broadcast_to(
        jnp.arange(count_tokens, dtype=jnp.int32)[:, None], (count_tokens, 2)
    ).reshape(-1)
    table_size = EXPERTS * rows_per_expert
    row_token_all = jnp.zeros((table_size,), jnp.int32).at[row_id].set(token_ids)
    row_live_all = jnp.zeros((table_size,), jnp.float32).at[row_id].set(1.0)
    row_other_all = (
        jnp.zeros((table_size,), jnp.int32).at[row_id].set(flat_routes[:, ::-1].reshape(-1))
    )
    row_start = lax.axis_index("kv") * rows_local
    row_token = lax.dynamic_slice_in_dim(row_token_all, row_start, rows_local)
    row_live = lax.dynamic_slice_in_dim(row_live_all, row_start, rows_local)
    row_other = lax.dynamic_slice_in_dim(row_other_all, row_start, rows_local)
    row_own = (row_start + jnp.arange(rows_local, dtype=jnp.int32)) // rows_per_expert
    in_flat = expert_in.reshape(experts_local, MODEL_WIDTH, 2 * ff_local)
    gain_wide = ffn_gain.astype(jnp.float32)
    full_rows = jnp.moveaxis(
        lax.all_to_all(
            jnp.broadcast_to(residual[None], (blk_size,) + residual.shape), "blk", 0, 0, tiled=True
        ),
        0,
        1,
    ).reshape(residual.shape[0], -1)
    chosen = full_rows[row_token].astype(jnp.float32)
    pre_rows = (chosen * gain_wide).astype(jnp.bfloat16)
    sums_in = jnp.einsum(
        "erd,edf->erf",
        pre_rows.reshape(experts_local, rows_per_expert, MODEL_WIDTH),
        in_flat,
        preferred_element_type=jnp.float32,
    )
    sums_router = jnp.dot(pre_rows, router_weight, preferred_element_type=jnp.float32)
    sum_sq = jnp.sum(chosen * chosen, axis=1)
    inv_rows = lax.rsqrt(sum_sq / MODEL_WIDTH + NORM_FLOOR)
    expert_act = sums_in * inv_rows.reshape(experts_local, rows_per_expert)[:, :, None]
    expert_hidden = (jax.nn.silu(expert_act[..., :ff_local]) * expert_act[..., ff_local:]).astype(
        jnp.bfloat16
    )
    down_part = jnp.einsum(
        "erf,efd->erd", expert_hidden, expert_down, preferred_element_type=jnp.float32
    ).reshape(rows_local, MODEL_WIDTH)
    expert_pieces = jnp.moveaxis(down_part.reshape(rows_local, blk_size, -1), 1, 0)
    expert_result = jnp.sum(lax.all_to_all(expert_pieces, "blk", 0, 0, tiled=True), axis=0)
    logits = sums_router * inv_rows[:, None]
    expert_ids = jnp.arange(EXPERTS, dtype=jnp.int32)
    own_logit = jnp.sum(jnp.where(row_own[:, None] == expert_ids[None, :], logits, 0.0), axis=1)
    other_logit = jnp.sum(jnp.where(row_other[:, None] == expert_ids[None, :], logits, 0.0), axis=1)
    gate_share = row_live / (1.0 + jnp.exp(other_logit - own_logit))
    weighted_values = expert_result * gate_share[:, None]
    placement = (row_token[None, :] == jnp.arange(count_tokens, dtype=jnp.int32)[:, None]).astype(
        jnp.float32
    )
    mixture_part = jnp.dot(placement, weighted_values, precision=lax.Precision.HIGHEST)
    mixture = head_total(mixture_part, kv_size)
    layer_out = (residual.astype(jnp.float32) + mixture).astype(jnp.bfloat16)
    return layer_out.reshape(DECODE_STEPS, BEAM_TOTAL, width_local)


def solution(mesh):
    placed = (
        P(None, None, "blk"),
        P("blk"),
        P(),
        P("blk", "kv", None),
        P("kv", "blk"),
        P(),
        P("kv", None, None, "blk"),
        P("kv", "blk", None),
        P("blk", None, "kv", None, None),
        P(),
        P(),
        P(),
        P(),
    )
    kv_size = mesh.shape["kv"]
    blk_size = mesh.shape["blk"]

    def sized(*arrays):
        return body(*arrays, kv_size, blk_size)

    return jax.shard_map(
        sized, mesh=mesh, in_specs=placed, out_specs=P(None, None, "blk"), check_vma=False
    )
```

```python
import functools
import math

import jax
import jax.numpy as jnp
from jax import lax
from jax.experimental import pallas as pl
from jax.experimental.pallas import tpu as pltpu
from jax.sharding import PartitionSpec as P

MODEL_WIDTH = 4096
HEAD_WIDTH = 128
QUERIES_PER_KEY = 4
EXPERTS = 8
BEAM_W = 8
GROUPS = 2
DECODE_STEPS = 4
BLOCK_POSITIONS = 128
BEAM_BLOCKS = 128
BEAM_TOTAL = 16
CAP = 6


NORM_FLOOR = 1e-05
ROPE_BASE = 1000000.0
NEG_FILL = -1e30
BLK_RADICES = (2, 4, 4)
SCATTER_RADICES = (4, 4, 2)
KV_RADICES = (4, 2)


def exchange(value, axis, size, distance):
    pairs = [(index, index ^ distance) for index in range(size)]
    return jax.tree.map(lambda part: lax.ppermute(part, axis, pairs), value)


def tree_join(parts, join):
    stride = 1
    while stride < len(parts):
        parts = [
            join(parts[place], parts[place + stride]) if place % (2 * stride) == 0 else parts[place]
            for place in range(len(parts))
        ]
        stride *= 2
    return parts[0]


def butterfly(value, axis, size, join, radices):
    distance = 1
    for radix in radices:
        parts = [value] + [
            exchange(value, axis, size, distance * offset) for offset in range(1, radix)
        ]
        value = tree_join(parts, join)
        distance *= radix
    assert distance == size
    return value


def add_parts(first, second):
    return jax.tree.map(lambda one, two: one + two, first, second)


def gather_doubling(block, axis, size, dim, radices):
    index = lax.axis_index(axis)
    distance = 1
    for radix in radices:
        place = (index // distance) % radix
        parts = [block] + [
            exchange(block, axis, size, distance * offset) for offset in range(1, radix)
        ]
        stacked = jnp.stack(parts)
        ordered = jnp.take(stacked, jnp.arange(radix, dtype=jnp.int32) ^ place, axis=0)
        block = jnp.concatenate([ordered[slot] for slot in range(radix)], dim)
        distance *= radix
    assert distance == size
    return block


def scatter_halving(value, axis, size, dim, radices):
    index = lax.axis_index(axis)
    distance = size
    for radix in radices:
        distance //= radix
        place = (index // distance) % radix
        piece = value.shape[dim] // radix
        received = [lax.dynamic_slice_in_dim(value, place * piece, piece, dim)]
        for offset in range(1, radix):
            send = lax.dynamic_slice_in_dim(value, (place ^ offset) * piece, piece, dim)
            received.append(exchange(send, axis, size, distance * offset))
        value = tree_join(received, add_parts)
    assert distance == 1
    return value


def rotate_pairs(vectors, positions):
    half_width = vectors.shape[-1] // 2
    exponents = jnp.arange(half_width, dtype=jnp.float32) * (2.0 / vectors.shape[-1])
    frequency = ROPE_BASE ** (-exponents)
    angles = positions.astype(jnp.float32)[..., None] * frequency
    cosine = jnp.cos(angles)
    sine_part = jnp.sin(angles)
    lower_half = vectors[..., :half_width]
    upper_half = vectors[..., half_width:]
    return jnp.concatenate(
        [
            lower_half * cosine - upper_half * sine_part,
            upper_half * cosine + lower_half * sine_part,
        ],
        axis=-1,
    )


def slot_attention_kernel(group_ref, live_ref, owner_ref, used_ref, kv_ref, query_ref, anchor_ref,
                          vector_ref, max_ref, sum_ref, *, scale):
    vector_ref[...] = jnp.zeros(vector_ref.shape, jnp.float32)
    max_ref[...] = jnp.full(max_ref.shape, NEG_FILL, jnp.float32)
    sum_ref[...] = jnp.zeros(sum_ref.shape, jnp.float32)

    def accumulate(slot, whole):
        group = group_ref[slot]
        keys = kv_ref[slot, 0]
        values = kv_ref[slot, 1]
        queries = query_ref[group]
        scores = lax.dot_general(
            queries, keys, (((1,), (1,)), ((), ())), preferred_element_type=jnp.float32
        ) * scale
        allowed = anchor_ref[group] == owner_ref[slot]
        if not whole:
            position = lax.broadcasted_iota(jnp.int32, scores.shape, 1)
            allowed = allowed & (position < live_ref[slot])
        masked = jnp.where(allowed, scores, NEG_FILL)
        old_max = max_ref[group]
        new_max = jnp.maximum(old_max, jnp.max(masked, axis=1, keepdims=True))
        weights = jnp.where(allowed, jnp.exp(masked - new_max), 0.0)
        keep = jnp.exp(old_max - new_max)
        sum_ref[group] = keep * sum_ref[group] + jnp.sum(weights, axis=1, keepdims=True)
        vector_ref[group] = keep * vector_ref[group] + jnp.dot(
            weights.astype(jnp.bfloat16), values, preferred_element_type=jnp.float32
        )
        max_ref[group] = new_max

    def visit(slot, carry):
        used = used_ref[slot] > 0
        whole = live_ref[slot] >= kv_ref.shape[2]

        @pl.when(used & whole)
        def _():
            accumulate(slot, True)

        @pl.when(used & jnp.logical_not(whole))
        def _():
            accumulate(slot, False)

        return carry

    lax.fori_loop(0, kv_ref.shape[0], visit, 0)


def slot_attention(group_here, live_here, owner_here, used_here, kv_pairs, query_groups, anchor_lanes, scale):
    groups, rows, width = query_groups.shape
    smem = pl.BlockSpec(memory_space=pltpu.SMEM)
    vmem = pl.BlockSpec(memory_space=pltpu.VMEM)
    shape = jax.ShapeDtypeStruct((groups, rows, width), jnp.float32)
    return pl.pallas_call(
        functools.partial(slot_attention_kernel, scale=scale),
        in_specs=[smem, smem, smem, smem, vmem, vmem, vmem],
        out_specs=[vmem, vmem, vmem],
        out_shape=[shape, shape, shape],
    )(group_here, live_here, owner_here, used_here, kv_pairs, query_groups, anchor_lanes)


def lookup(table, index):
    hits = index[..., None] == jnp.arange(table.shape[0], dtype=jnp.int32)
    shaped = hits.reshape(hits.shape + (1,) * (table.ndim - 1))
    return jnp.sum(jnp.where(shaped, table, jnp.zeros((), table.dtype)), axis=index.ndim)


def lineage(parents):
    steps_count, beam_count = parents.shape
    beam_ids = jnp.arange(beam_count, dtype=jnp.int32)
    line_rows = []
    anchor_rows = []
    for step_index in range(steps_count):
        current = beam_ids
        levels = [jnp.full((beam_count,), -1, jnp.int32) for level_index in range(steps_count)]
        for level_index in range(step_index, -1, -1):
            levels[level_index] = current
            current = lookup(parents[level_index], current)
        line_rows.append(jnp.stack(levels))
        anchor_rows.append(current)
    return (jnp.stack(line_rows), jnp.stack(anchor_rows))


def expert_rank(routes):
    steps_count, beam_count, pick_count = routes.shape
    onehot = (routes[..., None] == jnp.arange(EXPERTS, dtype=jnp.int32)).astype(jnp.int32)
    flat_hits = onehot.reshape(steps_count, beam_count * pick_count, EXPERTS)
    before = jnp.cumsum(flat_hits, axis=1) - flat_hits
    return jnp.sum(before * flat_hits, axis=-1).reshape(steps_count, beam_count, pick_count)


def head_total(partial_value, kv_size):
    return butterfly(partial_value, "kv", kv_size, add_parts, KV_RADICES)


def combine_parts(part_one, part_two):
    max_one, sum_one, vector_one = part_one
    max_two, sum_two, vector_two = part_two
    larger = jnp.maximum(max_one, max_two)
    scale_one = jnp.exp(max_one - larger)
    scale_two = jnp.exp(max_two - larger)
    return (
        larger,
        sum_one * scale_one + sum_two * scale_two,
        vector_one * scale_one[..., None] + vector_two * scale_two[..., None],
    )


def groups_to_beams(grouped):
    shaped = grouped.reshape((GROUPS, DECODE_STEPS, BEAM_W, QUERIES_PER_KEY) + grouped.shape[2:])
    shaped = jnp.moveaxis(shaped, 1, 0)
    return shaped.reshape((DECODE_STEPS, BEAM_TOTAL, QUERIES_PER_KEY) + grouped.shape[2:])


def body(
    hidden_in,
    attn_gain,
    ffn_gain,
    query_key_value_weight,
    out_weight,
    router_weight,
    expert_in,
    expert_down,
    kv_cache,
    lengths,
    tables,
    parents,
    routes,
    kv_size,
    blk_size,
):
    count_tokens = DECODE_STEPS * BEAM_TOTAL
    width_local = hidden_in.shape[2]
    heads_local = query_key_value_weight.shape[1]
    logit_scale = 1.0 / math.sqrt(HEAD_WIDTH)
    line_beams, anchor = lineage(parents)
    flat_in = hidden_in.reshape(count_tokens, width_local).astype(jnp.float32)
    pre_attn = (flat_in * attn_gain.astype(jnp.float32)).astype(jnp.bfloat16)
    partial_proj = jnp.dot(
        pre_attn,
        query_key_value_weight.reshape(width_local, -1),
        preferred_element_type=jnp.float32,
    )
    partial_sq = jnp.sum(flat_in * flat_in, axis=1)
    proj_rows = partial_proj.reshape(-1, HEAD_WIDTH)
    sq_rows = jnp.pad(partial_sq, (0, -partial_sq.shape[0] % HEAD_WIDTH)).reshape(-1, HEAD_WIDTH)
    stacked = jnp.concatenate([proj_rows, sq_rows], axis=0)
    chunk_rows = -(-stacked.shape[0] // (8 * blk_size)) * 8
    stacked = jnp.pad(stacked, ((0, chunk_rows * blk_size - stacked.shape[0]), (0, 0)))
    owned = jnp.sum(
        lax.all_to_all(stacked.reshape(blk_size, chunk_rows, HEAD_WIDTH), "blk", 0, 0, tiled=True),
        axis=0,
    )
    summed = lax.all_to_all(
        jnp.broadcast_to(owned[None], (blk_size,) + owned.shape), "blk", 0, 0, tiled=True
    ).reshape(-1, HEAD_WIDTH)
    projected_rows = summed[: proj_rows.shape[0]].reshape(partial_proj.shape)
    square_sum = summed[proj_rows.shape[0] :].reshape(-1)[: partial_sq.shape[0]]
    projected_rows = (
        projected_rows * lax.rsqrt(square_sum / MODEL_WIDTH + NORM_FLOOR)[:, None]
    ).reshape(DECODE_STEPS, BEAM_TOTAL, heads_local, QUERIES_PER_KEY + 2, HEAD_WIDTH)
    beam_groups = jnp.arange(BEAM_TOTAL, dtype=jnp.int32) // BEAM_W
    positions = lookup(lengths, beam_groups)[None, :] + jnp.arange(DECODE_STEPS, dtype=jnp.int32)[:, None]
    queries = rotate_pairs(
        projected_rows[:, :, :, :QUERIES_PER_KEY], positions[:, :, None, None]
    ).astype(jnp.bfloat16)
    new_key = rotate_pairs(projected_rows[:, :, :, QUERIES_PER_KEY], positions[:, :, None]).astype(
        jnp.bfloat16
    )
    new_value = projected_rows[:, :, :, QUERIES_PER_KEY + 1].astype(jnp.bfloat16)
    slot_count = kv_cache.shape[0]
    slot_base = lax.axis_index("blk") * slot_count
    entry_ids = jnp.arange(BEAM_TOTAL * BEAM_BLOCKS, dtype=jnp.int32)
    slot_ids = slot_base + jnp.arange(slot_count, dtype=jnp.int32)
    slot_hits = tables.reshape(-1)[None, :] == slot_ids[:, None]
    entry_here = jnp.sum(jnp.where(slot_hits, entry_ids[None, :], 0), axis=1)
    owner_here = entry_here // BEAM_BLOCKS
    block_here = entry_here % BEAM_BLOCKS
    group_here = owner_here // BEAM_W
    anchor_groups = jnp.moveaxis(anchor.reshape(DECODE_STEPS, GROUPS, BEAM_W), 1, 0)
    anchor_query = jnp.broadcast_to(
        anchor_groups[..., None], (GROUPS, DECODE_STEPS, BEAM_W, QUERIES_PER_KEY)
    ).reshape(GROUPS, -1)
    recent_allowed = jnp.transpose(
        line_beams[:, :, :, None] == jnp.arange(BEAM_TOTAL, dtype=jnp.int32), (0, 2, 1, 3)
    ).reshape(DECODE_STEPS, BEAM_TOTAL, 1, count_tokens)
    is_first = lax.axis_index("blk") == 0
    query_head = queries[:, :, 0]
    query_groups = jnp.moveaxis(
        query_head.reshape(DECODE_STEPS, GROUPS, BEAM_W, QUERIES_PER_KEY, HEAD_WIDTH), 1, 0
    ).reshape(GROUPS, -1, HEAD_WIDTH)
    live_here = lookup(lengths, group_here) - block_here * BLOCK_POSITIONS
    query_match = lookup(anchor_query, group_here) == owner_here[:, None]
    used_here = (jnp.any(query_match, axis=1) & (live_here > 0)).astype(jnp.int32)
    anchor_lanes = jnp.broadcast_to(anchor_query[:, :, None], anchor_query.shape + (HEAD_WIDTH,))
    kv_pairs = kv_cache.reshape(slot_count, 2, BLOCK_POSITIONS, HEAD_WIDTH)
    vector_lanes, max_lanes, sum_lanes = slot_attention(
        group_here, live_here, owner_here, used_here, kv_pairs, query_groups, anchor_lanes, logit_scale
    )
    group_max = max_lanes[:, :, 0]
    group_sum = sum_lanes[:, :, 0]
    group_vector = vector_lanes
    cache_max = groups_to_beams(group_max)
    cache_sum = groups_to_beams(group_sum)
    cache_vector = groups_to_beams(group_vector)
    newest_keys = new_key[:, :, 0].reshape(count_tokens, HEAD_WIDTH)
    newest_values = new_value[:, :, 0].reshape(count_tokens, HEAD_WIDTH)
    newest_logits = (
        jnp.einsum("sbqd,kd->sbqk", query_head, newest_keys, preferred_element_type=jnp.float32)
        * logit_scale
    )
    recent_masked = jnp.where(recent_allowed, newest_logits, NEG_FILL)
    recent_max = jnp.max(recent_masked, axis=-1)
    recent_weights = jnp.where(recent_allowed, jnp.exp(recent_masked - recent_max[..., None]), 0.0)
    recent_sum = jnp.sum(recent_weights, axis=-1)
    recent_vector = jnp.einsum(
        "sbqk,kd->sbqd",
        recent_weights.astype(jnp.bfloat16),
        newest_values,
        preferred_element_type=jnp.float32,
    )
    recent_max = jnp.where(is_first, recent_max, NEG_FILL)
    recent_sum = jnp.where(is_first, recent_sum, 0.0)
    recent_vector = jnp.where(is_first, recent_vector, 0.0)
    local_max, local_sum, local_vector = combine_parts(
        (cache_max, cache_sum, cache_vector), (recent_max, recent_sum, recent_vector)
    )
    max_heads = [local_max]
    sum_heads = [local_sum]
    vector_heads = [local_vector]
    part_max = jnp.stack(max_heads, axis=2)
    part_sum = jnp.stack(sum_heads, axis=2)
    part_vector = jnp.stack(vector_heads, axis=2)
    query_rows = part_vector.reshape(-1, HEAD_WIDTH)
    row_count = query_rows.shape[0]
    packed_rows = jnp.concatenate(
        [
            query_rows,
            part_max.reshape(-1, 1),
            part_sum.reshape(-1, 1),
            jnp.zeros((row_count, HEAD_WIDTH - 2), jnp.float32),
        ],
        axis=1,
    ).reshape(blk_size, row_count // blk_size, 2 * HEAD_WIDTH)
    peer_rows = lax.all_to_all(packed_rows, "blk", 0, 0, tiled=True)
    peer_max = peer_rows[:, :, HEAD_WIDTH]
    peer_scale = jnp.exp(peer_max - jnp.max(peer_max, axis=0)[None])
    merged_sum = jnp.sum(peer_rows[:, :, HEAD_WIDTH + 1] * peer_scale, axis=0)
    merged_vector = jnp.sum(peer_rows[:, :, :HEAD_WIDTH] * peer_scale[:, :, None], axis=0)
    owned_rows = (merged_vector / merged_sum[:, None]).astype(jnp.bfloat16)
    attended_rows = lax.all_to_all(
        jnp.broadcast_to(owned_rows[None], (blk_size,) + owned_rows.shape), "blk", 0, 0, tiled=True
    ).reshape(count_tokens, -1)
    attn_partial = jnp.dot(attended_rows, out_weight, preferred_element_type=jnp.float32)
    attn_out = head_total(attn_partial, kv_size)
    residual = (flat_in + attn_out).astype(jnp.bfloat16)
    experts_local = expert_in.shape[0]
    ff_local = expert_in.shape[3]
    rows_per_expert = DECODE_STEPS * CAP
    rows_local = experts_local * rows_per_expert
    flat_routes = routes.reshape(count_tokens, 2)
    rank = expert_rank(routes).reshape(count_tokens, 2)
    step_of = jnp.arange(count_tokens, dtype=jnp.int32) // BEAM_TOTAL
    row_id = (flat_routes * rows_per_expert + step_of[:, None] * CAP + rank).reshape(-1)
    token_ids = jnp.broadcast_to(
        jnp.arange(count_tokens, dtype=jnp.int32)[:, None], (count_tokens, 2)
    ).reshape(-1)
    table_size = EXPERTS * rows_per_expert
    row_token_all = jnp.zeros((table_size,), jnp.int32).at[row_id].set(token_ids)
    row_live_all = jnp.zeros((table_size,), jnp.float32).at[row_id].set(1.0)
    row_other_all = (
        jnp.zeros((table_size,), jnp.int32).at[row_id].set(flat_routes[:, ::-1].reshape(-1))
    )
    row_start = lax.axis_index("kv") * rows_local
    row_token = lax.dynamic_slice_in_dim(row_token_all, row_start, rows_local)
    row_live = lax.dynamic_slice_in_dim(row_live_all, row_start, rows_local)
    row_other = lax.dynamic_slice_in_dim(row_other_all, row_start, rows_local)
    row_own = (row_start + jnp.arange(rows_local, dtype=jnp.int32)) // rows_per_expert
    in_flat = expert_in.reshape(experts_local, MODEL_WIDTH, 2 * ff_local)
    gain_wide = ffn_gain.astype(jnp.float32)
    full_rows = jnp.moveaxis(
        lax.all_to_all(
            jnp.broadcast_to(residual[None], (blk_size,) + residual.shape), "blk", 0, 0, tiled=True
        ),
        0,
        1,
    ).reshape(residual.shape[0], -1)
    chosen = full_rows[row_token].astype(jnp.float32)
    pre_rows = (chosen * gain_wide).astype(jnp.bfloat16)
    sums_in = jnp.einsum(
        "erd,edf->erf",
        pre_rows.reshape(experts_local, rows_per_expert, MODEL_WIDTH),
        in_flat,
        preferred_element_type=jnp.float32,
    )
    sums_router = jnp.dot(pre_rows, router_weight, preferred_element_type=jnp.float32)
    sum_sq = jnp.sum(chosen * chosen, axis=1)
    inv_rows = lax.rsqrt(sum_sq / MODEL_WIDTH + NORM_FLOOR)
    expert_act = sums_in * inv_rows.reshape(experts_local, rows_per_expert)[:, :, None]
    expert_hidden = (jax.nn.silu(expert_act[..., :ff_local]) * expert_act[..., ff_local:]).astype(
        jnp.bfloat16
    )
    down_part = jnp.einsum(
        "erf,efd->erd", expert_hidden, expert_down, preferred_element_type=jnp.float32
    ).reshape(rows_local, MODEL_WIDTH)
    expert_pieces = jnp.moveaxis(down_part.reshape(rows_local, blk_size, -1), 1, 0)
    expert_result = jnp.sum(lax.all_to_all(expert_pieces, "blk", 0, 0, tiled=True), axis=0)
    logits = sums_router * inv_rows[:, None]
    expert_ids = jnp.arange(EXPERTS, dtype=jnp.int32)
    own_logit = jnp.sum(jnp.where(row_own[:, None] == expert_ids[None, :], logits, 0.0), axis=1)
    other_logit = jnp.sum(jnp.where(row_other[:, None] == expert_ids[None, :], logits, 0.0), axis=1)
    gate_share = row_live / (1.0 + jnp.exp(other_logit - own_logit))
    weighted_values = expert_result * gate_share[:, None]
    placement = (row_token[None, :] == jnp.arange(count_tokens, dtype=jnp.int32)[:, None]).astype(
        jnp.float32
    )
    mixture_part = jnp.dot(placement, weighted_values, precision=lax.Precision.HIGHEST)
    mixture = head_total(mixture_part, kv_size)
    layer_out = (residual.astype(jnp.float32) + mixture).astype(jnp.bfloat16)
    return layer_out.reshape(DECODE_STEPS, BEAM_TOTAL, width_local)


def solution(mesh):
    placed = (
        P(None, None, "blk"),
        P("blk"),
        P(),
        P("blk", "kv", None),
        P("kv", "blk"),
        P(),
        P("kv", None, None, "blk"),
        P("kv", "blk", None),
        P("blk", None, "kv", None, None),
        P(),
        P(),
        P(),
        P(),
    )
    kv_size = mesh.shape["kv"]
    blk_size = mesh.shape["blk"]

    def sized(*arrays):
        return body(*arrays, kv_size, blk_size)

    return jax.shard_map(
        sized, mesh=mesh, in_specs=placed, out_specs=P(None, None, "blk"), check_vma=False
    )
```
